128 devices in a mesh: dp: 32 (over y, z, core), mp: 4 (over x).
Axes of the slice: x: 4, y: 4, z: 4, core: 2. Of those that a mesh axis runs over, the one named last changes fastest.
Arguments:
- hidden_rows: bfloat16 [16384, 4096], P('dp', 'mp'), may hold values from -3 to 3
- destination: int32 [16384], P('dp'), may hold values from 0 to 16383, as said below
- doc_ids: int32 [16384], P('dp'), may hold values from 0 to 63, never falling along the last dimension, each value on 1 to 8704 neighbouring positions
- norm_gain: float32 [4096], replicated, may hold values from 0.1 to 1.9
- w_query: bfloat16 [4096, 2048], P(None, 'mp'), may hold values from -1 to 1
- w_key: bfloat16 [4096, 512], P(None, 'mp'), may hold values from -1 to 1
- w_value: bfloat16 [4096, 512], P(None, 'mp'), may hold values from -0.09375 to 0.09375
- w_out: bfloat16 [2048, 4096], P('mp'), may hold values from -0.125 to 0.125
Outputs:
- layer_out: bfloat16 [16384, 4096], P('dp', 'mp')
The draws below stay inside these ranges and needn't reach their ends.
Inputs may be any that keep to these rules, and one draw needn't show every extreme that they name: `destination`: A permutation of the rows. Each aligned block of 512 rows sends exactly 32 rows to each of half of the 512-row blocks of document order and none to the other half, and each block of document order receives exactly 32 rows from each of half of the blocks of token order.
All inputs are finite; a program needn't handle non-finite values.
Results may differ from the reference program's by a relative error of at most 0.011.
Values may be sent and summed in bfloat16 or wider, within the bound.
No kernel may reach another device: no remote copies, remote signals or barrier semaphores. Data moves between devices by JAX's collectives and lax.ppermute only.
A program may use at most 128 MiB of HBM per device.

```python
import math
import jax
import jax.numpy as jnp
import numpy as np
from jax import lax

D = 4096
HEADS = 16
KVH = 4
HD = 128
TOK_DEV = 512
TOKENS = 16384
DOCS = 64
DOC_MAX = 8704


INPUT_SCALE = 0.2


KEY_SPREAD = 2.5


def drift_component(key):
    drift_key = jax.random.fold_in(key, 13)
    direction = jnp.where(jax.random.bernoulli(drift_key, 0.5, (D,)), 1.0, -1.0).astype(jnp.float32)
    place = draw_destination(key, 0).astype(jnp.float32)
    return jnp.cos(jnp.float32(3.14159265) * place / jnp.float32(TOKENS))[:, None] * direction[None, :]


def drawn_projection(key, salt, heads_count, spread):
    weight_key = jax.random.fold_in(key, salt)
    return spread * jnp.clip(jax.random.normal(weight_key, (D, heads_count * HD), jnp.float32), -6.0, 6.0) / jnp.sqrt(jnp.float32(D))


def draw_hidden_rows(key, part):
    noise_key = jax.random.fold_in(jax.random.fold_in(key, 11), 0)
    noise_draw = jnp.clip(jax.random.normal(noise_key, (TOKENS, D), jnp.float32), -6.0, 6.0)
    drift = drift_component(key)
    return (INPUT_SCALE * (noise_draw + drift)).astype(jnp.bfloat16)


def draw_w_query(key, part):
    return drawn_projection(key, 31, HEADS, 1.0).astype(jnp.bfloat16)


def draw_w_key(key, part):
    return drawn_projection(key, 37, KVH, KEY_SPREAD).astype(jnp.bfloat16)


def draw_destination(key, part):
    owners = TOKENS // TOK_DEV
    capacity = 2 * TOK_DEV // owners
    order_key, send_key, recv_key = jax.random.split(jax.random.fold_in(key, 23), 3)
    owner_order = jax.random.permutation(order_key, owners).astype(jnp.int32)
    owner_inverse = jnp.argsort(owner_order, stable=True).astype(jnp.int32)
    send_perm = jax.vmap(partial_permutation)(jax.random.split(send_key, owners)).reshape(-1)
    recv_perm = jax.vmap(partial_permutation)(jax.random.split(recv_key, owners))
    source = jnp.arange(TOKENS, dtype=jnp.int32) // TOK_DEV
    slot_group = send_perm // capacity
    within = send_perm % capacity
    owner_of = owner_inverse[(source + slot_group) % owners]
    offset = slot_group * capacity + within
    return (owner_of * TOK_DEV + recv_perm[owner_of, offset]).astype(jnp.int32)


def partial_permutation(sub_key):
    return jax.random.permutation(sub_key, TOK_DEV).astype(jnp.int32)


def level_of(stream_key, dims, cuts, least, high):
    loudness = 1.0
    for position, blocks in cuts:
        draws = jax.random.uniform(jax.random.fold_in(jax.random.fold_in(stream_key, 6), position), (blocks,), jnp.float32, least / len(cuts), high / len(cuts))
        loudness = loudness * jnp.repeat(jnp.exp(draws), dims[position] // blocks).reshape((-1,) + (1,) * (len(dims) - 1 - position))
    return loudness


def length_profile(amount, total, most, skew):
    weights = [(1 << 20) // math.isqrt(rank ** skew) + 1 for rank in range(2, amount + 1)]
    spare, holding = total - most - (amount - 1), [1] * (amount - 1)
    while spare > 0:
        free = [i for i in range(amount - 1) if holding[i] < most]
        pool, remaining = sum([weights[i] for i in free]), spare
        for i in free:
            addition = min(most - holding[i], max(1, remaining * weights[i] // pool), spare)
            holding[i] = holding[i] + addition
            spare = spare - addition
    return np.array([most] + holding)


def ragged(key, count, total, reach, slope):
    if count == 2:
        one = jax.random.randint(key, (), max(1, total - reach), min(reach, total - 1) + 1)
        return jnp.stack([one, total - one])
    lengths = jnp.asarray(length_profile(count, total, reach, slope), jnp.int32)
    pairs = (count - 1) // 2
    source_of, taker = lengths[1:1 + 2 * pairs:2], lengths[2:2 + 2 * pairs:2]
    room = jnp.minimum(source_of - 1, reach - taker)
    moved = jax.random.randint(jax.random.fold_in(key, 1), (pairs,), 0, 1 << 20) % (room + 1)
    lengths = lengths.at[1:1 + 2 * pairs:2].set(source_of - moved).at[2:2 + 2 * pairs:2].set(taker + moved)
    return lengths[jax.random.permutation(jax.random.fold_in(key, 2), count)]


def noise(rng, shape, scale, limit, shards=(), kind=jnp.bfloat16):
    array = scale * jax.random.normal(rng, shape, jnp.float32)
    if shards:
        array = array * level_of(rng, shape, shards, -0.22, 0.18)
    return jnp.clip(array, -limit, limit).astype(kind)


def setup_inputs(seed: int = 0) -> dict:
    keys = jax.random.split(jax.random.key(seed), 9)
    hidden_rows = draw_hidden_rows(jax.random.fold_in(keys[8], 71), 0)
    destination = draw_destination(jax.random.fold_in(keys[8], 71), 0)
    doc_ids = jnp.searchsorted(jnp.cumsum(ragged(keys[2], DOCS, TOKENS, DOC_MAX, 2)), jnp.arange(TOKENS), side="right").astype(jnp.int32)
    norm_gain = jnp.clip(1.0 + 0.18 * jax.random.normal(keys[3], (D,), jnp.float32), 0.1, 1.9)
    w_query = draw_w_query(jax.random.fold_in(keys[8], 71), 0)
    w_key = draw_w_key(jax.random.fold_in(keys[8], 71), 0)
    w_value = noise(keys[6], (D, KVH * HD), D ** -0.5, 0.09375, ((1, 4),))
    w_out = noise(keys[7], (HEADS * HD, D), (HEADS * HD) ** -0.5, 0.125, ((0, 4),))
    return dict(hidden_rows=hidden_rows, destination=destination, doc_ids=doc_ids, norm_gain=norm_gain, w_query=w_query, w_key=w_key, w_value=w_value, w_out=w_out)


ROPE_BASE = 500000.0
NORM_EPS = 1e-05

def rope_angles(row_index):
    lane_index = jnp.arange(HD // 2, dtype=jnp.float32)
    frequency = jnp.power(jnp.float32(ROPE_BASE), -2.0 * lane_index / HD)
    return row_index.astype(jnp.float32)[:, None] * frequency[None, :]

def rotate(head_values, angles):
    half_width = head_values.shape[-1] // 2
    first_half = head_values[..., :half_width]
    second_half = head_values[..., half_width:]
    cosine = jnp.cos(angles)[:, None, :]
    sine_part = jnp.sin(angles)[:, None, :]
    return jnp.concatenate([first_half * cosine - second_half * sine_part, second_half * cosine + first_half * sine_part], axis=-1)

def normalize(routed, norm_gain):
    wide_rows = routed.astype(jnp.float32)
    inv_rms = lax.rsqrt(lax.optimization_barrier(jnp.mean(wide_rows * wide_rows, axis=1, keepdims=True)) + NORM_EPS)
    return (wide_rows * inv_rms * norm_gain[None, :]).astype(jnp.bfloat16)

def reference(hidden_rows, destination, doc_ids, norm_gain, w_query, w_key, w_value, w_out):
    group_size = HEADS // KVH
    routed = jnp.zeros_like(hidden_rows).at[destination].set(hidden_rows)
    normed = normalize(routed, norm_gain)
    angles = rope_angles(jnp.arange(TOKENS, dtype=jnp.int32))
    queries = jnp.dot(normed, w_query, preferred_element_type=jnp.float32).reshape(TOKENS, HEADS, HD)
    queries = rotate(queries, angles).astype(jnp.bfloat16)
    keys_all = jnp.dot(normed, w_key, preferred_element_type=jnp.float32).reshape(TOKENS, KVH, HD)
    keys_all = rotate(keys_all, angles).astype(jnp.bfloat16)
    values_all = jnp.dot(normed, w_value, preferred_element_type=jnp.float32).astype(jnp.bfloat16).reshape(TOKENS, KVH, HD)
    window = min(DOC_MAX + TOK_DEV, TOKENS)
    block_count = TOKENS // TOK_DEV
    score_scale = HD ** (-0.5)

    def one_block(block_index):
        first_row = (block_index * TOK_DEV).astype(jnp.int32)
        low_row = jnp.clip(first_row + TOK_DEV - window, 0, TOKENS - window).astype(jnp.int32)
        query_blk = lax.dynamic_slice_in_dim(queries, first_row, TOK_DEV, 0).astype(jnp.float32).reshape(TOK_DEV, KVH, group_size, HD)
        keys_blk = lax.dynamic_slice_in_dim(keys_all, low_row, window, 0).astype(jnp.float32)
        values_blk = lax.dynamic_slice_in_dim(values_all, low_row, window, 0).astype(jnp.float32)
        query_ids = lax.dynamic_slice_in_dim(doc_ids, first_row, TOK_DEV, 0)
        key_ids = lax.dynamic_slice_in_dim(doc_ids, low_row, window, 0)
        query_rows = first_row + jnp.arange(TOK_DEV, dtype=jnp.int32)
        key_rows = low_row + jnp.arange(window, dtype=jnp.int32)
        allowed = (query_ids[:, None] == key_ids[None, :]) & (key_rows[None, :] <= query_rows[:, None])
        scores = jnp.einsum('qgrd,kgd->grqk', query_blk, keys_blk) * score_scale
        scores = jnp.where(allowed[None, None], scores, -jnp.inf)
        row_best = lax.optimization_barrier(jnp.max(scores, axis=-1, keepdims=True))
        exp_scores = jnp.exp(scores - row_best)
        row_total = lax.optimization_barrier(jnp.sum(exp_scores, axis=-1))
        weights = lax.optimization_barrier(exp_scores.astype(jnp.bfloat16)).astype(jnp.float32)
        context = jnp.einsum('grqk,kgd->qgrd', weights, values_blk) / jnp.transpose(row_total, (2, 0, 1))[..., None]
        return context.reshape(TOK_DEV, HEADS * HD).astype(jnp.bfloat16)
    context = lax.map(one_block, jnp.arange(block_count, dtype=jnp.int32)).reshape(TOKENS, HEADS * HD)
    branch = jnp.dot(context, w_out, preferred_element_type=jnp.float32)
    attended = (routed.astype(jnp.float32) + branch).astype(jnp.bfloat16)
    return attended[destination]
```

```python
import functools
import math

import jax
import jax.numpy as jnp
from jax import lax
from jax.experimental import pallas as pl
from jax.experimental.pallas import tpu as pltpu
from jax.sharding import PartitionSpec as P

HD = 128
DOC_MAX = 8704

ROPE_BASE = 500000.0
NORM_EPS = 1e-05
NEG_START = -1e30
KEY_BLOCK = 512


def rope_angles(row_index):
    lane_index = jnp.arange(HD // 2, dtype=jnp.float32)
    frequency = jnp.power(jnp.float32(ROPE_BASE), -2.0 * lane_index / HD)
    return row_index.astype(jnp.float32)[:, None] * frequency[None, :]


def rotate(head_values, angles):
    half_width = head_values.shape[-1] // 2
    first_half = head_values[..., :half_width]
    second_half = head_values[..., half_width:]
    cosine = jnp.cos(angles)[:, None, :]
    sine_part = jnp.sin(angles)[:, None, :]
    return jnp.concatenate(
        [
            first_half * cosine - second_half * sine_part,
            second_half * cosine + first_half * sine_part,
        ],
        axis=-1,
    )


def normalize(routed, norm_gain):
    wide_rows = routed.astype(jnp.float32)
    inv_rms = lax.rsqrt(jnp.mean(wide_rows * wide_rows, axis=1, keepdims=True) + NORM_EPS)
    return (wide_rows * inv_rms * norm_gain[None, :]).astype(jnp.bfloat16)


def flash_kernel(span_ref, q_ref, k_ref, v_ref, start_ref, row_ref, o_ref, m_sc, l_sc, acc_sc):
    step = pl.program_id(0)
    heads = q_ref.shape[0]
    block = k_ref.shape[0]
    scale = HD ** (-0.5)

    @pl.when(step == 0)
    def _init():
        m_sc[...] = jnp.full(m_sc.shape, NEG_START, jnp.float32)
        l_sc[...] = jnp.zeros(l_sc.shape, jnp.float32)
        acc_sc[...] = jnp.zeros(acc_sc.shape, jnp.float32)

    @pl.when(step < span_ref[1])
    def _body():
        key_first = (span_ref[0] + step) * block
        key_rows = key_first + lax.broadcasted_iota(jnp.int32, (1, block), 1)
        allowed = (key_rows >= start_ref[...]) & (key_rows <= row_ref[...])
        keys = k_ref[...]
        values = v_ref[...]
        for h in range(heads):
            scores = lax.dot_general(
                q_ref[h], keys, (((1,), (1,)), ((), ())), preferred_element_type=jnp.float32
            ) * scale
            scores = jnp.where(allowed, scores, -jnp.inf)
            m_old = m_sc[h]
            m_new = jnp.maximum(m_old, jnp.max(scores, axis=-1, keepdims=True))
            rescale = jnp.exp(m_old - m_new)
            exp_scores = jnp.exp(scores - m_new)
            l_sc[h] = l_sc[h] * rescale + jnp.sum(exp_scores, axis=-1, keepdims=True)
            acc_sc[h] = acc_sc[h] * rescale + jnp.dot(
                exp_scores.astype(jnp.bfloat16), values, preferred_element_type=jnp.float32
            )
            m_sc[h] = m_new

    @pl.when(step == pl.num_programs(0) - 1)
    def _finish():
        for h in range(heads):
            o_ref[h] = (acc_sc[h] / l_sc[h]).astype(o_ref.dtype)


def flash_attention(span, queries, keys, values, row_start, row_index, max_blocks):
    heads, rows, _ = queries.shape
    block = KEY_BLOCK

    def kv_map(step, span_ref):
        return (span_ref[0] + jnp.minimum(step, span_ref[1] - 1), 0)

    grid_spec = pltpu.PrefetchScalarGridSpec(
        num_scalar_prefetch=1,
        grid=(max_blocks,),
        in_specs=[
            pl.BlockSpec((heads, rows, HD), lambda step, span_ref: (0, 0, 0)),
            pl.BlockSpec((block, HD), kv_map),
            pl.BlockSpec((block, HD), kv_map),
            pl.BlockSpec((rows, 1), lambda step, span_ref: (0, 0)),
            pl.BlockSpec((rows, 1), lambda step, span_ref: (0, 0)),
        ],
        out_specs=pl.BlockSpec((heads, rows, HD), lambda step, span_ref: (0, 0, 0)),
        scratch_shapes=[
            pltpu.VMEM((heads, rows, 1), jnp.float32),
            pltpu.VMEM((heads, rows, 1), jnp.float32),
            pltpu.VMEM((heads, rows, HD), jnp.float32),
        ],
    )
    flops = 4 * heads * rows * block * HD * max_blocks
    return pl.pallas_call(
        flash_kernel,
        grid_spec=grid_spec,
        out_shape=jax.ShapeDtypeStruct((heads, rows, HD), jnp.bfloat16),
        compiler_params=pltpu.CompilerParams(dimension_semantics=("arbitrary",)),
        cost_estimate=pl.CostEstimate(
            flops=flops,
            transcendentals=heads * rows * block * max_blocks,
            bytes_accessed=2 * block * HD * 2 * max_blocks + 2 * 2 * heads * rows * HD,
        ),
    )(span, queries, keys, values, row_start, row_index)


def local(hidden_rows, destination, doc_ids, norm_gain, w_query, w_key, w_value, w_out):
    owners = lax.axis_size("dp")
    my_index = lax.axis_index("dp")
    tok_dev, columns = hidden_rows.shape
    capacity = 2 * tok_dev // owners
    target = destination // tok_dev
    owner_ids = jnp.arange(owners, dtype=jnp.int32)
    one_hot = (target[:, None] == owner_ids[None, :]).astype(jnp.int32)
    slot_rank = jnp.sum((jnp.cumsum(one_hot, axis=0) - 1) * one_hot, axis=1)
    flat_slot = target * capacity + slot_rank
    outgoing = (
        jnp.zeros((owners * capacity, columns), hidden_rows.dtype).at[flat_slot].set(hidden_rows)
    )
    places = (
        jnp.full((owners * capacity,), tok_dev, jnp.int32).at[flat_slot].set(destination % tok_dev)
    )
    block_first = my_index * tok_dev
    first_id = doc_ids[0]
    last_id = doc_ids[tok_dev - 1]
    less_count = jnp.sum((doc_ids[None, :] < doc_ids[:, None]).astype(jnp.int32), axis=1)
    last_run_start = block_first + less_count[tok_dev - 1]
    info = jnp.broadcast_to(jnp.stack([last_id, last_run_start])[None, :], (owners, 2))
    places_info = jnp.concatenate([places.reshape(owners, capacity), info], axis=1)
    arrived = lax.all_to_all(
        outgoing.reshape(owners, capacity, columns), "dp", split_axis=0, concat_axis=0, tiled=True
    )
    arrived_info = lax.all_to_all(places_info, "dp", split_axis=0, concat_axis=0, tiled=True)
    arrived_rows = arrived_info[:, :capacity].reshape(-1)
    peer_last_id = arrived_info[:, capacity]
    peer_run_start = arrived_info[:, capacity + 1]
    earlier = (owner_ids < my_index) & (peer_last_id == first_id)
    doc_low = jnp.minimum(block_first, jnp.min(jnp.where(earlier, peer_run_start, block_first)))
    row_index = block_first + jnp.arange(tok_dev, dtype=jnp.int32)
    row_start = jnp.where(doc_ids == first_id, doc_low, block_first + less_count)

    routed_part = (
        jnp.zeros((tok_dev, columns), hidden_rows.dtype)
        .at[arrived_rows]
        .set(arrived.reshape(-1, columns), mode="drop")
    )
    routed = lax.all_gather(routed_part, "mp", axis=1, tiled=True)
    normed = normalize(routed, norm_gain)
    heads_dev = w_query.shape[1] // HD
    kv_dev = w_key.shape[1] // HD
    angles = rope_angles(row_index)
    queries = jnp.dot(normed, w_query, preferred_element_type=jnp.float32).reshape(
        tok_dev, heads_dev, HD
    )
    queries = rotate(queries, angles).astype(jnp.bfloat16)
    keys_own = jnp.dot(normed, w_key, preferred_element_type=jnp.float32).reshape(
        tok_dev, kv_dev, HD
    )
    keys_own = rotate(keys_own, angles).astype(jnp.bfloat16).reshape(tok_dev, kv_dev * HD)
    values_own = jnp.dot(normed, w_value, preferred_element_type=jnp.float32).astype(jnp.bfloat16)
    keys_all = lax.all_gather(keys_own, "dp", axis=0, tiled=True)
    values_all = lax.all_gather(values_own, "dp", axis=0, tiled=True)

    block = KEY_BLOCK
    last_block = (block_first + tok_dev - 1) // block
    first_block = doc_low // block
    max_blocks = min((tok_dev - 1) // block + -(-(DOC_MAX - 1) // block) + 1, owners * tok_dev // block)
    span = jnp.stack([first_block, last_block - first_block + 1]).astype(jnp.int32)
    context = flash_attention(
        span,
        jnp.transpose(queries, (1, 0, 2)),
        keys_all,
        values_all,
        row_start[:, None],
        row_index[:, None],
        max_blocks,
    )
    context = jnp.transpose(context, (1, 0, 2)).reshape(tok_dev, heads_dev * HD)
    context_all = lax.all_gather(context, "mp", axis=1, tiled=True)
    w_cols = lax.all_to_all(w_out, "mp", split_axis=1, concat_axis=0, tiled=True)
    summed = jnp.dot(context_all, w_cols, preferred_element_type=jnp.float32)
    attended = (routed_part.astype(jnp.float32) + summed).astype(jnp.bfloat16)
    backward = attended[jnp.minimum(arrived_rows, tok_dev - 1)].reshape(owners, capacity, columns)
    returned = lax.all_to_all(backward, "dp", split_axis=0, concat_axis=0, tiled=True)
    return returned.reshape(owners * capacity, columns)[flat_slot]


def solution(mesh):
    in_specs = (
        P("dp", "mp"),
        P("dp"),
        P("dp"),
        P(),
        P(None, "mp"),
        P(None, "mp"),
        P(None, "mp"),
        P("mp", None),
    )
    out_specs = P("dp", "mp")
    return jax.shard_map(local, mesh=mesh, in_specs=in_specs, out_specs=out_specs, check_vma=False)
```

```python
import functools
import math

import jax
import jax.numpy as jnp
from jax import lax
from jax.experimental import pallas as pl
from jax.experimental.pallas import tpu as pltpu
from jax.sharding import PartitionSpec as P

HD = 128
DOC_MAX = 8704

ROPE_BASE = 500000.0
NORM_EPS = 1e-05
NEG_START = -1e30
KEY_BLOCK = 512


def rope_angles(row_index):
    lane_index = jnp.arange(HD // 2, dtype=jnp.float32)
    frequency = jnp.power(jnp.float32(ROPE_BASE), -2.0 * lane_index / HD)
    return row_index.astype(jnp.float32)[:, None] * frequency[None, :]


def rotate(head_values, angles):
    half_width = head_values.shape[-1] // 2
    first_half = head_values[..., :half_width]
    second_half = head_values[..., half_width:]
    cosine = jnp.cos(angles)[:, None, :]
    sine_part = jnp.sin(angles)[:, None, :]
    return jnp.concatenate(
        [
            first_half * cosine - second_half * sine_part,
            second_half * cosine + first_half * sine_part,
        ],
        axis=-1,
    )


def normalize(routed, norm_gain):
    wide_rows = routed.astype(jnp.float32)
    inv_rms = lax.rsqrt(jnp.mean(wide_rows * wide_rows, axis=1, keepdims=True) + NORM_EPS)
    return (wide_rows * inv_rms * norm_gain[None, :]).astype(jnp.bfloat16)


def flash_kernel(span_ref, q_ref, k_ref, v_ref, start_ref, row_ref, o_ref, m_sc, l_sc, acc_sc):
    step = pl.program_id(0)
    heads = m_sc.shape[0]
    block = k_ref.shape[0]
    scale = HD ** (-0.5)

    @pl.when(step == 0)
    def _init():
        m_sc[...] = jnp.full(m_sc.shape, NEG_START, jnp.float32)
        l_sc[...] = jnp.zeros(l_sc.shape, jnp.float32)
        acc_sc[...] = jnp.zeros(acc_sc.shape, jnp.float32)

    key_first = (span_ref[0] + step) * block
    active = step < span_ref[1]
    whole = (key_first >= span_ref[2]) & (key_first + block - 1 <= span_ref[3])

    def accumulate(masked):
        keys = k_ref[...]
        values = v_ref[...]
        if masked:
            key_rows = key_first + lax.broadcasted_iota(jnp.int32, (1, block), 1)
            allowed = (key_rows >= start_ref[...]) & (key_rows <= row_ref[...])
        for h in range(heads):
            scores = lax.dot_general(
                q_ref[:, h * HD:(h + 1) * HD], keys, (((1,), (1,)), ((), ())),
                preferred_element_type=jnp.float32,
            ) * scale
            if masked:
                scores = jnp.where(allowed, scores, -jnp.inf)
            m_old = m_sc[h]
            m_new = jnp.maximum(m_old, jnp.max(scores, axis=-1, keepdims=True))
            rescale = jnp.exp(m_old - m_new)
            exp_scores = jnp.exp(scores - m_new)
            l_sc[h] = l_sc[h] * rescale + jnp.sum(exp_scores, axis=-1, keepdims=True)
            acc_sc[h] = acc_sc[h] * rescale + jnp.dot(
                exp_scores.astype(jnp.bfloat16), values, preferred_element_type=jnp.float32
            )
            m_sc[h] = m_new

    @pl.when(active & whole)
    def _whole():
        accumulate(False)

    @pl.when(active & jnp.logical_not(whole))
    def _masked():
        accumulate(True)

    @pl.when(step == pl.num_programs(0) - 1)
    def _finish():
        for h in range(heads):
            o_ref[:, h * HD:(h + 1) * HD] = (acc_sc[h] / l_sc[h]).astype(o_ref.dtype)


def flash_attention(span, queries, kv_all, row_start, row_index, max_blocks):
    rows, width = queries.shape
    heads = width // HD
    block = KEY_BLOCK
    halves = kv_all.shape[0]

    def kv_map(column):
        def index_map(step, span_ref):
            key_block = span_ref[0] + jnp.minimum(step, span_ref[1] - 1)
            return (key_block % halves, key_block // halves, 0, column)
        return index_map

    grid_spec = pltpu.PrefetchScalarGridSpec(
        num_scalar_prefetch=1,
        grid=(max_blocks,),
        in_specs=[
            pl.BlockSpec((rows, width), lambda step, span_ref: (0, 0)),
            pl.BlockSpec((None, None, block, HD), kv_map(0)),
            pl.BlockSpec((None, None, block, HD), kv_map(1)),
            pl.BlockSpec((rows, 1), lambda step, span_ref: (0, 0)),
            pl.BlockSpec((rows, 1), lambda step, span_ref: (0, 0)),
        ],
        out_specs=pl.BlockSpec((rows, width), lambda step, span_ref: (0, 0)),
        scratch_shapes=[
            pltpu.VMEM((heads, rows, 1), jnp.float32),
            pltpu.VMEM((heads, rows, 1), jnp.float32),
            pltpu.VMEM((heads, rows, HD), jnp.float32),
        ],
    )
    flops = 4 * heads * rows * block * HD * max_blocks
    return pl.pallas_call(
        flash_kernel,
        grid_spec=grid_spec,
        out_shape=jax.ShapeDtypeStruct((rows, width), jnp.bfloat16),
        compiler_params=pltpu.CompilerParams(dimension_semantics=("arbitrary",)),
        cost_estimate=pl.CostEstimate(
            flops=flops,
            transcendentals=heads * rows * block * max_blocks,
            bytes_accessed=2 * block * HD * 2 * max_blocks + 2 * 2 * rows * width,
        ),
    )(span, queries, kv_all, kv_all, row_start, row_index)


def local(hidden_rows, destination, doc_ids, norm_gain, w_query, w_key, w_value, w_out):
    owners = lax.axis_size(("chip", "core"))
    my_index = lax.axis_index(("chip", "core"))
    tok_dev, columns = hidden_rows.shape
    capacity = 2 * tok_dev // owners
    target = destination // tok_dev
    owner_ids = jnp.arange(owners, dtype=jnp.int32)
    one_hot = (target[:, None] == owner_ids[None, :]).astype(jnp.int32)
    slot_rank = jnp.sum((jnp.cumsum(one_hot, axis=0) - 1) * one_hot, axis=1)
    flat_slot = target * capacity + slot_rank
    outgoing = (
        jnp.zeros((owners * capacity, columns), hidden_rows.dtype).at[flat_slot].set(hidden_rows)
    )
    places = (
        jnp.full((owners * capacity,), tok_dev, jnp.int32).at[flat_slot].set(destination % tok_dev)
    )
    block_first = my_index * tok_dev
    first_id = doc_ids[0]
    last_id = doc_ids[tok_dev - 1]
    less_count = jnp.sum((doc_ids[None, :] < doc_ids[:, None]).astype(jnp.int32), axis=1)
    last_run_start = block_first + less_count[tok_dev - 1]
    info = jnp.broadcast_to(jnp.stack([last_id, last_run_start])[None, :], (owners, 2))
    places_info = jnp.concatenate([places.reshape(owners, capacity), info], axis=1)
    arrived = lax.all_to_all(
        outgoing.reshape(owners, capacity, columns), ("chip", "core"), split_axis=0, concat_axis=0, tiled=True
    )
    arrived_info = lax.all_to_all(places_info, ("chip", "core"), split_axis=0, concat_axis=0, tiled=True)
    arrived_rows = arrived_info[:, :capacity].reshape(-1)
    peer_last_id = arrived_info[:, capacity]
    peer_run_start = arrived_info[:, capacity + 1]
    earlier = (owner_ids < my_index) & (peer_last_id == first_id)
    doc_low = jnp.minimum(block_first, jnp.min(jnp.where(earlier, peer_run_start, block_first)))
    row_index = block_first + jnp.arange(tok_dev, dtype=jnp.int32)
    row_start = jnp.where(doc_ids == first_id, doc_low, block_first + less_count)

    routed_part = (
        jnp.zeros((tok_dev, columns), hidden_rows.dtype)
        .at[arrived_rows]
        .set(arrived.reshape(-1, columns), mode="drop")
    )
    routed = lax.all_gather(routed_part, "mp", axis=1, tiled=True)
    normed = normalize(routed, norm_gain)
    heads_dev = w_query.shape[1] // HD
    kv_dev = w_key.shape[1] // HD
    angles = rope_angles(row_index)
    queries = jnp.dot(normed, w_query, preferred_element_type=jnp.float32).reshape(
        tok_dev, heads_dev, HD
    )
    queries = rotate(queries, angles).astype(jnp.bfloat16).reshape(tok_dev, heads_dev * HD)
    keys_own = jnp.dot(normed, w_key, preferred_element_type=jnp.float32).reshape(
        tok_dev, kv_dev, HD
    )
    keys_own = rotate(keys_own, angles).astype(jnp.bfloat16).reshape(tok_dev, kv_dev * HD)
    values_own = jnp.dot(normed, w_value, preferred_element_type=jnp.float32).astype(jnp.bfloat16)
    kv_own = jnp.concatenate([keys_own, values_own], axis=1)
    kv_chips = lax.all_gather(kv_own, "chip", axis=0, tiled=False)
    kv_all = lax.all_gather(kv_chips, "core", axis=0, tiled=False)

    block = KEY_BLOCK
    last_block = (block_first + tok_dev - 1) // block
    first_block = doc_low // block
    max_blocks = min((tok_dev - 1) // block + -(-(DOC_MAX - 1) // block) + 1, owners * tok_dev // block)
    span = jnp.stack(
        [first_block, last_block - first_block + 1, jnp.max(row_start), block_first]
    ).astype(jnp.int32)
    context = flash_attention(
        span, queries, kv_all, row_start[:, None], row_index[:, None], max_blocks
    )
    context_all = lax.all_gather(context, "mp", axis=1, tiled=True)
    mp_size = lax.axis_size("mp")
    w_split = jnp.transpose(w_out.reshape(w_out.shape[0], mp_size, -1), (1, 0, 2))
    w_cols = lax.all_to_all(w_split, "mp", split_axis=0, concat_axis=0, tiled=True)
    summed = jnp.dot(
        context_all, w_cols.reshape(-1, w_cols.shape[2]), preferred_element_type=jnp.float32
    )
    attended = (routed_part.astype(jnp.float32) + summed).astype(jnp.bfloat16)
    backward = attended[jnp.minimum(arrived_rows, tok_dev - 1)].reshape(owners, capacity, columns)
    returned = lax.all_to_all(backward, ("chip", "core"), split_axis=0, concat_axis=0, tiled=True)
    return returned.reshape(owners * capacity, columns)[flat_slot]


def solution(mesh):
    dp_size, mp_size = mesh.devices.shape
    split_mesh = jax.sharding.Mesh(
        mesh.devices.reshape(dp_size // 2, 2, mp_size), ("chip", "core", "mp")
    )
    rows = ("chip", "core")
    in_specs = (
        P(rows, "mp"),
        P(rows),
        P(rows),
        P(),
        P(None, "mp"),
        P(None, "mp"),
        P(None, "mp"),
        P("mp", None),
    )
    out_specs = P(rows, "mp")
    return jax.shard_map(
        local, mesh=split_mesh, in_specs=in_specs, out_specs=out_specs, check_vma=False
    )
```

```python
import functools
import math

import jax
import jax.numpy as jnp
from jax import lax
from jax.experimental import pallas as pl
from jax.experimental.pallas import tpu as pltpu
from jax.sharding import PartitionSpec as P

HD = 128
DOC_MAX = 8704

ROPE_BASE = 500000.0
NORM_EPS = 1e-05
NEG_START = -1e30
KEY_BLOCK = 512


def rope_angles(row_index):
    lane_index = jnp.arange(HD // 2, dtype=jnp.float32)
    frequency = jnp.power(jnp.float32(ROPE_BASE), -2.0 * lane_index / HD)
    return row_index.astype(jnp.float32)[:, None] * frequency[None, :]


def rotate(head_values, angles):
    half_width = head_values.shape[-1] // 2
    first_half = head_values[..., :half_width]
    second_half = head_values[..., half_width:]
    cosine = jnp.cos(angles)[:, None, :]
    sine_part = jnp.sin(angles)[:, None, :]
    return jnp.concatenate(
        [
            first_half * cosine - second_half * sine_part,
            second_half * cosine + first_half * sine_part,
        ],
        axis=-1,
    )


def normalize(routed, norm_gain):
    wide_rows = routed.astype(jnp.float32)
    inv_rms = lax.rsqrt(jnp.mean(wide_rows * wide_rows, axis=1, keepdims=True) + NORM_EPS)
    return (wide_rows * inv_rms * norm_gain[None, :]).astype(jnp.bfloat16)


def flash_kernel(span_ref, q_ref, k_ref, v_ref, start_ref, row_ref, o_ref, m_sc, l_sc, acc_sc):
    step = pl.program_id(0)
    heads = m_sc.shape[0]
    block = k_ref.shape[0]
    scale = HD ** (-0.5)

    @pl.when(step == 0)
    def _init():
        m_sc[...] = jnp.full(m_sc.shape, NEG_START, jnp.float32)
        l_sc[...] = jnp.zeros(l_sc.shape, jnp.float32)
        acc_sc[...] = jnp.zeros(acc_sc.shape, jnp.float32)

    key_first = (span_ref[0] + step) * block
    active = step < span_ref[1]
    whole = (key_first >= span_ref[2]) & (key_first + block - 1 <= span_ref[3])

    def accumulate(masked):
        keys = k_ref[...]
        values = v_ref[...]
        if masked:
            key_rows = key_first + lax.broadcasted_iota(jnp.int32, (1, block), 1)
            allowed = (key_rows >= start_ref[...]) & (key_rows <= row_ref[...])
        for h in range(heads):
            scores = lax.dot_general(
                q_ref[:, h * HD:(h + 1) * HD], keys, (((1,), (1,)), ((), ())),
                preferred_element_type=jnp.float32,
            ) * scale
            if masked:
                scores = jnp.where(allowed, scores, -jnp.inf)
            m_old = m_sc[h]
            m_new = jnp.maximum(m_old, jnp.max(scores, axis=-1, keepdims=True))
            rescale = jnp.exp(m_old - m_new)
            exp_scores = jnp.exp(scores - m_new)
            l_sc[h] = l_sc[h] * rescale + jnp.sum(exp_scores, axis=-1, keepdims=True)
            acc_sc[h] = acc_sc[h] * rescale + jnp.dot(
                exp_scores.astype(jnp.bfloat16), values, preferred_element_type=jnp.float32
            )
            m_sc[h] = m_new

    @pl.when(active & whole)
    def _whole():
        accumulate(False)

    @pl.when(active & jnp.logical_not(whole))
    def _masked():
        accumulate(True)

    @pl.when(step == pl.num_programs(0) - 1)
    def _finish():
        for h in range(heads):
            o_ref[:, h * HD:(h + 1) * HD] = (acc_sc[h] / l_sc[h]).astype(o_ref.dtype)


def flash_attention(span, queries, kv_all, row_start, row_index, max_blocks):
    rows, width = queries.shape
    heads = width // HD
    block = KEY_BLOCK

    def kv_map(column):
        def index_map(step, span_ref):
            return (span_ref[4] + jnp.minimum(step, span_ref[1] - 1), 0, column)
        return index_map

    grid_spec = pltpu.PrefetchScalarGridSpec(
        num_scalar_prefetch=1,
        grid=(max_blocks,),
        in_specs=[
            pl.BlockSpec((rows, width), lambda step, span_ref: (0, 0)),
            pl.BlockSpec((None, block, HD), kv_map(0)),
            pl.BlockSpec((None, block, HD), kv_map(1)),
            pl.BlockSpec((rows, 1), lambda step, span_ref: (0, 0)),
            pl.BlockSpec((rows, 1), lambda step, span_ref: (0, 0)),
        ],
        out_specs=pl.BlockSpec((rows, width), lambda step, span_ref: (0, 0)),
        scratch_shapes=[
            pltpu.VMEM((heads, rows, 1), jnp.float32),
            pltpu.VMEM((heads, rows, 1), jnp.float32),
            pltpu.VMEM((heads, rows, HD), jnp.float32),
        ],
    )
    flops = 4 * heads * rows * block * HD * max_blocks
    return pl.pallas_call(
        flash_kernel,
        grid_spec=grid_spec,
        out_shape=jax.ShapeDtypeStruct((rows, width), jnp.bfloat16),
        compiler_params=pltpu.CompilerParams(dimension_semantics=("arbitrary",)),
        cost_estimate=pl.CostEstimate(
            flops=flops,
            transcendentals=heads * rows * block * max_blocks,
            bytes_accessed=2 * block * HD * 2 * max_blocks + 2 * 2 * rows * width,
        ),
    )(span, queries, kv_all, kv_all, row_start, row_index)


def local(hidden_rows, destination, doc_ids, norm_gain, w_query, w_key, w_value, w_out):
    owners = lax.axis_size(("chip", "core"))
    my_index = lax.axis_index(("chip", "core"))
    tok_dev, columns = hidden_rows.shape
    capacity = 2 * tok_dev // owners
    target = destination // tok_dev
    owner_ids = jnp.arange(owners, dtype=jnp.int32)
    one_hot = (target[:, None] == owner_ids[None, :]).astype(jnp.int32)
    slot_rank = jnp.sum((jnp.cumsum(one_hot, axis=0) - 1) * one_hot, axis=1)
    flat_slot = target * capacity + slot_rank
    outgoing = (
        jnp.zeros((owners * capacity, columns), hidden_rows.dtype).at[flat_slot].set(hidden_rows)
    )
    places = (
        jnp.full((owners * capacity,), tok_dev, jnp.int32).at[flat_slot].set(destination % tok_dev)
    )
    block_first = my_index * tok_dev
    first_id = doc_ids[0]
    last_id = doc_ids[tok_dev - 1]
    less_count = jnp.sum((doc_ids[None, :] < doc_ids[:, None]).astype(jnp.int32), axis=1)
    last_run_start = block_first + less_count[tok_dev - 1]
    info = jnp.broadcast_to(jnp.stack([last_id, last_run_start])[None, :], (owners, 2))
    places_info = jnp.concatenate([places.reshape(owners, capacity), info], axis=1)
    arrived = lax.all_to_all(
        outgoing.reshape(owners, capacity, columns), ("chip", "core"), split_axis=0, concat_axis=0, tiled=True
    )
    arrived_info = lax.all_to_all(places_info, ("chip", "core"), split_axis=0, concat_axis=0, tiled=True)
    arrived_rows = arrived_info[:, :capacity].reshape(-1)
    peer_last_id = arrived_info[:, capacity]
    peer_run_start = arrived_info[:, capacity + 1]
    earlier = (owner_ids < my_index) & (peer_last_id == first_id)
    doc_low = jnp.minimum(block_first, jnp.min(jnp.where(earlier, peer_run_start, block_first)))
    row_index = block_first + jnp.arange(tok_dev, dtype=jnp.int32)
    row_start = jnp.where(doc_ids == first_id, doc_low, block_first + less_count)

    routed_part = (
        jnp.zeros((tok_dev, columns), hidden_rows.dtype)
        .at[arrived_rows]
        .set(arrived.reshape(-1, columns), mode="drop")
    )
    routed = lax.all_gather(routed_part, "mp", axis=1, tiled=True)
    normed = normalize(routed, norm_gain)
    heads_dev = w_query.shape[1] // HD
    kv_dev = w_key.shape[1] // HD
    angles = rope_angles(row_index)
    queries = jnp.dot(normed, w_query, preferred_element_type=jnp.float32).reshape(
        tok_dev, heads_dev, HD
    )
    queries = rotate(queries, angles).astype(jnp.bfloat16).reshape(tok_dev, heads_dev * HD)
    keys_own = jnp.dot(normed, w_key, preferred_element_type=jnp.float32).reshape(
        tok_dev, kv_dev, HD
    )
    keys_own = rotate(keys_own, angles).astype(jnp.bfloat16).reshape(tok_dev, kv_dev * HD)
    values_own = jnp.dot(normed, w_value, preferred_element_type=jnp.float32).astype(jnp.bfloat16)
    kv_own = jnp.concatenate([keys_own, values_own], axis=1)

    block = KEY_BLOCK
    last_block = (block_first + tok_dev - 1) // block
    first_block = doc_low // block
    max_blocks = min((tok_dev - 1) // block + -(-(DOC_MAX - 1) // block) + 1, owners * tok_dev // block)
    back = max_blocks - 1
    pieces = []
    for shift in range(back, 0, -1):
        pairs = [(source, (source + shift) % owners) for source in range(owners)]
        pieces.append(lax.ppermute(kv_own, ("chip", "core"), pairs))
    pieces.append(kv_own)
    kv_window = jnp.stack(pieces)
    span = jnp.stack(
        [
            first_block,
            last_block - first_block + 1,
            jnp.max(row_start),
            block_first,
            first_block - (last_block - back),
        ]
    ).astype(jnp.int32)
    context = flash_attention(
        span, queries, kv_window, row_start[:, None], row_index[:, None], max_blocks
    )
    context_all = lax.all_gather(context, "mp", axis=1, tiled=True)
    mp_size = lax.axis_size("mp")
    mp_index = lax.axis_index("mp")
    col_width = w_out.shape[1] // mp_size
    head_rows = w_out.shape[0]
    summed = jnp.dot(
        lax.dynamic_slice_in_dim(context_all, mp_index * head_rows, head_rows, 1),
        lax.dynamic_slice_in_dim(w_out, mp_index * col_width, col_width, 1),
        preferred_element_type=jnp.float32,
    )
    for shift in range(1, mp_size):
        to_send = lax.dynamic_slice_in_dim(
            w_out, ((mp_index + shift) % mp_size) * col_width, col_width, 1
        )
        pairs = [(source, (source + shift) % mp_size) for source in range(mp_size)]
        received = lax.ppermute(to_send, "mp", pairs)
        owner = (mp_index - shift) % mp_size
        summed = summed + jnp.dot(
            lax.dynamic_slice_in_dim(context_all, owner * head_rows, head_rows, 1),
            received,
            preferred_element_type=jnp.float32,
        )
    attended = (routed_part.astype(jnp.float32) + summed).astype(jnp.bfloat16)
    backward = attended[jnp.minimum(arrived_rows, tok_dev - 1)].reshape(owners, capacity, columns)
    returned = lax.all_to_all(backward, ("chip", "core"), split_axis=0, concat_axis=0, tiled=True)
    return returned.reshape(owners * capacity, columns)[flat_slot]


def solution(mesh):
    dp_size, mp_size = mesh.devices.shape
    split_mesh = jax.sharding.Mesh(
        mesh.devices.reshape(dp_size // 2, 2, mp_size), ("chip", "core", "mp")
    )
    rows = ("chip", "core")
    in_specs = (
        P(rows, "mp"),
        P(rows),
        P(rows),
        P(),
        P(None, "mp"),
        P(None, "mp"),
        P(None, "mp"),
        P("mp", None),
    )
    out_specs = P(rows, "mp")
    return jax.shard_map(
        local, mesh=split_mesh, in_specs=in_specs, out_specs=out_specs, check_vma=False
    )
```

```python
import functools
import math

import jax
import jax.numpy as jnp
from jax import lax
from jax.experimental import pallas as pl
from jax.experimental.pallas import tpu as pltpu
from jax.sharding import PartitionSpec as P

HD = 128
DOC_MAX = 8704

ROPE_BASE = 500000.0
NORM_EPS = 1e-05
NEG_START = -1e30
KEY_BLOCK = 512


def rope_angles(row_index):
    lane_index = jnp.arange(HD // 2, dtype=jnp.float32)
    frequency = jnp.power(jnp.float32(ROPE_BASE), -2.0 * lane_index / HD)
    return row_index.astype(jnp.float32)[:, None] * frequency[None, :]


def rotate(head_values, angles):
    half_width = head_values.shape[-1] // 2
    first_half = head_values[..., :half_width]
    second_half = head_values[..., half_width:]
    cosine = jnp.cos(angles)[:, None, :]
    sine_part = jnp.sin(angles)[:, None, :]
    return jnp.concatenate(
        [
            first_half * cosine - second_half * sine_part,
            second_half * cosine + first_half * sine_part,
        ],
        axis=-1,
    )


def normalize(routed, norm_gain):
    wide_rows = routed.astype(jnp.float32)
    inv_rms = lax.rsqrt(jnp.mean(wide_rows * wide_rows, axis=1, keepdims=True) + NORM_EPS)
    return (wide_rows * inv_rms * norm_gain[None, :]).astype(jnp.bfloat16)


def flash_kernel(final, span_ref, *refs):
    if final:
        q_ref, k_ref, v_ref, start_ref, row_ref, m_in, l_in, acc_in, o_ref, m_sc, l_sc, acc_sc = refs
    else:
        q_ref, k_ref, v_ref, start_ref, row_ref, m_sc, l_sc, acc_sc = refs
    step = pl.program_id(0)
    heads = m_sc.shape[0]
    block = k_ref.shape[0]
    scale = HD ** (-0.5)

    @pl.when(step == 0)
    def _init():
        if final:
            m_sc[...] = m_in[...]
            l_sc[...] = l_in[...]
            acc_sc[...] = acc_in[...]
        else:
            m_sc[...] = jnp.full(m_sc.shape, NEG_START, jnp.float32)
            l_sc[...] = jnp.zeros(l_sc.shape, jnp.float32)
            acc_sc[...] = jnp.zeros(acc_sc.shape, jnp.float32)

    key_first = (span_ref[0] + step) * span_ref[4] + span_ref[5]
    active = step < span_ref[1]
    whole = (key_first >= span_ref[2]) & (key_first + block - 1 <= span_ref[3])

    def accumulate(masked):
        keys = k_ref[...]
        values = v_ref[...]
        if masked:
            key_rows = key_first + lax.broadcasted_iota(jnp.int32, (1, block), 1)
            allowed = (key_rows >= start_ref[...]) & (key_rows <= row_ref[...])
        for h in range(heads):
            scores = lax.dot_general(
                q_ref[:, h * HD:(h + 1) * HD], keys, (((1,), (1,)), ((), ())),
                preferred_element_type=jnp.float32,
            ) * scale
            if masked:
                scores = jnp.where(allowed, scores, -jnp.inf)
            m_old = m_sc[h]
            m_new = jnp.maximum(m_old, jnp.max(scores, axis=-1, keepdims=True))
            rescale = jnp.exp(m_old - m_new)
            exp_scores = jnp.exp(scores - m_new)
            l_sc[h] = l_sc[h] * rescale + jnp.sum(exp_scores, axis=-1, keepdims=True)
            acc_sc[h] = acc_sc[h] * rescale + jnp.dot(
                exp_scores.astype(jnp.bfloat16), values, preferred_element_type=jnp.float32
            )
            m_sc[h] = m_new

    @pl.when(active & whole)
    def _whole():
        accumulate(False)

    @pl.when(active & jnp.logical_not(whole))
    def _masked():
        accumulate(True)

    if final:
        @pl.when(step == pl.num_programs(0) - 1)
        def _finish():
            for h in range(heads):
                o_ref[:, h * HD:(h + 1) * HD] = (acc_sc[h] / l_sc[h]).astype(o_ref.dtype)


def flash_pass(span, queries, kv_part, row_start, row_index, max_blocks, state):
    rows, width = queries.shape
    heads = width // HD
    block = row_start.shape[0] // 2
    final = state is not None

    def kv_map(column):
        def index_map(step, span_ref):
            return (span_ref[0] + jnp.minimum(step, span_ref[1] - 1), column)
        return index_map

    fixed2 = lambda step, span_ref: (0, 0)
    fixed3 = lambda step, span_ref: (0, 0, 0)
    in_specs = [
        pl.BlockSpec((rows, width), fixed2),
        pl.BlockSpec((block, HD), kv_map(0)),
        pl.BlockSpec((block, HD), kv_map(1)),
        pl.BlockSpec((rows, 1), fixed2),
        pl.BlockSpec((rows, 1), fixed2),
    ]
    state_shapes = [
        jax.ShapeDtypeStruct((heads, rows, 1), jnp.float32),
        jax.ShapeDtypeStruct((heads, rows, 1), jnp.float32),
        jax.ShapeDtypeStruct((heads, rows, HD), jnp.float32),
    ]
    state_specs = [pl.BlockSpec(x.shape, fixed3) for x in state_shapes]
    if final:
        in_specs = in_specs + state_specs
        out_specs = pl.BlockSpec((rows, width), fixed2)
        out_shape = jax.ShapeDtypeStruct((rows, width), jnp.bfloat16)
        scratch = [pltpu.VMEM(x.shape, jnp.float32) for x in state_shapes]
        operands = (span, queries, kv_part, kv_part, row_start, row_index) + tuple(state)
    else:
        out_specs = state_specs
        out_shape = state_shapes
        scratch = []
        operands = (span, queries, kv_part, kv_part, row_start, row_index)
    grid_spec = pltpu.PrefetchScalarGridSpec(
        num_scalar_prefetch=1,
        grid=(max_blocks,),
        in_specs=in_specs,
        out_specs=out_specs,
        scratch_shapes=scratch,
    )
    flops = 4 * heads * rows * block * HD * max_blocks
    return pl.pallas_call(
        functools.partial(flash_kernel, final),
        grid_spec=grid_spec,
        out_shape=out_shape,
        compiler_params=pltpu.CompilerParams(dimension_semantics=("arbitrary",)),
        cost_estimate=pl.CostEstimate(
            flops=flops,
            transcendentals=heads * rows * block * max_blocks,
            bytes_accessed=2 * block * HD * 2 * max_blocks + 2 * 2 * rows * width,
        ),
    )(*operands)


def local(hidden_rows, destination, doc_ids, norm_gain, w_query, w_key, w_value, w_out):
    owners = lax.axis_size(("chip", "core"))
    my_index = lax.axis_index(("chip", "core"))
    tok_dev, columns = hidden_rows.shape
    capacity = 2 * tok_dev // owners
    target = destination // tok_dev
    owner_ids = jnp.arange(owners, dtype=jnp.int32)
    one_hot = (target[:, None] == owner_ids[None, :]).astype(jnp.int32)
    slot_rank = jnp.sum((jnp.cumsum(one_hot, axis=0) - 1) * one_hot, axis=1)
    flat_slot = target * capacity + slot_rank
    outgoing = (
        jnp.zeros((owners * capacity, columns), hidden_rows.dtype).at[flat_slot].set(hidden_rows)
    )
    places = (
        jnp.full((owners * capacity,), tok_dev, jnp.int32).at[flat_slot].set(destination % tok_dev)
    )
    block_first = my_index * tok_dev
    first_id = doc_ids[0]
    last_id = doc_ids[tok_dev - 1]
    less_count = jnp.sum((doc_ids[None, :] < doc_ids[:, None]).astype(jnp.int32), axis=1)
    last_run_start = block_first + less_count[tok_dev - 1]
    info = jnp.broadcast_to(jnp.stack([last_id, last_run_start])[None, :], (owners, 2))
    places_info = jnp.concatenate([places.reshape(owners, capacity), info], axis=1)
    arrived = lax.all_to_all(
        outgoing.reshape(owners, capacity, columns), ("chip", "core"), split_axis=0, concat_axis=0, tiled=True
    )
    arrived_info = lax.all_to_all(places_info, ("chip", "core"), split_axis=0, concat_axis=0, tiled=True)
    arrived_rows = arrived_info[:, :capacity].reshape(-1)
    peer_last_id = arrived_info[:, capacity]
    peer_run_start = arrived_info[:, capacity + 1]
    earlier = (owner_ids < my_index) & (peer_last_id == first_id)
    doc_low = jnp.minimum(block_first, jnp.min(jnp.where(earlier, peer_run_start, block_first)))
    row_index = block_first + jnp.arange(tok_dev, dtype=jnp.int32)
    row_start = jnp.where(doc_ids == first_id, doc_low, block_first + less_count)

    routed_part = (
        jnp.zeros((tok_dev, columns), hidden_rows.dtype)
        .at[arrived_rows]
        .set(arrived.reshape(-1, columns), mode="drop")
    )
    routed = lax.all_gather(routed_part, "mp", axis=1, tiled=True)
    normed = normalize(routed, norm_gain)
    heads_dev = w_query.shape[1] // HD
    kv_dev = w_key.shape[1] // HD
    angles = rope_angles(row_index)
    queries = jnp.dot(normed, w_query, preferred_element_type=jnp.float32).reshape(
        tok_dev, heads_dev, HD
    )
    queries = rotate(queries, angles).astype(jnp.bfloat16).reshape(tok_dev, heads_dev * HD)
    keys_own = jnp.dot(normed, w_key, preferred_element_type=jnp.float32).reshape(
        tok_dev, kv_dev, HD
    )
    keys_own = rotate(keys_own, angles).astype(jnp.bfloat16).reshape(tok_dev, kv_dev * HD)
    values_own = jnp.dot(normed, w_value, preferred_element_type=jnp.float32).astype(jnp.bfloat16)
    kv_own = jnp.concatenate([keys_own, values_own], axis=1)
    half = tok_dev // 2
    kv_low = lax.all_gather(kv_own[:half], ("chip", "core"), axis=0, tiled=True)
    kv_high = lax.all_gather(kv_own[half:], ("chip", "core"), axis=0, tiled=True)

    block = KEY_BLOCK
    last_block = (block_first + tok_dev - 1) // block
    first_block = doc_low // block
    max_blocks = min((tok_dev - 1) // block + -(-(DOC_MAX - 1) // block) + 1, owners * tok_dev // block)
    max_start = jnp.max(row_start)

    def span_for(offset):
        return jnp.stack(
            [first_block, last_block - first_block + 1, max_start, block_first, block, offset]
        ).astype(jnp.int32)

    state = flash_pass(
        span_for(0), queries, kv_low, row_start[:, None], row_index[:, None], max_blocks, None
    )
    context = flash_pass(
        span_for(half), queries, kv_high, row_start[:, None], row_index[:, None], max_blocks, state
    )
    context_all = lax.all_gather(context, "mp", axis=1, tiled=True)
    mp_size = lax.axis_size("mp")
    w_split = jnp.transpose(w_out.reshape(w_out.shape[0], mp_size, -1), (1, 0, 2))
    w_cols = lax.all_to_all(w_split, "mp", split_axis=0, concat_axis=0, tiled=True)
    summed = jnp.dot(
        context_all, w_cols.reshape(-1, w_cols.shape[2]), preferred_element_type=jnp.float32
    )
    attended = (routed_part.astype(jnp.float32) + summed).astype(jnp.bfloat16)
    backward = attended[jnp.minimum(arrived_rows, tok_dev - 1)].reshape(owners, capacity, columns)
    returned = lax.all_to_all(backward, ("chip", "core"), split_axis=0, concat_axis=0, tiled=True)
    return returned.reshape(owners * capacity, columns)[flat_slot]


def solution(mesh):
    dp_size, mp_size = mesh.devices.shape
    split_mesh = jax.sharding.Mesh(
        mesh.devices.reshape(dp_size // 2, 2, mp_size), ("chip", "core", "mp")
    )
    rows = ("chip", "core")
    in_specs = (
        P(rows, "mp"),
        P(rows),
        P(rows),
        P(),
        P(None, "mp"),
        P(None, "mp"),
        P(None, "mp"),
        P("mp", None),
    )
    out_specs = P(rows, "mp")
    return jax.shard_map(
        local, mesh=split_mesh, in_specs=in_specs, out_specs=out_specs, check_vma=False
    )
```

```python
import functools
import math

import jax
import jax.numpy as jnp
from jax import lax
from jax.experimental import pallas as pl
from jax.experimental.pallas import tpu as pltpu
from jax.sharding import PartitionSpec as P

HD = 128
DOC_MAX = 8704

ROPE_BASE = 500000.0
NORM_EPS = 1e-05
NEG_START = -1e30
KEY_BLOCK = 512
CHUNK = 128


def rope_angles(row_index):
    lane_index = jnp.arange(HD // 2, dtype=jnp.float32)
    frequency = jnp.power(jnp.float32(ROPE_BASE), -2.0 * lane_index / HD)
    return row_index.astype(jnp.float32)[:, None] * frequency[None, :]


def rotate(head_values, angles):
    half_width = head_values.shape[-1] // 2
    first_half = head_values[..., :half_width]
    second_half = head_values[..., half_width:]
    cosine = jnp.cos(angles)[:, None, :]
    sine_part = jnp.sin(angles)[:, None, :]
    return jnp.concatenate(
        [
            first_half * cosine - second_half * sine_part,
            second_half * cosine + first_half * sine_part,
        ],
        axis=-1,
    )


def normalize(routed, norm_gain):
    wide_rows = routed.astype(jnp.float32)
    inv_rms = lax.rsqrt(jnp.mean(wide_rows * wide_rows, axis=1, keepdims=True) + NORM_EPS)
    return (wide_rows * inv_rms * norm_gain[None, :]).astype(jnp.bfloat16)


def flash_kernel(final, span_ref, *refs):
    if final:
        q_ref, k_ref, v_ref, start_ref, row_ref, m_in, l_in, acc_in, o_ref, m_sc, l_sc, acc_sc = refs
    else:
        q_ref, k_ref, v_ref, start_ref, row_ref, m_sc, l_sc, acc_sc = refs
    step = pl.program_id(0)
    heads = m_sc.shape[0]
    block = k_ref.shape[0]
    scale = HD ** (-0.5)

    @pl.when(step == 0)
    def _init():
        if final:
            m_sc[...] = m_in[...]
            l_sc[...] = l_in[...]
            acc_sc[...] = acc_in[...]
        else:
            m_sc[...] = jnp.full(m_sc.shape, NEG_START, jnp.float32)
            l_sc[...] = jnp.zeros(l_sc.shape, jnp.float32)
            acc_sc[...] = jnp.zeros(acc_sc.shape, jnp.float32)

    key_first = (span_ref[0] + step) * span_ref[4] + span_ref[5]
    key_last = key_first + block - 1
    active = step < span_ref[1]
    chunk = CHUNK
    chunks = q_ref.shape[0] // chunk

    def accumulate(c, masked):
        r0 = pl.multiple_of(c * chunk, chunk)
        keys = k_ref[...]
        values = v_ref[...]
        if masked:
            key_rows = key_first + lax.broadcasted_iota(jnp.int32, (1, block), 1)
            allowed = (key_rows >= start_ref[pl.ds(r0, chunk), :]) & (
                key_rows <= row_ref[pl.ds(r0, chunk), :]
            )
        for h in range(heads):
            scores = lax.dot_general(
                q_ref[pl.ds(r0, chunk), h * HD:(h + 1) * HD], keys, (((1,), (1,)), ((), ())),
                preferred_element_type=jnp.float32,
            ) * scale
            if masked:
                scores = jnp.where(allowed, scores, -jnp.inf)
            m_old = m_sc[h, pl.ds(r0, chunk), :]
            m_new = jnp.maximum(m_old, jnp.max(scores, axis=-1, keepdims=True))
            rescale = jnp.exp(m_old - m_new)
            exp_scores = jnp.exp(scores - m_new)
            l_sc[h, pl.ds(r0, chunk), :] = l_sc[h, pl.ds(r0, chunk), :] * rescale + jnp.sum(
                exp_scores, axis=-1, keepdims=True
            )
            acc_sc[h, pl.ds(r0, chunk), :] = acc_sc[h, pl.ds(r0, chunk), :] * rescale + jnp.dot(
                exp_scores.astype(jnp.bfloat16), values, preferred_element_type=jnp.float32
            )
            m_sc[h, pl.ds(r0, chunk), :] = m_new

    @pl.when(active)
    def _visit():
        @pl.loop(0, chunks)
        def _chunk(c):
            row_first = span_ref[3] + c * chunk
            row_last = row_first + chunk - 1
            least_start = span_ref[6 + c]
            most_start = span_ref[6 + chunks + c]
            needed = (least_start <= key_last) & (row_last >= key_first)
            whole = (most_start <= key_first) & (key_last <= row_first)

            @pl.when(needed & whole)
            def _whole():
                accumulate(c, False)

            @pl.when(needed & jnp.logical_not(whole))
            def _masked():
                accumulate(c, True)

    if final:
        @pl.when(step == pl.num_programs(0) - 1)
        def _finish():
            for h in range(heads):
                o_ref[:, h * HD:(h + 1) * HD] = (acc_sc[h] / l_sc[h]).astype(o_ref.dtype)


def flash_pass(span, queries, kv_part, row_start, row_index, max_blocks, state):
    rows, width = queries.shape
    heads = width // HD
    block = row_start.shape[0] // 2
    final = state is not None

    def kv_map(column):
        def index_map(step, span_ref):
            return (span_ref[0] + jnp.minimum(step, span_ref[1] - 1), column)
        return index_map

    fixed2 = lambda step, span_ref: (0, 0)
    fixed3 = lambda step, span_ref: (0, 0, 0)
    in_specs = [
        pl.BlockSpec((rows, width), fixed2),
        pl.BlockSpec((block, HD), kv_map(0)),
        pl.BlockSpec((block, HD), kv_map(1)),
        pl.BlockSpec((rows, 1), fixed2),
        pl.BlockSpec((rows, 1), fixed2),
    ]
    state_shapes = [
        jax.ShapeDtypeStruct((heads, rows, 1), jnp.float32),
        jax.ShapeDtypeStruct((heads, rows, 1), jnp.float32),
        jax.ShapeDtypeStruct((heads, rows, HD), jnp.float32),
    ]
    state_specs = [pl.BlockSpec(x.shape, fixed3) for x in state_shapes]
    if final:
        in_specs = in_specs + state_specs
        out_specs = pl.BlockSpec((rows, width), fixed2)
        out_shape = jax.ShapeDtypeStruct((rows, width), jnp.bfloat16)
        scratch = [pltpu.VMEM(x.shape, jnp.float32) for x in state_shapes]
        operands = (span, queries, kv_part, kv_part, row_start, row_index) + tuple(state)
    else:
        out_specs = state_specs
        out_shape = state_shapes
        scratch = []
        operands = (span, queries, kv_part, kv_part, row_start, row_index)
    grid_spec = pltpu.PrefetchScalarGridSpec(
        num_scalar_prefetch=1,
        grid=(max_blocks,),
        in_specs=in_specs,
        out_specs=out_specs,
        scratch_shapes=scratch,
    )
    flops = 4 * heads * rows * block * HD * max_blocks
    return pl.pallas_call(
        functools.partial(flash_kernel, final),
        grid_spec=grid_spec,
        out_shape=out_shape,
        compiler_params=pltpu.CompilerParams(dimension_semantics=("arbitrary",)),
        cost_estimate=pl.CostEstimate(
            flops=flops,
            transcendentals=heads * rows * block * max_blocks,
            bytes_accessed=2 * block * HD * 2 * max_blocks + 2 * 2 * rows * width,
        ),
    )(*operands)


def local(hidden_rows, destination, doc_ids, norm_gain, w_query, w_key, w_value, w_out):
    owners = lax.axis_size(("chip", "core"))
    my_index = lax.axis_index(("chip", "core"))
    tok_dev, columns = hidden_rows.shape
    capacity = 2 * tok_dev // owners
    target = destination // tok_dev
    owner_ids = jnp.arange(owners, dtype=jnp.int32)
    one_hot = (target[:, None] == owner_ids[None, :]).astype(jnp.int32)
    slot_rank = jnp.sum((jnp.cumsum(one_hot, axis=0) - 1) * one_hot, axis=1)
    flat_slot = target * capacity + slot_rank
    outgoing = (
        jnp.zeros((owners * capacity, columns), hidden_rows.dtype).at[flat_slot].set(hidden_rows)
    )
    places = (
        jnp.full((owners * capacity,), tok_dev, jnp.int32).at[flat_slot].set(destination % tok_dev)
    )
    block_first = my_index * tok_dev
    first_id = doc_ids[0]
    last_id = doc_ids[tok_dev - 1]
    less_count = jnp.sum((doc_ids[None, :] < doc_ids[:, None]).astype(jnp.int32), axis=1)
    last_run_start = block_first + less_count[tok_dev - 1]
    info = jnp.broadcast_to(jnp.stack([last_id, last_run_start])[None, :], (owners, 2))
    places_info = jnp.concatenate([places.reshape(owners, capacity), info], axis=1)
    arrived = lax.all_to_all(
        outgoing.reshape(owners, capacity, columns), ("chip", "core"), split_axis=0, concat_axis=0, tiled=True
    )
    arrived_info = lax.all_to_all(places_info, ("chip", "core"), split_axis=0, concat_axis=0, tiled=True)
    arrived_rows = arrived_info[:, :capacity].reshape(-1)
    peer_last_id = arrived_info[:, capacity]
    peer_run_start = arrived_info[:, capacity + 1]
    earlier = (owner_ids < my_index) & (peer_last_id == first_id)
    doc_low = jnp.minimum(block_first, jnp.min(jnp.where(earlier, peer_run_start, block_first)))
    row_index = block_first + jnp.arange(tok_dev, dtype=jnp.int32)
    row_start = jnp.where(doc_ids == first_id, doc_low, block_first + less_count)

    routed_part = (
        jnp.zeros((tok_dev, columns), hidden_rows.dtype)
        .at[arrived_rows]
        .set(arrived.reshape(-1, columns), mode="drop")
    )
    routed = lax.all_gather(routed_part, "mp", axis=1, tiled=True)
    normed = normalize(routed, norm_gain)
    heads_dev = w_query.shape[1] // HD
    kv_dev = w_key.shape[1] // HD
    angles = rope_angles(row_index)
    queries = jnp.dot(normed, w_query, preferred_element_type=jnp.float32).reshape(
        tok_dev, heads_dev, HD
    )
    queries = rotate(queries, angles).astype(jnp.bfloat16).reshape(tok_dev, heads_dev * HD)
    keys_own = jnp.dot(normed, w_key, preferred_element_type=jnp.float32).reshape(
        tok_dev, kv_dev, HD
    )
    keys_own = rotate(keys_own, angles).astype(jnp.bfloat16).reshape(tok_dev, kv_dev * HD)
    values_own = jnp.dot(normed, w_value, preferred_element_type=jnp.float32).astype(jnp.bfloat16)
    kv_own = jnp.concatenate([keys_own, values_own], axis=1)
    half = tok_dev // 2
    kv_low = lax.all_gather(kv_own[:half], ("chip", "core"), axis=0, tiled=True)
    kv_high = lax.all_gather(kv_own[half:], ("chip", "core"), axis=0, tiled=True)

    block = KEY_BLOCK
    last_block = (block_first + tok_dev - 1) // block
    first_block = doc_low // block
    max_blocks = min((tok_dev - 1) // block + -(-(DOC_MAX - 1) // block) + 1, owners * tok_dev // block)
    chunk_starts = row_start.reshape(-1, CHUNK)
    least_starts = jnp.min(chunk_starts, axis=1)
    most_starts = jnp.max(chunk_starts, axis=1)

    def span_for(offset):
        head = jnp.stack([first_block, last_block - first_block + 1, 0, block_first, block, offset])
        return jnp.concatenate([head, least_starts, most_starts]).astype(jnp.int32)

    state = flash_pass(
        span_for(0), queries, kv_low, row_start[:, None], row_index[:, None], max_blocks, None
    )
    mp_size = lax.axis_size("mp")
    w_split = jnp.transpose(w_out.reshape(w_out.shape[0], mp_size, -1), (1, 0, 2))
    w_cols = lax.all_to_all(w_split, "mp", split_axis=0, concat_axis=0, tiled=True)
    state, w_cols = lax.optimization_barrier((state, w_cols))
    context = flash_pass(
        span_for(half), queries, kv_high, row_start[:, None], row_index[:, None], max_blocks, state
    )
    context_all = lax.all_gather(context, "mp", axis=1, tiled=True)
    summed = jnp.dot(
        context_all, w_cols.reshape(-1, w_cols.shape[2]), preferred_element_type=jnp.float32
    )
    attended = (routed_part.astype(jnp.float32) + summed).astype(jnp.bfloat16)
    backward = attended[jnp.minimum(arrived_rows, tok_dev - 1)].reshape(owners, capacity, columns)
    returned = lax.all_to_all(backward, ("chip", "core"), split_axis=0, concat_axis=0, tiled=True)
    return returned.reshape(owners * capacity, columns)[flat_slot]


def solution(mesh):
    dp_size, mp_size = mesh.devices.shape
    split_mesh = jax.sharding.Mesh(
        mesh.devices.reshape(dp_size // 2, 2, mp_size), ("chip", "core", "mp")
    )
    rows = ("chip", "core")
    in_specs = (
        P(rows, "mp"),
        P(rows),
        P(rows),
        P(),
        P(None, "mp"),
        P(None, "mp"),
        P(None, "mp"),
        P("mp", None),
    )
    out_specs = P(rows, "mp")
    return jax.shard_map(
        local, mesh=split_mesh, in_specs=in_specs, out_specs=out_specs, check_vma=False
    )
```

```python
import functools
import math

import jax
import jax.numpy as jnp
from jax import lax
from jax.experimental import pallas as pl
from jax.experimental.pallas import tpu as pltpu
from jax.sharding import PartitionSpec as P

HD = 128
DOC_MAX = 8704

ROPE_BASE = 500000.0
NORM_EPS = 1e-05
NEG_START = -1e30
KEY_BLOCK = 512


def rope_angles(row_index):
    lane_index = jnp.arange(HD // 2, dtype=jnp.float32)
    frequency = jnp.power(jnp.float32(ROPE_BASE), -2.0 * lane_index / HD)
    return row_index.astype(jnp.float32)[:, None] * frequency[None, :]


def rotate(head_values, angles):
    half_width = head_values.shape[-1] // 2
    first_half = head_values[..., :half_width]
    second_half = head_values[..., half_width:]
    cosine = jnp.cos(angles)[:, None, :]
    sine_part = jnp.sin(angles)[:, None, :]
    return jnp.concatenate(
        [
            first_half * cosine - second_half * sine_part,
            second_half * cosine + first_half * sine_part,
        ],
        axis=-1,
    )


def normalize(routed, norm_gain):
    wide_rows = routed.astype(jnp.float32)
    inv_rms = lax.rsqrt(jnp.mean(wide_rows * wide_rows, axis=1, keepdims=True) + NORM_EPS)
    return (wide_rows * inv_rms * norm_gain[None, :]).astype(jnp.bfloat16)


def flash_kernel(final, span_ref, *refs):
    if final:
        q_ref, k_ref, v_ref, start_ref, row_ref, m_in, l_in, acc_in, o_ref, m_sc, l_sc, acc_sc = refs
    else:
        q_ref, k_ref, v_ref, start_ref, row_ref, m_sc, l_sc, acc_sc = refs
    step = pl.program_id(0)
    heads = m_sc.shape[0]
    block = k_ref.shape[0]
    scale = HD ** (-0.5)

    @pl.when(step == 0)
    def _init():
        if final:
            m_sc[...] = m_in[...]
            l_sc[...] = l_in[...]
            acc_sc[...] = acc_in[...]
        else:
            m_sc[...] = jnp.full(m_sc.shape, NEG_START, jnp.float32)
            l_sc[...] = jnp.zeros(l_sc.shape, jnp.float32)
            acc_sc[...] = jnp.zeros(acc_sc.shape, jnp.float32)

    key_first = (span_ref[0] + step) * span_ref[4] + span_ref[5]
    active = step < span_ref[1]
    whole = (key_first >= span_ref[2]) & (key_first + block - 1 <= span_ref[3])

    def accumulate(masked):
        keys = k_ref[...]
        values = v_ref[...]
        if masked:
            key_rows = key_first + lax.broadcasted_iota(jnp.int32, (1, block), 1)
            allowed = (key_rows >= start_ref[...]) & (key_rows <= row_ref[...])
        for h in range(heads):
            scores = lax.dot_general(
                q_ref[:, h * HD:(h + 1) * HD], keys, (((1,), (1,)), ((), ())),
                preferred_element_type=jnp.float32,
            ) * scale
            if masked:
                scores = jnp.where(allowed, scores, -jnp.inf)
            m_old = m_sc[h]
            m_new = jnp.maximum(m_old, jnp.max(scores, axis=-1, keepdims=True))
            rescale = jnp.exp(m_old - m_new)
            exp_scores = jnp.exp(scores - m_new)
            l_sc[h] = l_sc[h] * rescale + jnp.sum(exp_scores, axis=-1, keepdims=True)
            acc_sc[h] = acc_sc[h] * rescale + jnp.dot(
                exp_scores.astype(jnp.bfloat16), values, preferred_element_type=jnp.float32
            )
            m_sc[h] = m_new

    @pl.when(active & whole)
    def _whole():
        accumulate(False)

    @pl.when(active & jnp.logical_not(whole))
    def _masked():
        accumulate(True)

    if final:
        @pl.when(step == pl.num_programs(0) - 1)
        def _finish():
            for h in range(heads):
                o_ref[:, h * HD:(h + 1) * HD] = (acc_sc[h] / l_sc[h]).astype(o_ref.dtype)


def flash_pass(span, queries, kv_part, row_start, row_index, max_blocks, state):
    rows, width = queries.shape
    heads = width // HD
    block = row_start.shape[0] // 2
    final = state is not None

    def kv_map(column):
        def index_map(step, span_ref):
            return (span_ref[0] + jnp.minimum(step, span_ref[1] - 1), column)
        return index_map

    fixed2 = lambda step, span_ref: (0, 0)
    fixed3 = lambda step, span_ref: (0, 0, 0)
    in_specs = [
        pl.BlockSpec((rows, width), fixed2),
        pl.BlockSpec((block, HD), kv_map(0)),
        pl.BlockSpec((block, HD), kv_map(1)),
        pl.BlockSpec((rows, 1), fixed2),
        pl.BlockSpec((rows, 1), fixed2),
    ]
    state_shapes = [
        jax.ShapeDtypeStruct((heads, rows, 1), jnp.float32),
        jax.ShapeDtypeStruct((heads, rows, 1), jnp.float32),
        jax.ShapeDtypeStruct((heads, rows, HD), jnp.float32),
    ]
    state_specs = [pl.BlockSpec(x.shape, fixed3) for x in state_shapes]
    if final:
        in_specs = in_specs + state_specs
        out_specs = pl.BlockSpec((rows, width), fixed2)
        out_shape = jax.ShapeDtypeStruct((rows, width), jnp.bfloat16)
        scratch = [pltpu.VMEM(x.shape, jnp.float32) for x in state_shapes]
        operands = (span, queries, kv_part, kv_part, row_start, row_index) + tuple(state)
    else:
        out_specs = state_specs
        out_shape = state_shapes
        scratch = []
        operands = (span, queries, kv_part, kv_part, row_start, row_index)
    grid_spec = pltpu.PrefetchScalarGridSpec(
        num_scalar_prefetch=1,
        grid=(max_blocks,),
        in_specs=in_specs,
        out_specs=out_specs,
        scratch_shapes=scratch,
    )
    flops = 4 * heads * rows * block * HD * max_blocks
    return pl.pallas_call(
        functools.partial(flash_kernel, final),
        grid_spec=grid_spec,
        out_shape=out_shape,
        compiler_params=pltpu.CompilerParams(dimension_semantics=("arbitrary",)),
        cost_estimate=pl.CostEstimate(
            flops=flops,
            transcendentals=heads * rows * block * max_blocks,
            bytes_accessed=2 * block * HD * 2 * max_blocks + 2 * 2 * rows * width,
        ),
    )(*operands)


def local(hidden_rows, destination, doc_ids, norm_gain, w_query, w_key, w_value, w_out):
    owners = lax.axis_size(("chip", "core"))
    my_index = lax.axis_index(("chip", "core"))
    tok_dev, columns = hidden_rows.shape
    capacity = 2 * tok_dev // owners
    target = destination // tok_dev
    owner_ids = jnp.arange(owners, dtype=jnp.int32)
    one_hot = (target[:, None] == owner_ids[None, :]).astype(jnp.int32)
    slot_rank = jnp.sum((jnp.cumsum(one_hot, axis=0) - 1) * one_hot, axis=1)
    flat_slot = target * capacity + slot_rank
    outgoing = (
        jnp.zeros((owners * capacity, columns), hidden_rows.dtype).at[flat_slot].set(hidden_rows)
    )
    places = (
        jnp.full((owners * capacity,), tok_dev, jnp.int32).at[flat_slot].set(destination % tok_dev)
    )
    block_first = my_index * tok_dev
    first_id = doc_ids[0]
    last_id = doc_ids[tok_dev - 1]
    less_count = jnp.sum((doc_ids[None, :] < doc_ids[:, None]).astype(jnp.int32), axis=1)
    last_run_start = block_first + less_count[tok_dev - 1]
    info = jnp.broadcast_to(jnp.stack([last_id, last_run_start])[None, :], (owners, 2))
    places_info = jnp.concatenate([places.reshape(owners, capacity), info], axis=1)
    arrived = lax.all_to_all(
        outgoing.reshape(owners, capacity, columns), ("chip", "core"), split_axis=0, concat_axis=0, tiled=True
    )
    arrived_info = lax.all_to_all(places_info, ("chip", "core"), split_axis=0, concat_axis=0, tiled=True)
    arrived_rows = arrived_info[:, :capacity].reshape(-1)
    peer_last_id = arrived_info[:, capacity]
    peer_run_start = arrived_info[:, capacity + 1]
    earlier = (owner_ids < my_index) & (peer_last_id == first_id)
    doc_low = jnp.minimum(block_first, jnp.min(jnp.where(earlier, peer_run_start, block_first)))
    row_index = block_first + jnp.arange(tok_dev, dtype=jnp.int32)
    row_start = jnp.where(doc_ids == first_id, doc_low, block_first + less_count)

    routed_part = (
        jnp.zeros((tok_dev, columns), hidden_rows.dtype)
        .at[arrived_rows]
        .set(arrived.reshape(-1, columns), mode="drop")
    )
    half = tok_dev // 2
    mp_size = lax.axis_size("mp")
    routed_low = lax.all_gather(routed_part[:half], "mp", axis=1, tiled=True)
    copies = jnp.broadcast_to(routed_part[half:][None], (mp_size, half, columns))
    pieces = lax.all_to_all(copies, "mp", split_axis=0, concat_axis=0, tiled=True)
    routed_high = jnp.transpose(pieces, (1, 0, 2)).reshape(half, mp_size * columns)
    heads_dev = w_query.shape[1] // HD
    kv_dev = w_key.shape[1] // HD

    def project(routed_rows, rows):
        normed = normalize(routed_rows, norm_gain)
        angles = rope_angles(rows)
        queries = jnp.dot(normed, w_query, preferred_element_type=jnp.float32).reshape(
            rows.shape[0], heads_dev, HD
        )
        queries = rotate(queries, angles).astype(jnp.bfloat16).reshape(rows.shape[0], heads_dev * HD)
        keys = jnp.dot(normed, w_key, preferred_element_type=jnp.float32).reshape(
            rows.shape[0], kv_dev, HD
        )
        keys = rotate(keys, angles).astype(jnp.bfloat16).reshape(rows.shape[0], kv_dev * HD)
        values = jnp.dot(normed, w_value, preferred_element_type=jnp.float32).astype(jnp.bfloat16)
        return queries, jnp.concatenate([keys, values], axis=1)

    queries_low, kv_a = project(routed_low, row_index[:half])
    kv_low = lax.all_gather(kv_a, ("chip", "core"), axis=0, tiled=True)
    queries_high, kv_b = project(routed_high, row_index[half:])
    kv_high = lax.all_gather(kv_b, ("chip", "core"), axis=0, tiled=True)
    queries = jnp.concatenate([queries_low, queries_high], axis=0)

    block = KEY_BLOCK
    last_block = (block_first + tok_dev - 1) // block
    first_block = doc_low // block
    max_blocks = min((tok_dev - 1) // block + -(-(DOC_MAX - 1) // block) + 1, owners * tok_dev // block)
    max_start = jnp.max(row_start)

    def span_for(offset):
        return jnp.stack(
            [first_block, last_block - first_block + 1, max_start, block_first, block, offset]
        ).astype(jnp.int32)

    state = flash_pass(
        span_for(0), queries, kv_low, row_start[:, None], row_index[:, None], max_blocks, None
    )
    context = flash_pass(
        span_for(half), queries, kv_high, row_start[:, None], row_index[:, None], max_blocks, state
    )
    context_all = lax.all_gather(context, "mp", axis=1, tiled=True)
    w_split = jnp.transpose(w_out.reshape(w_out.shape[0], mp_size, -1), (1, 0, 2))
    w_cols = lax.all_to_all(w_split, "mp", split_axis=0, concat_axis=0, tiled=True)
    summed = jnp.dot(
        context_all, w_cols.reshape(-1, w_cols.shape[2]), preferred_element_type=jnp.float32
    )
    attended = (routed_part.astype(jnp.float32) + summed).astype(jnp.bfloat16)
    backward = attended[jnp.minimum(arrived_rows, tok_dev - 1)].reshape(owners, capacity, columns)
    returned = lax.all_to_all(backward, ("chip", "core"), split_axis=0, concat_axis=0, tiled=True)
    return returned.reshape(owners * capacity, columns)[flat_slot]


def solution(mesh):
    dp_size, mp_size = mesh.devices.shape
    split_mesh = jax.sharding.Mesh(
        mesh.devices.reshape(dp_size // 2, 2, mp_size), ("chip", "core", "mp")
    )
    rows = ("chip", "core")
    in_specs = (
        P(rows, "mp"),
        P(rows),
        P(rows),
        P(),
        P(None, "mp"),
        P(None, "mp"),
        P(None, "mp"),
        P("mp", None),
    )
    out_specs = P(rows, "mp")
    return jax.shard_map(
        local, mesh=split_mesh, in_specs=in_specs, out_specs=out_specs, check_vma=False
    )
```

```python
import functools
import math

import jax
import jax.numpy as jnp
from jax import lax
from jax.experimental import pallas as pl
from jax.experimental.pallas import tpu as pltpu
from jax.sharding import PartitionSpec as P

HD = 128
DOC_MAX = 8704

ROPE_BASE = 500000.0
NORM_EPS = 1e-05
NEG_START = -1e30
KEY_BLOCK = 512


def rope_angles(row_index):
    lane_index = jnp.arange(HD // 2, dtype=jnp.float32)
    frequency = jnp.power(jnp.float32(ROPE_BASE), -2.0 * lane_index / HD)
    return row_index.astype(jnp.float32)[:, None] * frequency[None, :]


def rotate(head_values, angles):
    half_width = head_values.shape[-1] // 2
    first_half = head_values[..., :half_width]
    second_half = head_values[..., half_width:]
    cosine = jnp.cos(angles)[:, None, :]
    sine_part = jnp.sin(angles)[:, None, :]
    return jnp.concatenate(
        [
            first_half * cosine - second_half * sine_part,
            second_half * cosine + first_half * sine_part,
        ],
        axis=-1,
    )


def normalize(routed, norm_gain):
    wide_rows = routed.astype(jnp.float32)
    inv_rms = lax.rsqrt(jnp.mean(wide_rows * wide_rows, axis=1, keepdims=True) + NORM_EPS)
    return (wide_rows * inv_rms * norm_gain[None, :]).astype(jnp.bfloat16)


def flash_kernel(final, span_ref, *refs):
    if final:
        q_ref, k_ref, v_ref, start_ref, row_ref, m_in, l_in, acc_in, o_ref, m_sc, l_sc, acc_sc = refs
    else:
        q_ref, k_ref, v_ref, start_ref, row_ref, m_sc, l_sc, acc_sc = refs
    step = pl.program_id(0)
    heads = m_sc.shape[0]
    block = k_ref.shape[0]
    scale = HD ** (-0.5)

    @pl.when(step == 0)
    def _init():
        if final:
            m_sc[...] = m_in[...]
            l_sc[...] = l_in[...]
            acc_sc[...] = acc_in[...]
        else:
            m_sc[...] = jnp.full(m_sc.shape, NEG_START, jnp.float32)
            l_sc[...] = jnp.zeros(l_sc.shape, jnp.float32)
            acc_sc[...] = jnp.zeros(acc_sc.shape, jnp.float32)

    key_first = (span_ref[0] + step) * span_ref[4] + span_ref[5]
    active = step < span_ref[1]
    whole = (key_first >= span_ref[2]) & (key_first + block - 1 <= span_ref[3])

    def accumulate(masked):
        keys = k_ref[...]
        values = v_ref[...]
        if masked:
            key_rows = key_first + lax.broadcasted_iota(jnp.int32, (block, 1), 0)
            allowed = (key_rows >= start_ref[...]) & (key_rows <= row_ref[...])
        for h in range(heads):
            scores = jnp.dot(keys, q_ref[h], preferred_element_type=jnp.float32) * scale
            if masked:
                scores = jnp.where(allowed, scores, -jnp.inf)
            m_old = m_sc[h]
            m_new = jnp.maximum(m_old, jnp.max(scores, axis=0, keepdims=True))
            rescale = jnp.exp(m_old - m_new)
            exp_scores = jnp.exp(scores - m_new)
            l_sc[h] = l_sc[h] * rescale + jnp.sum(exp_scores, axis=0, keepdims=True)
            acc_sc[h] = acc_sc[h] * rescale + lax.dot_general(
                values, exp_scores.astype(jnp.bfloat16), (((0,), (0,)), ((), ())),
                preferred_element_type=jnp.float32,
            )
            m_sc[h] = m_new

    @pl.when(active & whole)
    def _whole():
        accumulate(False)

    @pl.when(active & jnp.logical_not(whole))
    def _masked():
        accumulate(True)

    if final:
        @pl.when(step == pl.num_programs(0) - 1)
        def _finish():
            for h in range(heads):
                o_ref[h] = (acc_sc[h] / l_sc[h]).astype(o_ref.dtype)


def flash_pass(span, queries_t, kv_part, row_start, row_index, block, max_blocks, state):
    heads, _, rows = queries_t.shape
    final = state is not None

    def kv_map(column):
        def index_map(step, span_ref):
            return (span_ref[0] + jnp.minimum(step, span_ref[1] - 1), column)
        return index_map

    fixed2 = lambda step, span_ref: (0, 0)
    fixed3 = lambda step, span_ref: (0, 0, 0)
    in_specs = [
        pl.BlockSpec((heads, HD, rows), fixed3),
        pl.BlockSpec((block, HD), kv_map(0)),
        pl.BlockSpec((block, HD), kv_map(1)),
        pl.BlockSpec((1, rows), fixed2),
        pl.BlockSpec((1, rows), fixed2),
    ]
    state_shapes = [
        jax.ShapeDtypeStruct((heads, 1, rows), jnp.float32),
        jax.ShapeDtypeStruct((heads, 1, rows), jnp.float32),
        jax.ShapeDtypeStruct((heads, HD, rows), jnp.float32),
    ]
    state_specs = [pl.BlockSpec(x.shape, fixed3) for x in state_shapes]
    if final:
        in_specs = in_specs + state_specs
        out_specs = pl.BlockSpec((heads, HD, rows), fixed3)
        out_shape = jax.ShapeDtypeStruct((heads, HD, rows), jnp.bfloat16)
        scratch = [pltpu.VMEM(x.shape, jnp.float32) for x in state_shapes]
        operands = (span, queries_t, kv_part, kv_part, row_start, row_index) + tuple(state)
    else:
        out_specs = state_specs
        out_shape = state_shapes
        scratch = []
        operands = (span, queries_t, kv_part, kv_part, row_start, row_index)
    grid_spec = pltpu.PrefetchScalarGridSpec(
        num_scalar_prefetch=1,
        grid=(max_blocks,),
        in_specs=in_specs,
        out_specs=out_specs,
        scratch_shapes=scratch,
    )
    flops = 4 * heads * rows * block * HD * max_blocks
    return pl.pallas_call(
        functools.partial(flash_kernel, final),
        grid_spec=grid_spec,
        out_shape=out_shape,
        compiler_params=pltpu.CompilerParams(dimension_semantics=("arbitrary",)),
        cost_estimate=pl.CostEstimate(
            flops=flops,
            transcendentals=heads * rows * block * max_blocks,
            bytes_accessed=2 * block * HD * 2 * max_blocks + 2 * 2 * rows * heads * HD,
        ),
    )(*operands)


def local(hidden_rows, destination, doc_ids, norm_gain, w_query, w_key, w_value, w_out):
    owners = lax.axis_size(("chip", "core"))
    my_index = lax.axis_index(("chip", "core"))
    tok_dev, columns = hidden_rows.shape
    capacity = 2 * tok_dev // owners
    target = destination // tok_dev
    owner_ids = jnp.arange(owners, dtype=jnp.int32)
    one_hot = (target[:, None] == owner_ids[None, :]).astype(jnp.int32)
    slot_rank = jnp.sum((jnp.cumsum(one_hot, axis=0) - 1) * one_hot, axis=1)
    flat_slot = target * capacity + slot_rank
    outgoing = (
        jnp.zeros((owners * capacity, columns), hidden_rows.dtype).at[flat_slot].set(hidden_rows)
    )
    places = (
        jnp.full((owners * capacity,), tok_dev, jnp.int32).at[flat_slot].set(destination % tok_dev)
    )
    block_first = my_index * tok_dev
    first_id = doc_ids[0]
    last_id = doc_ids[tok_dev - 1]
    less_count = jnp.sum((doc_ids[None, :] < doc_ids[:, None]).astype(jnp.int32), axis=1)
    last_run_start = block_first + less_count[tok_dev - 1]
    info = jnp.broadcast_to(jnp.stack([last_id, last_run_start])[None, :], (owners, 2))
    places_info = jnp.concatenate([places.reshape(owners, capacity), info], axis=1)
    arrived = lax.all_to_all(
        outgoing.reshape(owners, capacity, columns), ("chip", "core"), split_axis=0, concat_axis=0, tiled=True
    )
    arrived_info = lax.all_to_all(places_info, ("chip", "core"), split_axis=0, concat_axis=0, tiled=True)
    arrived_rows = arrived_info[:, :capacity].reshape(-1)
    peer_last_id = arrived_info[:, capacity]
    peer_run_start = arrived_info[:, capacity + 1]
    earlier = (owner_ids < my_index) & (peer_last_id == first_id)
    doc_low = jnp.minimum(block_first, jnp.min(jnp.where(earlier, peer_run_start, block_first)))
    row_index = block_first + jnp.arange(tok_dev, dtype=jnp.int32)
    row_start = jnp.where(doc_ids == first_id, doc_low, block_first + less_count)

    routed_part = (
        jnp.zeros((tok_dev, columns), hidden_rows.dtype)
        .at[arrived_rows]
        .set(arrived.reshape(-1, columns), mode="drop")
    )
    routed = lax.all_gather(routed_part, "mp", axis=1, tiled=True)
    normed = normalize(routed, norm_gain)
    heads_dev = w_query.shape[1] // HD
    kv_dev = w_key.shape[1] // HD
    angles = rope_angles(row_index)
    queries = jnp.dot(normed, w_query, preferred_element_type=jnp.float32).reshape(
        tok_dev, heads_dev, HD
    )
    queries = rotate(queries, angles).astype(jnp.bfloat16).reshape(tok_dev, heads_dev * HD)
    keys_own = jnp.dot(normed, w_key, preferred_element_type=jnp.float32).reshape(
        tok_dev, kv_dev, HD
    )
    keys_own = rotate(keys_own, angles).astype(jnp.bfloat16).reshape(tok_dev, kv_dev * HD)
    values_own = jnp.dot(normed, w_value, preferred_element_type=jnp.float32).astype(jnp.bfloat16)
    kv_own = jnp.concatenate([keys_own, values_own], axis=1)
    half = tok_dev // 2
    kv_low = lax.all_gather(kv_own[:half], ("chip", "core"), axis=0, tiled=True)
    kv_high = lax.all_gather(kv_own[half:], ("chip", "core"), axis=0, tiled=True)

    block = KEY_BLOCK
    last_block = (block_first + tok_dev - 1) // block
    first_block = doc_low // block
    max_blocks = min((tok_dev - 1) // block + -(-(DOC_MAX - 1) // block) + 1, owners * tok_dev // block)
    max_start = jnp.max(row_start)

    def span_for(offset):
        return jnp.stack(
            [first_block, last_block - first_block + 1, max_start, block_first, block, offset]
        ).astype(jnp.int32)

    queries_t = jnp.transpose(queries.reshape(tok_dev, heads_dev, HD), (1, 2, 0))
    state = flash_pass(
        span_for(0), queries_t, kv_low, row_start[None, :], row_index[None, :], half, max_blocks, None
    )
    context_t = flash_pass(
        span_for(half), queries_t, kv_high, row_start[None, :], row_index[None, :], half, max_blocks,
        state,
    )
    context = jnp.transpose(context_t, (2, 0, 1)).reshape(tok_dev, heads_dev * HD)
    context_all = lax.all_gather(context, "mp", axis=1, tiled=True)
    mp_size = lax.axis_size("mp")
    w_split = jnp.transpose(w_out.reshape(w_out.shape[0], mp_size, -1), (1, 0, 2))
    w_cols = lax.all_to_all(w_split, "mp", split_axis=0, concat_axis=0, tiled=True)
    summed = jnp.dot(
        context_all, w_cols.reshape(-1, w_cols.shape[2]), preferred_element_type=jnp.float32
    )
    attended = (routed_part.astype(jnp.float32) + summed).astype(jnp.bfloat16)
    backward = attended[jnp.minimum(arrived_rows, tok_dev - 1)].reshape(owners, capacity, columns)
    returned = lax.all_to_all(backward, ("chip", "core"), split_axis=0, concat_axis=0, tiled=True)
    return returned.reshape(owners * capacity, columns)[flat_slot]


def solution(mesh):
    dp_size, mp_size = mesh.devices.shape
    split_mesh = jax.sharding.Mesh(
        mesh.devices.reshape(dp_size // 2, 2, mp_size), ("chip", "core", "mp")
    )
    rows = ("chip", "core")
    in_specs = (
        P(rows, "mp"),
        P(rows),
        P(rows),
        P(),
        P(None, "mp"),
        P(None, "mp"),
        P(None, "mp"),
        P("mp", None),
    )
    out_specs = P(rows, "mp")
    return jax.shard_map(
        local, mesh=split_mesh, in_specs=in_specs, out_specs=out_specs, check_vma=False
    )
```

```python
import functools
import math

import jax
import jax.numpy as jnp
from jax import lax
from jax.experimental import pallas as pl
from jax.experimental.pallas import tpu as pltpu
from jax.sharding import PartitionSpec as P

HD = 128
DOC_MAX = 8704

ROPE_BASE = 500000.0
NORM_EPS = 1e-05
NEG_START = -1e30
KEY_BLOCK = 512


def rope_angles(row_index):
    lane_index = jnp.arange(HD // 2, dtype=jnp.float32)
    frequency = jnp.power(jnp.float32(ROPE_BASE), -2.0 * lane_index / HD)
    return row_index.astype(jnp.float32)[:, None] * frequency[None, :]


def rotate(head_values, angles):
    half_width = head_values.shape[-1] // 2
    first_half = head_values[..., :half_width]
    second_half = head_values[..., half_width:]
    cosine = jnp.cos(angles)[:, None, :]
    sine_part = jnp.sin(angles)[:, None, :]
    return jnp.concatenate(
        [
            first_half * cosine - second_half * sine_part,
            second_half * cosine + first_half * sine_part,
        ],
        axis=-1,
    )


def normalize(routed, norm_gain):
    wide_rows = routed.astype(jnp.float32)
    inv_rms = lax.rsqrt(jnp.mean(wide_rows * wide_rows, axis=1, keepdims=True) + NORM_EPS)
    return (wide_rows * inv_rms * norm_gain[None, :]).astype(jnp.bfloat16)


def flash_kernel(final, span_ref, *refs):
    if final:
        q_ref, k_ref, v_ref, start_ref, row_ref, m_in, l_in, acc_in, o_ref, m_sc, l_sc, acc_sc = refs
    else:
        q_ref, k_ref, v_ref, start_ref, row_ref, m_sc, l_sc, acc_sc = refs
    step = pl.program_id(0)
    heads = m_sc.shape[0]
    block = k_ref.shape[0]
    scale = HD ** (-0.5)

    @pl.when(step == 0)
    def _init():
        if final:
            m_sc[...] = m_in[...]
            l_sc[...] = l_in[...]
            acc_sc[...] = acc_in[...]
        else:
            m_sc[...] = jnp.full(m_sc.shape, NEG_START, jnp.float32)
            l_sc[...] = jnp.zeros(l_sc.shape, jnp.float32)
            acc_sc[...] = jnp.zeros(acc_sc.shape, jnp.float32)

    key_first = (span_ref[0] + step) * span_ref[4] + span_ref[5]
    active = step < span_ref[1]
    whole = (key_first >= span_ref[2]) & (key_first + block - 1 <= span_ref[3])

    def accumulate(masked):
        keys = k_ref[...]
        values = v_ref[...]
        if masked:
            key_rows = key_first + lax.broadcasted_iota(jnp.int32, (block, 1), 0)
            allowed = (key_rows >= start_ref[...]) & (key_rows <= row_ref[...])
        for h in range(heads):
            scores = jnp.dot(keys, q_ref[h], preferred_element_type=jnp.float32) * scale
            if masked:
                scores = jnp.where(allowed, scores, -jnp.inf)
            m_old = m_sc[h]
            m_new = jnp.maximum(m_old, jnp.max(scores, axis=0, keepdims=True))
            rescale = jnp.exp(m_old - m_new)
            exp_scores = jnp.exp(scores - m_new)
            l_sc[h] = l_sc[h] * rescale + jnp.sum(exp_scores, axis=0, keepdims=True)
            acc_sc[h] = acc_sc[h] * rescale + lax.dot_general(
                values, exp_scores.astype(jnp.bfloat16), (((0,), (0,)), ((), ())),
                preferred_element_type=jnp.float32,
            )
            m_sc[h] = m_new

    @pl.when(active & whole)
    def _whole():
        accumulate(False)

    @pl.when(active & jnp.logical_not(whole))
    def _masked():
        accumulate(True)

    if final:
        @pl.when(step == pl.num_programs(0) - 1)
        def _finish():
            for h in range(heads):
                o_ref[h] = (acc_sc[h] / l_sc[h]).astype(o_ref.dtype)


def flash_pass(span, queries_t, kv_part, row_start, row_index, block, max_blocks, state):
    heads, _, rows = queries_t.shape
    final = state is not None

    def kv_map(column):
        def index_map(step, span_ref):
            return (span_ref[0] + jnp.minimum(step, span_ref[1] - 1), column)
        return index_map

    fixed2 = lambda step, span_ref: (0, 0)
    fixed3 = lambda step, span_ref: (0, 0, 0)
    in_specs = [
        pl.BlockSpec((heads, HD, rows), fixed3),
        pl.BlockSpec((block, HD), kv_map(0)),
        pl.BlockSpec((block, HD), kv_map(1)),
        pl.BlockSpec((1, rows), fixed2),
        pl.BlockSpec((1, rows), fixed2),
    ]
    state_shapes = [
        jax.ShapeDtypeStruct((heads, 1, rows), jnp.float32),
        jax.ShapeDtypeStruct((heads, 1, rows), jnp.float32),
        jax.ShapeDtypeStruct((heads, HD, rows), jnp.float32),
    ]
    state_specs = [pl.BlockSpec(x.shape, fixed3) for x in state_shapes]
    if final:
        in_specs = in_specs + state_specs
        out_specs = pl.BlockSpec((heads, HD, rows), fixed3)
        out_shape = jax.ShapeDtypeStruct((heads, HD, rows), jnp.bfloat16)
        scratch = [pltpu.VMEM(x.shape, jnp.float32) for x in state_shapes]
        operands = (span, queries_t, kv_part, kv_part, row_start, row_index) + tuple(state)
    else:
        out_specs = state_specs
        out_shape = state_shapes
        scratch = []
        operands = (span, queries_t, kv_part, kv_part, row_start, row_index)
    grid_spec = pltpu.PrefetchScalarGridSpec(
        num_scalar_prefetch=1,
        grid=(max_blocks,),
        in_specs=in_specs,
        out_specs=out_specs,
        scratch_shapes=scratch,
    )
    flops = 4 * heads * rows * block * HD * max_blocks
    return pl.pallas_call(
        functools.partial(flash_kernel, final),
        grid_spec=grid_spec,
        out_shape=out_shape,
        compiler_params=pltpu.CompilerParams(dimension_semantics=("arbitrary",)),
        cost_estimate=pl.CostEstimate(
            flops=flops,
            transcendentals=heads * rows * block * max_blocks,
            bytes_accessed=2 * block * HD * 2 * max_blocks + 2 * 2 * rows * heads * HD,
        ),
    )(*operands)


def local(hidden_rows, destination, doc_ids, norm_gain, w_query, w_key, w_value, w_out):
    owners = lax.axis_size(("chip", "core"))
    my_index = lax.axis_index(("chip", "core"))
    tok_dev, columns = hidden_rows.shape
    capacity = 2 * tok_dev // owners
    target = destination // tok_dev
    owner_ids = jnp.arange(owners, dtype=jnp.int32)
    one_hot = (target[:, None] == owner_ids[None, :]).astype(jnp.int32)
    slot_rank = jnp.sum((jnp.cumsum(one_hot, axis=0) - 1) * one_hot, axis=1)
    flat_slot = target * capacity + slot_rank
    outgoing = (
        jnp.zeros((owners * capacity, columns), hidden_rows.dtype).at[flat_slot].set(hidden_rows)
    )
    places = (
        jnp.full((owners * capacity,), tok_dev, jnp.int32).at[flat_slot].set(destination % tok_dev)
    )
    block_first = my_index * tok_dev
    first_id = doc_ids[0]
    last_id = doc_ids[tok_dev - 1]
    less_count = jnp.sum((doc_ids[None, :] < doc_ids[:, None]).astype(jnp.int32), axis=1)
    last_run_start = block_first + less_count[tok_dev - 1]
    info = jnp.broadcast_to(jnp.stack([last_id, last_run_start])[None, :], (owners, 2))
    places_info = jnp.concatenate([places.reshape(owners, capacity), info], axis=1)
    arrived = lax.all_to_all(
        outgoing.reshape(owners, capacity, columns), ("chip", "core"), split_axis=0, concat_axis=0, tiled=True
    )
    arrived_info = lax.all_to_all(places_info, ("chip", "core"), split_axis=0, concat_axis=0, tiled=True)
    arrived_rows = arrived_info[:, :capacity].reshape(-1)
    peer_last_id = arrived_info[:, capacity]
    peer_run_start = arrived_info[:, capacity + 1]
    earlier = (owner_ids < my_index) & (peer_last_id == first_id)
    doc_low = jnp.minimum(block_first, jnp.min(jnp.where(earlier, peer_run_start, block_first)))
    row_index = block_first + jnp.arange(tok_dev, dtype=jnp.int32)
    row_start = jnp.where(doc_ids == first_id, doc_low, block_first + less_count)

    routed_part = (
        jnp.zeros((tok_dev, columns), hidden_rows.dtype)
        .at[arrived_rows]
        .set(arrived.reshape(-1, columns), mode="drop")
    )
    routed = lax.all_gather(routed_part, "mp", axis=1, tiled=True)
    normed = normalize(routed, norm_gain)
    heads_dev = w_query.shape[1] // HD
    kv_dev = w_key.shape[1] // HD
    angles = rope_angles(row_index)
    queries = jnp.dot(normed, w_query, preferred_element_type=jnp.float32).reshape(
        tok_dev, heads_dev, HD
    )
    queries = rotate(queries, angles).astype(jnp.bfloat16).reshape(tok_dev, heads_dev * HD)
    keys_own = jnp.dot(normed, w_key, preferred_element_type=jnp.float32).reshape(
        tok_dev, kv_dev, HD
    )
    keys_own = rotate(keys_own, angles).astype(jnp.bfloat16).reshape(tok_dev, kv_dev * HD)
    values_own = jnp.dot(normed, w_value, preferred_element_type=jnp.float32).astype(jnp.bfloat16)
    kv_own = jnp.concatenate([keys_own, values_own], axis=1)
    half = tok_dev // 2
    kv_low = lax.all_gather(kv_own[:half], ("chip", "core"), axis=0, tiled=True)
    kv_copies = jnp.broadcast_to(kv_own[half:][None], (owners, half, kv_own.shape[1]))
    kv_high = lax.all_to_all(
        kv_copies, ("chip", "core"), split_axis=0, concat_axis=0, tiled=True
    ).reshape(owners * half, kv_own.shape[1])

    block = KEY_BLOCK
    last_block = (block_first + tok_dev - 1) // block
    first_block = doc_low // block
    max_blocks = min((tok_dev - 1) // block + -(-(DOC_MAX - 1) // block) + 1, owners * tok_dev // block)
    max_start = jnp.max(row_start)

    def span_for(offset):
        return jnp.stack(
            [first_block, last_block - first_block + 1, max_start, block_first, block, offset]
        ).astype(jnp.int32)

    queries_t = jnp.transpose(queries.reshape(tok_dev, heads_dev, HD), (1, 2, 0))
    state = flash_pass(
        span_for(0), queries_t, kv_low, row_start[None, :], row_index[None, :], half, max_blocks, None
    )
    context_t = flash_pass(
        span_for(half), queries_t, kv_high, row_start[None, :], row_index[None, :], half, max_blocks,
        state,
    )
    context = jnp.transpose(context_t, (2, 0, 1)).reshape(tok_dev, heads_dev * HD)
    context_all = lax.all_gather(context, "mp", axis=1, tiled=True)
    mp_size = lax.axis_size("mp")
    w_split = jnp.transpose(w_out.reshape(w_out.shape[0], mp_size, -1), (1, 0, 2))
    w_cols = lax.all_to_all(w_split, "mp", split_axis=0, concat_axis=0, tiled=True)
    summed = jnp.einsum(
        "tsr,src->tc",
        context_all.reshape(tok_dev, mp_size, -1),
        w_cols,
        preferred_element_type=jnp.float32,
    )
    attended = (routed_part.astype(jnp.float32) + summed).astype(jnp.bfloat16)
    backward = attended[jnp.minimum(arrived_rows, tok_dev - 1)].reshape(owners, capacity, columns)
    returned = lax.all_to_all(backward, ("chip", "core"), split_axis=0, concat_axis=0, tiled=True)
    return returned.reshape(owners * capacity, columns)[flat_slot]


def solution(mesh):
    dp_size, mp_size = mesh.devices.shape
    split_mesh = jax.sharding.Mesh(
        mesh.devices.reshape(dp_size // 2, 2, mp_size), ("chip", "core", "mp")
    )
    rows = ("chip", "core")
    in_specs = (
        P(rows, "mp"),
        P(rows),
        P(rows),
        P(),
        P(None, "mp"),
        P(None, "mp"),
        P(None, "mp"),
        P("mp", None),
    )
    out_specs = P(rows, "mp")
    return jax.shard_map(
        local, mesh=split_mesh, in_specs=in_specs, out_specs=out_specs, check_vma=False
    )
```

```python
import functools
import math

import jax
import jax.numpy as jnp
from jax import lax
from jax.experimental import pallas as pl
from jax.experimental.pallas import tpu as pltpu
from jax.sharding import PartitionSpec as P

HD = 128
DOC_MAX = 8704

ROPE_BASE = 500000.0
NORM_EPS = 1e-05
NEG_START = -1e30
KEY_BLOCK = 512


def rope_angles(row_index):
    lane_index = jnp.arange(HD // 2, dtype=jnp.float32)
    frequency = jnp.power(jnp.float32(ROPE_BASE), -2.0 * lane_index / HD)
    return row_index.astype(jnp.float32)[:, None] * frequency[None, :]


def rotate(head_values, angles):
    half_width = head_values.shape[-1] // 2
    first_half = head_values[..., :half_width]
    second_half = head_values[..., half_width:]
    cosine = jnp.cos(angles)[:, None, :]
    sine_part = jnp.sin(angles)[:, None, :]
    return jnp.concatenate(
        [
            first_half * cosine - second_half * sine_part,
            second_half * cosine + first_half * sine_part,
        ],
        axis=-1,
    )


def normalize(routed, norm_gain):
    wide_rows = routed.astype(jnp.float32)
    inv_rms = lax.rsqrt(jnp.mean(wide_rows * wide_rows, axis=1, keepdims=True) + NORM_EPS)
    return (wide_rows * inv_rms * norm_gain[None, :]).astype(jnp.bfloat16)


def flash_kernel(final, span_ref, *refs):
    if final:
        q_ref, k_ref, v_ref, start_ref, row_ref, m_in, l_in, acc_in, o_ref, m_sc, l_sc, acc_sc = refs
    else:
        q_ref, k_ref, v_ref, start_ref, row_ref, m_sc, l_sc, acc_sc = refs
    step = pl.program_id(0)
    heads = m_sc.shape[0]
    block = k_ref.shape[0]
    scale = HD ** (-0.5)

    @pl.when(step == 0)
    def _init():
        if final:
            m_sc[...] = m_in[...]
            l_sc[...] = l_in[...]
            acc_sc[...] = acc_in[...]
        else:
            m_sc[...] = jnp.full(m_sc.shape, NEG_START, jnp.float32)
            l_sc[...] = jnp.zeros(l_sc.shape, jnp.float32)
            acc_sc[...] = jnp.zeros(acc_sc.shape, jnp.float32)

    key_first = (span_ref[0] + step) * span_ref[4] + span_ref[5]
    active = step < span_ref[1]
    whole = (key_first >= span_ref[2]) & (key_first + block - 1 <= span_ref[3])

    def accumulate(masked):
        keys = k_ref[...]
        values = v_ref[...]
        if masked:
            key_rows = key_first + lax.broadcasted_iota(jnp.int32, (block, 1), 0)
            allowed = (key_rows >= start_ref[...]) & (key_rows <= row_ref[...])
        for h in range(heads):
            scores = jnp.dot(keys, q_ref[h], preferred_element_type=jnp.float32) * scale
            if masked:
                scores = jnp.where(allowed, scores, -jnp.inf)
            m_old = m_sc[h]
            m_new = jnp.maximum(m_old, jnp.max(scores, axis=0, keepdims=True))
            rescale = jnp.exp(m_old - m_new)
            exp_scores = jnp.exp(scores - m_new)
            l_sc[h] = l_sc[h] * rescale + jnp.sum(exp_scores, axis=0, keepdims=True)
            acc_sc[h] = acc_sc[h] * rescale + lax.dot_general(
                values, exp_scores.astype(jnp.bfloat16), (((0,), (0,)), ((), ())),
                preferred_element_type=jnp.float32,
            )
            m_sc[h] = m_new

    @pl.when(active & whole)
    def _whole():
        accumulate(False)

    @pl.when(active & jnp.logical_not(whole))
    def _masked():
        accumulate(True)

    if final:
        @pl.when(step == pl.num_programs(0) - 1)
        def _finish():
            for h in range(heads):
                o_ref[h] = (acc_sc[h] / l_sc[h]).astype(o_ref.dtype)


def flash_pass(span, queries_t, kv_part, row_start, row_index, block, max_blocks, state):
    heads, _, rows = queries_t.shape
    final = state is not None

    def kv_map(column):
        def index_map(step, span_ref):
            return (span_ref[0] + jnp.minimum(step, span_ref[1] - 1), column)
        return index_map

    fixed2 = lambda step, span_ref: (0, 0)
    fixed3 = lambda step, span_ref: (0, 0, 0)
    in_specs = [
        pl.BlockSpec((heads, HD, rows), fixed3),
        pl.BlockSpec((block, HD), kv_map(0)),
        pl.BlockSpec((block, HD), kv_map(1)),
        pl.BlockSpec((1, rows), fixed2),
        pl.BlockSpec((1, rows), fixed2),
    ]
    state_shapes = [
        jax.ShapeDtypeStruct((heads, 1, rows), jnp.float32),
        jax.ShapeDtypeStruct((heads, 1, rows), jnp.float32),
        jax.ShapeDtypeStruct((heads, HD, rows), jnp.float32),
    ]
    state_specs = [pl.BlockSpec(x.shape, fixed3) for x in state_shapes]
    if final:
        in_specs = in_specs + state_specs
        out_specs = pl.BlockSpec((heads, HD, rows), fixed3)
        out_shape = jax.ShapeDtypeStruct((heads, HD, rows), jnp.bfloat16)
        scratch = [pltpu.VMEM(x.shape, jnp.float32) for x in state_shapes]
        operands = (span, queries_t, kv_part, kv_part, row_start, row_index) + tuple(state)
    else:
        out_specs = state_specs
        out_shape = state_shapes
        scratch = []
        operands = (span, queries_t, kv_part, kv_part, row_start, row_index)
    grid_spec = pltpu.PrefetchScalarGridSpec(
        num_scalar_prefetch=1,
        grid=(max_blocks,),
        in_specs=in_specs,
        out_specs=out_specs,
        scratch_shapes=scratch,
    )
    flops = 4 * heads * rows * block * HD * max_blocks
    return pl.pallas_call(
        functools.partial(flash_kernel, final),
        grid_spec=grid_spec,
        out_shape=out_shape,
        compiler_params=pltpu.CompilerParams(dimension_semantics=("arbitrary",)),
        cost_estimate=pl.CostEstimate(
            flops=flops,
            transcendentals=heads * rows * block * max_blocks,
            bytes_accessed=2 * block * HD * 2 * max_blocks + 2 * 2 * rows * heads * HD,
        ),
    )(*operands)


def local(hidden_rows, destination, doc_ids, norm_gain, w_query, w_key, w_value, w_out):
    owners = lax.axis_size(("chip", "core"))
    my_index = lax.axis_index(("chip", "core"))
    tok_dev, columns = hidden_rows.shape
    capacity = 2 * tok_dev // owners
    target = destination // tok_dev
    owner_ids = jnp.arange(owners, dtype=jnp.int32)
    one_hot = (target[:, None] == owner_ids[None, :]).astype(jnp.int32)
    slot_rank = jnp.sum((jnp.cumsum(one_hot, axis=0) - 1) * one_hot, axis=1)
    flat_slot = target * capacity + slot_rank
    outgoing = (
        jnp.zeros((owners * capacity, columns), hidden_rows.dtype).at[flat_slot].set(hidden_rows)
    )
    places = (
        jnp.full((owners * capacity,), tok_dev, jnp.int32).at[flat_slot].set(destination % tok_dev)
    )
    block_first = my_index * tok_dev
    first_id = doc_ids[0]
    last_id = doc_ids[tok_dev - 1]
    less_count = jnp.sum((doc_ids[None, :] < doc_ids[:, None]).astype(jnp.int32), axis=1)
    last_run_start = block_first + less_count[tok_dev - 1]
    info = jnp.broadcast_to(jnp.stack([last_id, last_run_start])[None, :], (owners, 2))
    places_info = jnp.concatenate([places.reshape(owners, capacity), info], axis=1)
    arrived = lax.all_to_all(
        outgoing.reshape(owners, capacity, columns), ("chip", "core"), split_axis=0, concat_axis=0, tiled=True
    )
    arrived_info = lax.all_to_all(places_info, ("chip", "core"), split_axis=0, concat_axis=0, tiled=True)
    arrived_rows = arrived_info[:, :capacity].reshape(-1)
    peer_last_id = arrived_info[:, capacity]
    peer_run_start = arrived_info[:, capacity + 1]
    earlier = (owner_ids < my_index) & (peer_last_id == first_id)
    doc_low = jnp.minimum(block_first, jnp.min(jnp.where(earlier, peer_run_start, block_first)))
    row_index = block_first + jnp.arange(tok_dev, dtype=jnp.int32)
    row_start = jnp.where(doc_ids == first_id, doc_low, block_first + less_count)

    routed_part = (
        jnp.zeros((tok_dev, columns), hidden_rows.dtype)
        .at[arrived_rows]
        .set(arrived.reshape(-1, columns), mode="drop")
    )
    routed = lax.all_gather(routed_part, "mp", axis=1, tiled=True)
    normed = normalize(routed, norm_gain)
    heads_dev = w_query.shape[1] // HD
    kv_dev = w_key.shape[1] // HD
    angles = rope_angles(row_index)
    queries = jnp.dot(normed, w_query, preferred_element_type=jnp.float32).reshape(
        tok_dev, heads_dev, HD
    )
    queries = rotate(queries, angles).astype(jnp.bfloat16).reshape(tok_dev, heads_dev * HD)
    keys_own = jnp.dot(normed, w_key, preferred_element_type=jnp.float32).reshape(
        tok_dev, kv_dev, HD
    )
    keys_own = rotate(keys_own, angles).astype(jnp.bfloat16).reshape(tok_dev, kv_dev * HD)
    values_own = jnp.dot(normed, w_value, preferred_element_type=jnp.float32).astype(jnp.bfloat16)
    kv_own = jnp.concatenate([keys_own, values_own], axis=1)
    half = tok_dev // 2
    kv_low = lax.all_gather(kv_own[:half], ("chip", "core"), axis=0, tiled=True)
    kv_high = lax.all_gather(kv_own[half:], ("chip", "core"), axis=0, tiled=True)

    block = KEY_BLOCK
    last_block = (block_first + tok_dev - 1) // block
    first_block = doc_low // block
    max_blocks = min((tok_dev - 1) // block + -(-(DOC_MAX - 1) // block) + 1, owners * tok_dev // block)
    max_start = jnp.max(row_start)

    def span_for(offset):
        return jnp.stack(
            [first_block, last_block - first_block + 1, max_start, block_first, block, offset]
        ).astype(jnp.int32)

    queries_t = jnp.transpose(queries.reshape(tok_dev, heads_dev, HD), (1, 2, 0))
    state = flash_pass(
        span_for(0), queries_t, kv_low, row_start[None, :], row_index[None, :], half, max_blocks, None
    )
    context_t = flash_pass(
        span_for(half), queries_t, kv_high, row_start[None, :], row_index[None, :], half, max_blocks,
        state,
    )
    context = jnp.transpose(context_t, (2, 0, 1)).reshape(tok_dev, heads_dev * HD)
    context_all = lax.all_gather(context, "mp", axis=1, tiled=True)
    mp_size = lax.axis_size("mp")
    w_split = jnp.transpose(w_out.reshape(w_out.shape[0], mp_size, -1), (1, 0, 2))
    w_cols = lax.all_to_all(w_split, "mp", split_axis=0, concat_axis=0, tiled=True)
    summed = jnp.einsum(
        "tsr,src->tc",
        context_all.reshape(tok_dev, mp_size, -1),
        w_cols,
        preferred_element_type=jnp.float32,
    )
    attended = (routed_part.astype(jnp.float32) + summed).astype(jnp.bfloat16)
    backward = attended[jnp.minimum(arrived_rows, tok_dev - 1)].reshape(owners, capacity, columns)
    returned = lax.all_to_all(backward, ("chip", "core"), split_axis=0, concat_axis=0, tiled=True)
    return returned.reshape(owners * capacity, columns)[flat_slot]


def solution(mesh):
    dp_size, mp_size = mesh.devices.shape
    split_mesh = jax.sharding.Mesh(
        mesh.devices.reshape(dp_size // 2, 2, mp_size), ("chip", "core", "mp")
    )
    rows = ("chip", "core")
    in_specs = (
        P(rows, "mp"),
        P(rows),
        P(rows),
        P(),
        P(None, "mp"),
        P(None, "mp"),
        P(None, "mp"),
        P("mp", None),
    )
    out_specs = P(rows, "mp")
    return jax.shard_map(
        local, mesh=split_mesh, in_specs=in_specs, out_specs=out_specs, check_vma=False
    )
```

```python
import functools
import math

import jax
import jax.numpy as jnp
from jax import lax
from jax.experimental import pallas as pl
from jax.experimental.pallas import tpu as pltpu
from jax.sharding import PartitionSpec as P

HD = 128
DOC_MAX = 8704

ROPE_BASE = 500000.0
NORM_EPS = 1e-05
NEG_START = -1e30
KEY_BLOCK = 512


def rope_angles(row_index):
    lane_index = jnp.arange(HD // 2, dtype=jnp.float32)
    frequency = jnp.power(jnp.float32(ROPE_BASE), -2.0 * lane_index / HD)
    return row_index.astype(jnp.float32)[:, None] * frequency[None, :]


def rotate(head_values, angles):
    half_width = head_values.shape[-1] // 2
    first_half = head_values[..., :half_width]
    second_half = head_values[..., half_width:]
    cosine = jnp.cos(angles)[:, None, :]
    sine_part = jnp.sin(angles)[:, None, :]
    return jnp.concatenate(
        [
            first_half * cosine - second_half * sine_part,
            second_half * cosine + first_half * sine_part,
        ],
        axis=-1,
    )


def normalize(routed, norm_gain):
    wide_rows = routed.astype(jnp.float32)
    inv_rms = lax.rsqrt(jnp.mean(wide_rows * wide_rows, axis=1, keepdims=True) + NORM_EPS)
    return (wide_rows * inv_rms * norm_gain[None, :]).astype(jnp.bfloat16)


def flash_kernel(carried, final, span_ref, *refs):
    if carried and final:
        q_ref, k_ref, v_ref, start_ref, row_ref, m_in, l_in, acc_in, o_ref, m_sc, l_sc, acc_sc = refs
    elif carried:
        q_ref, k_ref, v_ref, start_ref, row_ref, m_in, l_in, acc_in, m_sc, l_sc, acc_sc = refs
    else:
        q_ref, k_ref, v_ref, start_ref, row_ref, m_sc, l_sc, acc_sc = refs
    step = pl.program_id(0)
    heads = m_sc.shape[0]
    block = k_ref.shape[0]
    scale = HD ** (-0.5)

    @pl.when(step == 0)
    def _init():
        if carried:
            m_sc[...] = m_in[...]
            l_sc[...] = l_in[...]
            acc_sc[...] = acc_in[...]
        else:
            m_sc[...] = jnp.full(m_sc.shape, NEG_START, jnp.float32)
            l_sc[...] = jnp.zeros(l_sc.shape, jnp.float32)
            acc_sc[...] = jnp.zeros(acc_sc.shape, jnp.float32)

    key_first = (span_ref[0] + step) * span_ref[4] + span_ref[5]
    active = step < span_ref[1]
    whole = (key_first >= span_ref[2]) & (key_first + block - 1 <= span_ref[3])

    def accumulate(masked):
        keys = k_ref[...]
        values = v_ref[...]
        if masked:
            key_rows = key_first + lax.broadcasted_iota(jnp.int32, (block, 1), 0)
            allowed = (key_rows >= start_ref[...]) & (key_rows <= row_ref[...])
        for h in range(heads):
            scores = jnp.dot(keys, q_ref[h], preferred_element_type=jnp.float32) * scale
            if masked:
                scores = jnp.where(allowed, scores, -jnp.inf)
            m_old = m_sc[h]
            m_new = jnp.maximum(m_old, jnp.max(scores, axis=0, keepdims=True))
            rescale = jnp.exp(m_old - m_new)
            exp_scores = jnp.exp(scores - m_new)
            l_sc[h] = l_sc[h] * rescale + jnp.sum(exp_scores, axis=0, keepdims=True)
            acc_sc[h] = acc_sc[h] * rescale + lax.dot_general(
                values, exp_scores.astype(jnp.bfloat16), (((0,), (0,)), ((), ())),
                preferred_element_type=jnp.float32,
            )
            m_sc[h] = m_new

    @pl.when(active & whole)
    def _whole():
        accumulate(False)

    @pl.when(active & jnp.logical_not(whole))
    def _masked():
        accumulate(True)

    if final:
        @pl.when(step == pl.num_programs(0) - 1)
        def _finish():
            for h in range(heads):
                o_ref[h] = (acc_sc[h] / l_sc[h]).astype(o_ref.dtype)


def flash_pass(span, queries_t, kv_part, row_start, row_index, block, max_blocks, state, final):
    heads, _, rows = queries_t.shape
    carried = state is not None

    def kv_map(column):
        def index_map(step, span_ref):
            return (span_ref[0] + jnp.minimum(step, span_ref[1] - 1), column)
        return index_map

    fixed2 = lambda step, span_ref: (0, 0)
    fixed3 = lambda step, span_ref: (0, 0, 0)
    in_specs = [
        pl.BlockSpec((heads, HD, rows), fixed3),
        pl.BlockSpec((block, HD), kv_map(0)),
        pl.BlockSpec((block, HD), kv_map(1)),
        pl.BlockSpec((1, rows), fixed2),
        pl.BlockSpec((1, rows), fixed2),
    ]
    state_shapes = [
        jax.ShapeDtypeStruct((heads, 1, rows), jnp.float32),
        jax.ShapeDtypeStruct((heads, 1, rows), jnp.float32),
        jax.ShapeDtypeStruct((heads, HD, rows), jnp.float32),
    ]
    state_specs = [pl.BlockSpec(x.shape, fixed3) for x in state_shapes]
    operands = (span, queries_t, kv_part, kv_part, row_start, row_index)
    if carried:
        in_specs = in_specs + state_specs
        operands = operands + tuple(state)
    if final:
        out_specs = pl.BlockSpec((heads, HD, rows), fixed3)
        out_shape = jax.ShapeDtypeStruct((heads, HD, rows), jnp.bfloat16)
        scratch = [pltpu.VMEM(x.shape, jnp.float32) for x in state_shapes]
    else:
        out_specs = state_specs
        out_shape = state_shapes
        scratch = []
    grid_spec = pltpu.PrefetchScalarGridSpec(
        num_scalar_prefetch=1,
        grid=(max_blocks,),
        in_specs=in_specs,
        out_specs=out_specs,
        scratch_shapes=scratch,
    )
    flops = 4 * heads * rows * block * HD * max_blocks
    return pl.pallas_call(
        functools.partial(flash_kernel, carried, final),
        grid_spec=grid_spec,
        out_shape=out_shape,
        compiler_params=pltpu.CompilerParams(dimension_semantics=("arbitrary",)),
        cost_estimate=pl.CostEstimate(
            flops=flops,
            transcendentals=heads * rows * block * max_blocks,
            bytes_accessed=2 * block * HD * 2 * max_blocks + 2 * 2 * rows * heads * HD,
        ),
    )(*operands)


def local(hidden_rows, destination, doc_ids, norm_gain, w_query, w_key, w_value, w_out):
    owners = lax.axis_size(("chip", "core"))
    my_index = lax.axis_index(("chip", "core"))
    tok_dev, columns = hidden_rows.shape
    capacity = 2 * tok_dev // owners
    target = destination // tok_dev
    owner_ids = jnp.arange(owners, dtype=jnp.int32)
    one_hot = (target[:, None] == owner_ids[None, :]).astype(jnp.int32)
    slot_rank = jnp.sum((jnp.cumsum(one_hot, axis=0) - 1) * one_hot, axis=1)
    flat_slot = target * capacity + slot_rank
    outgoing = (
        jnp.zeros((owners * capacity, columns), hidden_rows.dtype).at[flat_slot].set(hidden_rows)
    )
    places = (
        jnp.full((owners * capacity,), tok_dev, jnp.int32).at[flat_slot].set(destination % tok_dev)
    )
    block_first = my_index * tok_dev
    first_id = doc_ids[0]
    last_id = doc_ids[tok_dev - 1]
    less_count = jnp.sum((doc_ids[None, :] < doc_ids[:, None]).astype(jnp.int32), axis=1)
    last_run_start = block_first + less_count[tok_dev - 1]
    info = jnp.broadcast_to(jnp.stack([last_id, last_run_start])[None, :], (owners, 2))
    places_info = jnp.concatenate([places.reshape(owners, capacity), info], axis=1)
    arrived = lax.all_to_all(
        outgoing.reshape(owners, capacity, columns), ("chip", "core"), split_axis=0, concat_axis=0, tiled=True
    )
    arrived_info = lax.all_to_all(places_info, ("chip", "core"), split_axis=0, concat_axis=0, tiled=True)
    arrived_rows = arrived_info[:, :capacity].reshape(-1)
    peer_last_id = arrived_info[:, capacity]
    peer_run_start = arrived_info[:, capacity + 1]
    earlier = (owner_ids < my_index) & (peer_last_id == first_id)
    doc_low = jnp.minimum(block_first, jnp.min(jnp.where(earlier, peer_run_start, block_first)))
    row_index = block_first + jnp.arange(tok_dev, dtype=jnp.int32)
    row_start = jnp.where(doc_ids == first_id, doc_low, block_first + less_count)

    routed_part = (
        jnp.zeros((tok_dev, columns), hidden_rows.dtype)
        .at[arrived_rows]
        .set(arrived.reshape(-1, columns), mode="drop")
    )
    routed = lax.all_gather(routed_part, "mp", axis=1, tiled=True)
    normed = normalize(routed, norm_gain)
    heads_dev = w_query.shape[1] // HD
    kv_dev = w_key.shape[1] // HD
    angles = rope_angles(row_index)
    queries = jnp.dot(normed, w_query, preferred_element_type=jnp.float32).reshape(
        tok_dev, heads_dev, HD
    )
    queries = rotate(queries, angles).astype(jnp.bfloat16).reshape(tok_dev, heads_dev * HD)
    keys_own = jnp.dot(normed, w_key, preferred_element_type=jnp.float32).reshape(
        tok_dev, kv_dev, HD
    )
    keys_own = rotate(keys_own, angles).astype(jnp.bfloat16).reshape(tok_dev, kv_dev * HD)
    values_own = jnp.dot(normed, w_value, preferred_element_type=jnp.float32).astype(jnp.bfloat16)
    kv_own = jnp.concatenate([keys_own, values_own], axis=1)
    parts = [(0, tok_dev // 2), (tok_dev // 2, tok_dev // 4), (3 * tok_dev // 4, tok_dev // 4)]
    kv_parts = [
        lax.all_gather(kv_own[first:first + size], ("chip", "core"), axis=0, tiled=True)
        for first, size in parts
    ]
    block = KEY_BLOCK
    last_block = (block_first + tok_dev - 1) // block
    first_block = doc_low // block
    max_blocks = min((tok_dev - 1) // block + -(-(DOC_MAX - 1) // block) + 1, owners * tok_dev // block)
    max_start = jnp.max(row_start)

    def span_for(offset):
        return jnp.stack(
            [first_block, last_block - first_block + 1, max_start, block_first, block, offset]
        ).astype(jnp.int32)

    queries_t = jnp.transpose(queries.reshape(tok_dev, heads_dev, HD), (1, 2, 0))
    state = None
    for number, ((first, size), kv_part) in enumerate(zip(parts, kv_parts)):
        state = flash_pass(
            span_for(first), queries_t, kv_part, row_start[None, :], row_index[None, :], size,
            max_blocks, state, number == len(parts) - 1,
        )
    context_t = state
    context = jnp.transpose(context_t, (2, 0, 1)).reshape(tok_dev, heads_dev * HD)
    context_all = lax.all_gather(context, "mp", axis=1, tiled=True)
    mp_size = lax.axis_size("mp")
    w_split = jnp.transpose(w_out.reshape(w_out.shape[0], mp_size, -1), (1, 0, 2))
    w_cols = lax.all_to_all(w_split, "mp", split_axis=0, concat_axis=0, tiled=True)
    summed = jnp.einsum(
        "tsr,src->tc",
        context_all.reshape(tok_dev, mp_size, -1),
        w_cols,
        preferred_element_type=jnp.float32,
    )
    attended = (routed_part.astype(jnp.float32) + summed).astype(jnp.bfloat16)
    backward = attended[jnp.minimum(arrived_rows, tok_dev - 1)].reshape(owners, capacity, columns)
    returned = lax.all_to_all(backward, ("chip", "core"), split_axis=0, concat_axis=0, tiled=True)
    return returned.reshape(owners * capacity, columns)[flat_slot]


def solution(mesh):
    dp_size, mp_size = mesh.devices.shape
    split_mesh = jax.sharding.Mesh(
        mesh.devices.reshape(dp_size // 2, 2, mp_size), ("chip", "core", "mp")
    )
    rows = ("chip", "core")
    in_specs = (
        P(rows, "mp"),
        P(rows),
        P(rows),
        P(),
        P(None, "mp"),
        P(None, "mp"),
        P(None, "mp"),
        P("mp", None),
    )
    out_specs = P(rows, "mp")
    return jax.shard_map(
        local, mesh=split_mesh, in_specs=in_specs, out_specs=out_specs, check_vma=False
    )
```

```python
import functools
import math

import jax
import jax.numpy as jnp
from jax import lax
from jax.experimental import pallas as pl
from jax.experimental.pallas import tpu as pltpu
from jax.sharding import PartitionSpec as P

HD = 128
DOC_MAX = 8704

ROPE_BASE = 500000.0
NORM_EPS = 1e-05
NEG_START = -1e30
KEY_BLOCK = 512


def rope_angles(row_index):
    lane_index = jnp.arange(HD // 2, dtype=jnp.float32)
    frequency = jnp.power(jnp.float32(ROPE_BASE), -2.0 * lane_index / HD)
    return row_index.astype(jnp.float32)[:, None] * frequency[None, :]


def rotate(head_values, angles):
    half_width = head_values.shape[-1] // 2
    first_half = head_values[..., :half_width]
    second_half = head_values[..., half_width:]
    cosine = jnp.cos(angles)[:, None, :]
    sine_part = jnp.sin(angles)[:, None, :]
    return jnp.concatenate(
        [
            first_half * cosine - second_half * sine_part,
            second_half * cosine + first_half * sine_part,
        ],
        axis=-1,
    )


def normalize(routed, norm_gain):
    wide_rows = routed.astype(jnp.float32)
    inv_rms = lax.rsqrt(jnp.mean(wide_rows * wide_rows, axis=1, keepdims=True) + NORM_EPS)
    return (wide_rows * inv_rms * norm_gain[None, :]).astype(jnp.bfloat16)


def flash_kernel(final, span_ref, *refs):
    if final:
        q_ref, k_ref, v_ref, start_ref, row_ref, m_in, l_in, acc_in, o_ref, m_sc, l_sc, acc_sc = refs
    else:
        q_ref, k_ref, v_ref, start_ref, row_ref, m_sc, l_sc, acc_sc = refs
    step = pl.program_id(0)
    heads = m_sc.shape[0]
    block = k_ref.shape[0]
    scale = HD ** (-0.5)

    @pl.when(step == 0)
    def _init():
        if final:
            m_sc[...] = m_in[...]
            l_sc[...] = l_in[...]
            acc_sc[...] = acc_in[...]
        else:
            m_sc[...] = jnp.full(m_sc.shape, NEG_START, jnp.float32)
            l_sc[...] = jnp.zeros(l_sc.shape, jnp.float32)
            acc_sc[...] = jnp.zeros(acc_sc.shape, jnp.float32)

    key_first = (span_ref[0] + step) * span_ref[4] + span_ref[5]
    active = step < span_ref[1]
    whole = (key_first >= span_ref[2]) & (key_first + block - 1 <= span_ref[3])

    def accumulate(masked):
        keys = k_ref[...]
        values = v_ref[...]
        if masked:
            key_rows = key_first + lax.broadcasted_iota(jnp.int32, (block, 1), 0)
            allowed = (key_rows >= start_ref[...]) & (key_rows <= row_ref[...])
        for h in range(heads):
            scores = jnp.dot(keys, q_ref[h], preferred_element_type=jnp.float32) * scale
            if masked:
                scores = jnp.where(allowed, scores, -jnp.inf)
            m_old = m_sc[h]
            m_new = jnp.maximum(m_old, jnp.max(scores, axis=0, keepdims=True))
            rescale = jnp.exp(m_old - m_new)
            exp_scores = jnp.exp(scores - m_new)
            l_sc[h] = l_sc[h] * rescale + jnp.sum(exp_scores, axis=0, keepdims=True)
            acc_sc[h] = acc_sc[h] * rescale + lax.dot_general(
                values, exp_scores.astype(jnp.bfloat16), (((0,), (0,)), ((), ())),
                preferred_element_type=jnp.float32,
            )
            m_sc[h] = m_new

    @pl.when(active & whole)
    def _whole():
        accumulate(False)

    @pl.when(active & jnp.logical_not(whole))
    def _masked():
        accumulate(True)

    if final:
        @pl.when(step == pl.num_programs(0) - 1)
        def _finish():
            for h in range(heads):
                o_ref[h] = (acc_sc[h] / l_sc[h]).astype(o_ref.dtype)


def flash_pass(span, queries_t, kv_part, row_start, row_index, block, max_blocks, state):
    heads, _, rows = queries_t.shape
    final = state is not None

    def kv_map(column):
        def index_map(step, span_ref):
            return (span_ref[0] + jnp.minimum(step, span_ref[1] - 1), column)
        return index_map

    fixed2 = lambda step, span_ref: (0, 0)
    fixed3 = lambda step, span_ref: (0, 0, 0)
    in_specs = [
        pl.BlockSpec((heads, HD, rows), fixed3),
        pl.BlockSpec((block, HD), kv_map(0)),
        pl.BlockSpec((block, HD), kv_map(1)),
        pl.BlockSpec((1, rows), fixed2),
        pl.BlockSpec((1, rows), fixed2),
    ]
    state_shapes = [
        jax.ShapeDtypeStruct((heads, 1, rows), jnp.float32),
        jax.ShapeDtypeStruct((heads, 1, rows), jnp.float32),
        jax.ShapeDtypeStruct((heads, HD, rows), jnp.float32),
    ]
    state_specs = [pl.BlockSpec(x.shape, fixed3) for x in state_shapes]
    if final:
        in_specs = in_specs + state_specs
        out_specs = pl.BlockSpec((heads, HD, rows), fixed3)
        out_shape = jax.ShapeDtypeStruct((heads, HD, rows), jnp.bfloat16)
        scratch = [pltpu.VMEM(x.shape, jnp.float32) for x in state_shapes]
        operands = (span, queries_t, kv_part, kv_part, row_start, row_index) + tuple(state)
    else:
        out_specs = state_specs
        out_shape = state_shapes
        scratch = []
        operands = (span, queries_t, kv_part, kv_part, row_start, row_index)
    grid_spec = pltpu.PrefetchScalarGridSpec(
        num_scalar_prefetch=1,
        grid=(max_blocks,),
        in_specs=in_specs,
        out_specs=out_specs,
        scratch_shapes=scratch,
    )
    flops = 4 * heads * rows * block * HD * max_blocks
    return pl.pallas_call(
        functools.partial(flash_kernel, final),
        grid_spec=grid_spec,
        out_shape=out_shape,
        compiler_params=pltpu.CompilerParams(dimension_semantics=("arbitrary",)),
        cost_estimate=pl.CostEstimate(
            flops=flops,
            transcendentals=heads * rows * block * max_blocks,
            bytes_accessed=2 * block * HD * 2 * max_blocks + 2 * 2 * rows * heads * HD,
        ),
    )(*operands)


def local(hidden_rows, destination, doc_ids, norm_gain, w_query, w_key, w_value, w_out):
    owners = lax.axis_size(("chip", "core"))
    my_index = lax.axis_index(("chip", "core"))
    tok_dev, columns = hidden_rows.shape
    capacity = 2 * tok_dev // owners
    target = destination // tok_dev
    owner_ids = jnp.arange(owners, dtype=jnp.int32)
    one_hot = (target[:, None] == owner_ids[None, :]).astype(jnp.int32)
    slot_rank = jnp.sum((jnp.cumsum(one_hot, axis=0) - 1) * one_hot, axis=1)
    flat_slot = target * capacity + slot_rank
    outgoing = (
        jnp.zeros((owners * capacity, columns), hidden_rows.dtype).at[flat_slot].set(hidden_rows)
    )
    places = (
        jnp.full((owners * capacity,), tok_dev, jnp.int32).at[flat_slot].set(destination % tok_dev)
    )
    block_first = my_index * tok_dev
    first_id = doc_ids[0]
    last_id = doc_ids[tok_dev - 1]
    less_count = jnp.sum((doc_ids[None, :] < doc_ids[:, None]).astype(jnp.int32), axis=1)
    last_run_start = block_first + less_count[tok_dev - 1]
    digit = 64
    slot_count = owners * capacity
    meta = jnp.stack(
        [
            places // digit,
            places % digit,
            jnp.broadcast_to(last_id, (slot_count,)),
            jnp.broadcast_to(last_run_start // digit, (slot_count,)),
            jnp.broadcast_to(last_run_start % digit, (slot_count,)),
        ],
        axis=1,
    )
    meta_width = 128
    meta = jnp.pad(meta, ((0, 0), (0, meta_width - meta.shape[1]))).astype(hidden_rows.dtype)
    wide = jnp.concatenate([outgoing, meta], axis=1)
    arrived_wide = lax.all_to_all(
        wide.reshape(owners, capacity, columns + meta_width), ("chip", "core"),
        split_axis=0, concat_axis=0, tiled=True,
    )
    arrived = arrived_wide[:, :, :columns]
    arrived_meta = arrived_wide[:, :, columns:columns + 5].astype(jnp.int32)
    arrived_rows = (arrived_meta[:, :, 0] * digit + arrived_meta[:, :, 1]).reshape(-1)
    peer_last_id = arrived_meta[:, 0, 2]
    peer_run_start = arrived_meta[:, 0, 3] * digit + arrived_meta[:, 0, 4]
    earlier = (owner_ids < my_index) & (peer_last_id == first_id)
    doc_low = jnp.minimum(block_first, jnp.min(jnp.where(earlier, peer_run_start, block_first)))
    row_index = block_first + jnp.arange(tok_dev, dtype=jnp.int32)
    row_start = jnp.where(doc_ids == first_id, doc_low, block_first + less_count)

    routed_part = (
        jnp.zeros((tok_dev, columns), hidden_rows.dtype)
        .at[arrived_rows]
        .set(arrived.reshape(-1, columns), mode="drop")
    )
    routed = lax.all_gather(routed_part, "mp", axis=1, tiled=True)
    normed = normalize(routed, norm_gain)
    heads_dev = w_query.shape[1] // HD
    kv_dev = w_key.shape[1] // HD
    angles = rope_angles(row_index)
    queries = jnp.dot(normed, w_query, preferred_element_type=jnp.float32).reshape(
        tok_dev, heads_dev, HD
    )
    queries = rotate(queries, angles).astype(jnp.bfloat16).reshape(tok_dev, heads_dev * HD)
    keys_own = jnp.dot(normed, w_key, preferred_element_type=jnp.float32).reshape(
        tok_dev, kv_dev, HD
    )
    keys_own = rotate(keys_own, angles).astype(jnp.bfloat16).reshape(tok_dev, kv_dev * HD)
    values_own = jnp.dot(normed, w_value, preferred_element_type=jnp.float32).astype(jnp.bfloat16)
    kv_own = jnp.concatenate([keys_own, values_own], axis=1)
    half = tok_dev // 2
    kv_low = lax.all_gather(kv_own[:half], ("chip", "core"), axis=0, tiled=True)
    kv_high = lax.all_gather(kv_own[half:], ("chip", "core"), axis=0, tiled=True)

    block = KEY_BLOCK
    last_block = (block_first + tok_dev - 1) // block
    first_block = doc_low // block
    max_blocks = min((tok_dev - 1) // block + -(-(DOC_MAX - 1) // block) + 1, owners * tok_dev // block)
    max_start = jnp.max(row_start)

    def span_for(offset):
        return jnp.stack(
            [first_block, last_block - first_block + 1, max_start, block_first, block, offset]
        ).astype(jnp.int32)

    queries_t = jnp.transpose(queries.reshape(tok_dev, heads_dev, HD), (1, 2, 0))
    state = flash_pass(
        span_for(0), queries_t, kv_low, row_start[None, :], row_index[None, :], half, max_blocks, None
    )
    context_t = flash_pass(
        span_for(half), queries_t, kv_high, row_start[None, :], row_index[None, :], half, max_blocks,
        state,
    )
    context = jnp.transpose(context_t, (2, 0, 1)).reshape(tok_dev, heads_dev * HD)
    context_all = lax.all_gather(context, "mp", axis=1, tiled=True)
    mp_size = lax.axis_size("mp")
    w_split = jnp.transpose(w_out.reshape(w_out.shape[0], mp_size, -1), (1, 0, 2))
    w_cols = lax.all_to_all(w_split, "mp", split_axis=0, concat_axis=0, tiled=True)
    summed = jnp.einsum(
        "tsr,src->tc",
        context_all.reshape(tok_dev, mp_size, -1),
        w_cols,
        preferred_element_type=jnp.float32,
    )
    attended = (routed_part.astype(jnp.float32) + summed).astype(jnp.bfloat16)
    backward = attended[jnp.minimum(arrived_rows, tok_dev - 1)].reshape(owners, capacity, columns)
    returned = lax.all_to_all(backward, ("chip", "core"), split_axis=0, concat_axis=0, tiled=True)
    return returned.reshape(owners * capacity, columns)[flat_slot]


def solution(mesh):
    dp_size, mp_size = mesh.devices.shape
    split_mesh = jax.sharding.Mesh(
        mesh.devices.reshape(dp_size // 2, 2, mp_size), ("chip", "core", "mp")
    )
    rows = ("chip", "core")
    in_specs = (
        P(rows, "mp"),
        P(rows),
        P(rows),
        P(),
        P(None, "mp"),
        P(None, "mp"),
        P(None, "mp"),
        P("mp", None),
    )
    out_specs = P(rows, "mp")
    return jax.shard_map(
        local, mesh=split_mesh, in_specs=in_specs, out_specs=out_specs, check_vma=False
    )
```

```python
import functools
import math

import jax
import jax.numpy as jnp
from jax import lax
from jax.experimental import pallas as pl
from jax.experimental.pallas import tpu as pltpu
from jax.sharding import PartitionSpec as P

HD = 128
DOC_MAX = 8704

ROPE_BASE = 500000.0
NORM_EPS = 1e-05
NEG_START = -1e30
KEY_BLOCK = 512


def rope_angles(row_index):
    lane_index = jnp.arange(HD // 2, dtype=jnp.float32)
    frequency = jnp.power(jnp.float32(ROPE_BASE), -2.0 * lane_index / HD)
    return row_index.astype(jnp.float32)[:, None] * frequency[None, :]


def rotate(head_values, angles):
    half_width = head_values.shape[-1] // 2
    first_half = head_values[..., :half_width]
    second_half = head_values[..., half_width:]
    cosine = jnp.cos(angles)[:, None, :]
    sine_part = jnp.sin(angles)[:, None, :]
    return jnp.concatenate(
        [
            first_half * cosine - second_half * sine_part,
            second_half * cosine + first_half * sine_part,
        ],
        axis=-1,
    )


def normalize(routed, norm_gain):
    wide_rows = routed.astype(jnp.float32)
    inv_rms = lax.rsqrt(jnp.mean(wide_rows * wide_rows, axis=1, keepdims=True) + NORM_EPS)
    return (wide_rows * inv_rms * norm_gain[None, :]).astype(jnp.bfloat16)


def flash_kernel(final, span_ref, *refs):
    if final:
        q_ref, k_ref, v_ref, start_ref, row_ref, m_in, l_in, acc_in, o_ref, m_sc, l_sc, acc_sc = refs
    else:
        q_ref, k_ref, v_ref, start_ref, row_ref, m_sc, l_sc, acc_sc = refs
    step = pl.program_id(0)
    heads = m_sc.shape[0]
    block = k_ref.shape[0]
    scale = HD ** (-0.5)

    @pl.when(step == 0)
    def _init():
        if final:
            m_sc[...] = m_in[...]
            l_sc[...] = l_in[...]
            acc_sc[...] = acc_in[...]
        else:
            m_sc[...] = jnp.full(m_sc.shape, NEG_START, jnp.float32)
            l_sc[...] = jnp.zeros(l_sc.shape, jnp.float32)
            acc_sc[...] = jnp.zeros(acc_sc.shape, jnp.float32)

    key_first = (span_ref[0] + step) * span_ref[4] + span_ref[5]
    active = step < span_ref[1]
    whole = (key_first >= span_ref[2]) & (key_first + block - 1 <= span_ref[3])

    def accumulate(masked):
        keys = k_ref[...]
        values = v_ref[...]
        if masked:
            key_rows = key_first + lax.broadcasted_iota(jnp.int32, (block, 1), 0)
            allowed = (key_rows >= start_ref[...]) & (key_rows <= row_ref[...])
        for h in range(heads):
            scores = jnp.dot(keys, q_ref[h], preferred_element_type=jnp.float32) * scale
            if masked:
                scores = jnp.where(allowed, scores, -jnp.inf)
            m_old = m_sc[h]
            m_new = jnp.maximum(m_old, jnp.max(scores, axis=0, keepdims=True))
            rescale = jnp.exp(m_old - m_new)
            exp_scores = jnp.exp(scores - m_new)
            l_sc[h] = l_sc[h] * rescale + jnp.sum(exp_scores, axis=0, keepdims=True)
            acc_sc[h] = acc_sc[h] * rescale + lax.dot_general(
                values, exp_scores.astype(jnp.bfloat16), (((0,), (0,)), ((), ())),
                preferred_element_type=jnp.float32,
            )
            m_sc[h] = m_new

    @pl.when(active & whole)
    def _whole():
        accumulate(False)

    @pl.when(active & jnp.logical_not(whole))
    def _masked():
        accumulate(True)

    if final:
        @pl.when(step == pl.num_programs(0) - 1)
        def _finish():
            for h in range(heads):
                o_ref[h] = (acc_sc[h] / l_sc[h]).astype(o_ref.dtype)


def flash_pass(span, queries_t, kv_part, row_start, row_index, block, max_blocks, state):
    heads, _, rows = queries_t.shape
    final = state is not None

    def kv_map(column):
        def index_map(step, span_ref):
            return (span_ref[0] + jnp.minimum(step, span_ref[1] - 1), column)
        return index_map

    fixed2 = lambda step, span_ref: (0, 0)
    fixed3 = lambda step, span_ref: (0, 0, 0)
    in_specs = [
        pl.BlockSpec((heads, HD, rows), fixed3),
        pl.BlockSpec((block, HD), kv_map(0)),
        pl.BlockSpec((block, HD), kv_map(1)),
        pl.BlockSpec((1, rows), fixed2),
        pl.BlockSpec((1, rows), fixed2),
    ]
    state_shapes = [
        jax.ShapeDtypeStruct((heads, 1, rows), jnp.float32),
        jax.ShapeDtypeStruct((heads, 1, rows), jnp.float32),
        jax.ShapeDtypeStruct((heads, HD, rows), jnp.float32),
    ]
    state_specs = [pl.BlockSpec(x.shape, fixed3) for x in state_shapes]
    if final:
        in_specs = in_specs + state_specs
        out_specs = pl.BlockSpec((heads, HD, rows), fixed3)
        out_shape = jax.ShapeDtypeStruct((heads, HD, rows), jnp.bfloat16)
        scratch = [pltpu.VMEM(x.shape, jnp.float32) for x in state_shapes]
        operands = (span, queries_t, kv_part, kv_part, row_start, row_index) + tuple(state)
    else:
        out_specs = state_specs
        out_shape = state_shapes
        scratch = []
        operands = (span, queries_t, kv_part, kv_part, row_start, row_index)
    grid_spec = pltpu.PrefetchScalarGridSpec(
        num_scalar_prefetch=1,
        grid=(max_blocks,),
        in_specs=in_specs,
        out_specs=out_specs,
        scratch_shapes=scratch,
    )
    flops = 4 * heads * rows * block * HD * max_blocks
    return pl.pallas_call(
        functools.partial(flash_kernel, final),
        grid_spec=grid_spec,
        out_shape=out_shape,
        compiler_params=pltpu.CompilerParams(dimension_semantics=("arbitrary",)),
        cost_estimate=pl.CostEstimate(
            flops=flops,
            transcendentals=heads * rows * block * max_blocks,
            bytes_accessed=2 * block * HD * 2 * max_blocks + 2 * 2 * rows * heads * HD,
        ),
    )(*operands)


def local(hidden_rows, destination, doc_ids, norm_gain, w_query, w_key, w_value, w_out):
    owners = lax.axis_size(("chip", "core"))
    my_index = lax.axis_index(("chip", "core"))
    tok_dev, columns = hidden_rows.shape
    capacity = 2 * tok_dev // owners
    target = destination // tok_dev
    owner_ids = jnp.arange(owners, dtype=jnp.int32)
    one_hot = (target[:, None] == owner_ids[None, :]).astype(jnp.int32)
    slot_rank = jnp.sum((jnp.cumsum(one_hot, axis=0) - 1) * one_hot, axis=1)
    flat_slot = target * capacity + slot_rank
    outgoing = (
        jnp.zeros((owners * capacity, columns), hidden_rows.dtype).at[flat_slot].set(hidden_rows)
    )
    places = (
        jnp.full((owners * capacity,), tok_dev, jnp.int32).at[flat_slot].set(destination % tok_dev)
    )
    block_first = my_index * tok_dev
    first_id = doc_ids[0]
    last_id = doc_ids[tok_dev - 1]
    less_count = jnp.sum((doc_ids[None, :] < doc_ids[:, None]).astype(jnp.int32), axis=1)
    last_run_start = block_first + less_count[tok_dev - 1]
    digit = 64
    slot_count = owners * capacity
    meta = jnp.stack(
        [
            places // digit,
            places % digit,
            jnp.broadcast_to(last_id, (slot_count,)),
            jnp.broadcast_to(last_run_start // digit, (slot_count,)),
            jnp.broadcast_to(last_run_start % digit, (slot_count,)),
        ],
        axis=1,
    )
    meta_width = 128
    meta = jnp.pad(meta, ((0, 0), (0, meta_width - meta.shape[1]))).astype(hidden_rows.dtype)
    wide = jnp.concatenate([outgoing, meta], axis=1)
    arrived_wide = lax.all_to_all(
        wide.reshape(owners, capacity, columns + meta_width), ("chip", "core"),
        split_axis=0, concat_axis=0, tiled=True,
    )
    arrived = arrived_wide[:, :, :columns]
    arrived_meta = arrived_wide[:, :, columns:columns + 5].astype(jnp.int32)
    arrived_rows = (arrived_meta[:, :, 0] * digit + arrived_meta[:, :, 1]).reshape(-1)
    peer_last_id = arrived_meta[:, 0, 2]
    peer_run_start = arrived_meta[:, 0, 3] * digit + arrived_meta[:, 0, 4]
    earlier = (owner_ids < my_index) & (peer_last_id == first_id)
    doc_low = jnp.minimum(block_first, jnp.min(jnp.where(earlier, peer_run_start, block_first)))
    row_index = block_first + jnp.arange(tok_dev, dtype=jnp.int32)
    row_start = jnp.where(doc_ids == first_id, doc_low, block_first + less_count)

    routed_part = (
        jnp.zeros((tok_dev, columns), hidden_rows.dtype)
        .at[arrived_rows]
        .set(arrived.reshape(-1, columns), mode="drop")
    )
    routed = lax.all_gather(routed_part, "mp", axis=1, tiled=True)
    normed = normalize(routed, norm_gain)
    heads_dev = w_query.shape[1] // HD
    kv_dev = w_key.shape[1] // HD
    angles = rope_angles(row_index)
    queries = jnp.dot(normed, w_query, preferred_element_type=jnp.float32).reshape(
        tok_dev, heads_dev, HD
    )
    queries = rotate(queries, angles).astype(jnp.bfloat16).reshape(tok_dev, heads_dev * HD)
    keys_own = jnp.dot(normed, w_key, preferred_element_type=jnp.float32).reshape(
        tok_dev, kv_dev, HD
    )
    keys_own = rotate(keys_own, angles).astype(jnp.bfloat16).reshape(tok_dev, kv_dev * HD)
    values_own = jnp.dot(normed, w_value, preferred_element_type=jnp.float32).astype(jnp.bfloat16)
    kv_own = jnp.concatenate([keys_own, values_own], axis=1)
    half = tok_dev // 2
    kv_low = lax.all_gather(kv_own[:half], ("chip", "core"), axis=0, tiled=True)
    kv_high = lax.all_gather(kv_own[half:], ("chip", "core"), axis=0, tiled=True)

    block = KEY_BLOCK
    last_block = (block_first + tok_dev - 1) // block
    first_block = doc_low // block
    max_blocks = min((tok_dev - 1) // block + -(-(DOC_MAX - 1) // block) + 1, owners * tok_dev // block)
    max_start = jnp.max(row_start)

    def span_for(offset):
        return jnp.stack(
            [first_block, last_block - first_block + 1, max_start, block_first, block, offset]
        ).astype(jnp.int32)

    queries_t = jnp.transpose(queries.reshape(tok_dev, heads_dev, HD), (1, 2, 0))
    state = flash_pass(
        span_for(0), queries_t, kv_low, row_start[None, :], row_index[None, :], half, max_blocks, None
    )
    head_groups = 2
    group = heads_dev // head_groups
    mp_size = lax.axis_size("mp")
    w_split = jnp.transpose(w_out.reshape(w_out.shape[0], mp_size, -1), (1, 0, 2))
    w_cols = lax.all_to_all(w_split, "mp", split_axis=0, concat_axis=0, tiled=True)
    w_groups = [
        w_cols.reshape(mp_size, head_groups, group * HD, w_cols.shape[2])[:, g]
        for g in range(head_groups)
    ]
    w_groups, state = lax.optimization_barrier((w_groups, state))
    summed = None
    for g in range(head_groups):
        heads_g = slice(g * group, (g + 1) * group)
        context_t = flash_pass(
            span_for(half), queries_t[heads_g], kv_high, row_start[None, :], row_index[None, :], half,
            max_blocks, tuple(x[heads_g] for x in state),
        )
        context = jnp.transpose(context_t, (2, 0, 1)).reshape(tok_dev, group * HD)
        context_all = lax.all_gather(context, "mp", axis=1, tiled=True)
        part = jnp.einsum(
            "tsr,src->tc",
            context_all.reshape(tok_dev, mp_size, -1),
            w_groups[g],
            preferred_element_type=jnp.float32,
        )
        summed = part if summed is None else summed + part
    attended = (routed_part.astype(jnp.float32) + summed).astype(jnp.bfloat16)
    backward = attended[jnp.minimum(arrived_rows, tok_dev - 1)].reshape(owners, capacity, columns)
    returned = lax.all_to_all(backward, ("chip", "core"), split_axis=0, concat_axis=0, tiled=True)
    return returned.reshape(owners * capacity, columns)[flat_slot]


def solution(mesh):
    dp_size, mp_size = mesh.devices.shape
    split_mesh = jax.sharding.Mesh(
        mesh.devices.reshape(dp_size // 2, 2, mp_size), ("chip", "core", "mp")
    )
    rows = ("chip", "core")
    in_specs = (
        P(rows, "mp"),
        P(rows),
        P(rows),
        P(),
        P(None, "mp"),
        P(None, "mp"),
        P(None, "mp"),
        P("mp", None),
    )
    out_specs = P(rows, "mp")
    return jax.shard_map(
        local, mesh=split_mesh, in_specs=in_specs, out_specs=out_specs, check_vma=False
    )
```

```python
import functools
import math

import jax
import jax.numpy as jnp
from jax import lax
from jax.experimental import pallas as pl
from jax.experimental.pallas import tpu as pltpu
from jax.sharding import PartitionSpec as P

HD = 128
DOC_MAX = 8704

ROPE_BASE = 500000.0
NORM_EPS = 1e-05
NEG_START = -1e30
KEY_BLOCK = 512


def rope_angles(row_index):
    lane_index = jnp.arange(HD // 2, dtype=jnp.float32)
    frequency = jnp.power(jnp.float32(ROPE_BASE), -2.0 * lane_index / HD)
    return row_index.astype(jnp.float32)[:, None] * frequency[None, :]


def rotate(head_values, angles):
    half_width = head_values.shape[-1] // 2
    first_half = head_values[..., :half_width]
    second_half = head_values[..., half_width:]
    cosine = jnp.cos(angles)[:, None, :]
    sine_part = jnp.sin(angles)[:, None, :]
    return jnp.concatenate(
        [
            first_half * cosine - second_half * sine_part,
            second_half * cosine + first_half * sine_part,
        ],
        axis=-1,
    )


def normalize(routed, norm_gain):
    wide_rows = routed.astype(jnp.float32)
    inv_rms = lax.rsqrt(jnp.mean(wide_rows * wide_rows, axis=1, keepdims=True) + NORM_EPS)
    return (wide_rows * inv_rms * norm_gain[None, :]).astype(jnp.bfloat16)


def flash_kernel(final, span_ref, *refs):
    if final:
        q_ref, k_ref, v_ref, start_ref, row_ref, m_in, l_in, acc_in, o_ref, m_sc, l_sc, acc_sc = refs
    else:
        q_ref, k_ref, v_ref, start_ref, row_ref, m_sc, l_sc, acc_sc = refs
    step = pl.program_id(0)
    heads = m_sc.shape[0]
    block = k_ref.shape[0]
    scale = HD ** (-0.5)

    @pl.when(step == 0)
    def _init():
        if final:
            m_sc[...] = m_in[...]
            l_sc[...] = l_in[...]
            acc_sc[...] = acc_in[...]
        else:
            m_sc[...] = jnp.full(m_sc.shape, NEG_START, jnp.float32)
            l_sc[...] = jnp.zeros(l_sc.shape, jnp.float32)
            acc_sc[...] = jnp.zeros(acc_sc.shape, jnp.float32)

    part = block // 2
    pair = span_ref[0] // 2 + step
    key_first = 2 * pair * span_ref[4] + span_ref[5]
    key_last = (2 * pair + 1) * span_ref[4] + span_ref[5] + part - 1
    active = step < span_ref[1]
    whole = (key_first >= span_ref[2]) & (key_last <= span_ref[3])

    def accumulate(masked):
        keys = k_ref[...]
        values = v_ref[...]
        if masked:
            sub = lax.broadcasted_iota(jnp.int32, (block, 1), 0)
            key_rows = key_first + (sub // part) * span_ref[4] + sub % part
            allowed = (key_rows >= start_ref[...]) & (key_rows <= row_ref[...])
        for h in range(heads):
            scores = jnp.dot(keys, q_ref[h], preferred_element_type=jnp.float32) * scale
            if masked:
                scores = jnp.where(allowed, scores, -jnp.inf)
            m_old = m_sc[h]
            m_new = jnp.maximum(m_old, jnp.max(scores, axis=0, keepdims=True))
            rescale = jnp.exp(m_old - m_new)
            exp_scores = jnp.exp(scores - m_new)
            l_sc[h] = l_sc[h] * rescale + jnp.sum(exp_scores, axis=0, keepdims=True)
            acc_sc[h] = acc_sc[h] * rescale + lax.dot_general(
                values, exp_scores.astype(jnp.bfloat16), (((0,), (0,)), ((), ())),
                preferred_element_type=jnp.float32,
            )
            m_sc[h] = m_new

    @pl.when(active & whole)
    def _whole():
        accumulate(False)

    @pl.when(active & jnp.logical_not(whole))
    def _masked():
        accumulate(True)

    if final:
        @pl.when(step == pl.num_programs(0) - 1)
        def _finish():
            for h in range(heads):
                o_ref[h] = (acc_sc[h] / l_sc[h]).astype(o_ref.dtype)


def flash_pass(span, queries_t, kv_part, row_start, row_index, block, max_blocks, state):
    heads, _, rows = queries_t.shape
    final = state is not None

    def kv_map(column):
        def index_map(step, span_ref):
            return (span_ref[0] // 2 + jnp.minimum(step, span_ref[1] - 1), column)
        return index_map

    fixed2 = lambda step, span_ref: (0, 0)
    fixed3 = lambda step, span_ref: (0, 0, 0)
    in_specs = [
        pl.BlockSpec((heads, HD, rows), fixed3),
        pl.BlockSpec((2 * block, HD), kv_map(0)),
        pl.BlockSpec((2 * block, HD), kv_map(1)),
        pl.BlockSpec((1, rows), fixed2),
        pl.BlockSpec((1, rows), fixed2),
    ]
    state_shapes = [
        jax.ShapeDtypeStruct((heads, 1, rows), jnp.float32),
        jax.ShapeDtypeStruct((heads, 1, rows), jnp.float32),
        jax.ShapeDtypeStruct((heads, HD, rows), jnp.float32),
    ]
    state_specs = [pl.BlockSpec(x.shape, fixed3) for x in state_shapes]
    if final:
        in_specs = in_specs + state_specs
        out_specs = pl.BlockSpec((heads, HD, rows), fixed3)
        out_shape = jax.ShapeDtypeStruct((heads, HD, rows), jnp.bfloat16)
        scratch = [pltpu.VMEM(x.shape, jnp.float32) for x in state_shapes]
        operands = (span, queries_t, kv_part, kv_part, row_start, row_index) + tuple(state)
    else:
        out_specs = state_specs
        out_shape = state_shapes
        scratch = []
        operands = (span, queries_t, kv_part, kv_part, row_start, row_index)
    grid_spec = pltpu.PrefetchScalarGridSpec(
        num_scalar_prefetch=1,
        grid=(max_blocks,),
        in_specs=in_specs,
        out_specs=out_specs,
        scratch_shapes=scratch,
    )
    flops = 8 * heads * rows * block * HD * max_blocks
    return pl.pallas_call(
        functools.partial(flash_kernel, final),
        grid_spec=grid_spec,
        out_shape=out_shape,
        compiler_params=pltpu.CompilerParams(dimension_semantics=("arbitrary",)),
        cost_estimate=pl.CostEstimate(
            flops=flops,
            transcendentals=2 * heads * rows * block * max_blocks,
            bytes_accessed=4 * block * HD * 2 * max_blocks + 2 * 2 * rows * heads * HD,
        ),
    )(*operands)


def local(hidden_rows, destination, doc_ids, norm_gain, w_query, w_key, w_value, w_out):
    owners = lax.axis_size(("chip", "core"))
    my_index = lax.axis_index(("chip", "core"))
    tok_dev, columns = hidden_rows.shape
    capacity = 2 * tok_dev // owners
    target = destination // tok_dev
    owner_ids = jnp.arange(owners, dtype=jnp.int32)
    one_hot = (target[:, None] == owner_ids[None, :]).astype(jnp.int32)
    slot_rank = jnp.sum((jnp.cumsum(one_hot, axis=0) - 1) * one_hot, axis=1)
    flat_slot = target * capacity + slot_rank
    outgoing = (
        jnp.zeros((owners * capacity, columns), hidden_rows.dtype).at[flat_slot].set(hidden_rows)
    )
    places = (
        jnp.full((owners * capacity,), tok_dev, jnp.int32).at[flat_slot].set(destination % tok_dev)
    )
    block_first = my_index * tok_dev
    first_id = doc_ids[0]
    last_id = doc_ids[tok_dev - 1]
    less_count = jnp.sum((doc_ids[None, :] < doc_ids[:, None]).astype(jnp.int32), axis=1)
    last_run_start = block_first + less_count[tok_dev - 1]
    digit = 64
    slot_count = owners * capacity
    meta = jnp.stack(
        [
            places // digit,
            places % digit,
            jnp.broadcast_to(last_id, (slot_count,)),
            jnp.broadcast_to(last_run_start // digit, (slot_count,)),
            jnp.broadcast_to(last_run_start % digit, (slot_count,)),
        ],
        axis=1,
    )
    meta_width = 128
    meta = jnp.pad(meta, ((0, 0), (0, meta_width - meta.shape[1]))).astype(hidden_rows.dtype)
    wide = jnp.concatenate([outgoing, meta], axis=1)
    arrived_wide = lax.all_to_all(
        wide.reshape(owners, capacity, columns + meta_width), ("chip", "core"),
        split_axis=0, concat_axis=0, tiled=True,
    )
    arrived = arrived_wide[:, :, :columns]
    arrived_meta = arrived_wide[:, :, columns:columns + 5].astype(jnp.int32)
    arrived_rows = (arrived_meta[:, :, 0] * digit + arrived_meta[:, :, 1]).reshape(-1)
    peer_last_id = arrived_meta[:, 0, 2]
    peer_run_start = arrived_meta[:, 0, 3] * digit + arrived_meta[:, 0, 4]
    earlier = (owner_ids < my_index) & (peer_last_id == first_id)
    doc_low = jnp.minimum(block_first, jnp.min(jnp.where(earlier, peer_run_start, block_first)))
    row_index = block_first + jnp.arange(tok_dev, dtype=jnp.int32)
    row_start = jnp.where(doc_ids == first_id, doc_low, block_first + less_count)

    routed_part = (
        jnp.zeros((tok_dev, columns), hidden_rows.dtype)
        .at[arrived_rows]
        .set(arrived.reshape(-1, columns), mode="drop")
    )
    routed = lax.all_gather(routed_part, "mp", axis=1, tiled=True)
    normed = normalize(routed, norm_gain)
    heads_dev = w_query.shape[1] // HD
    kv_dev = w_key.shape[1] // HD
    angles = rope_angles(row_index)
    queries = jnp.dot(normed, w_query, preferred_element_type=jnp.float32).reshape(
        tok_dev, heads_dev, HD
    )
    queries = rotate(queries, angles).astype(jnp.bfloat16).reshape(tok_dev, heads_dev * HD)
    keys_own = jnp.dot(normed, w_key, preferred_element_type=jnp.float32).reshape(
        tok_dev, kv_dev, HD
    )
    keys_own = rotate(keys_own, angles).astype(jnp.bfloat16).reshape(tok_dev, kv_dev * HD)
    values_own = jnp.dot(normed, w_value, preferred_element_type=jnp.float32).astype(jnp.bfloat16)
    kv_own = jnp.concatenate([keys_own, values_own], axis=1)
    half = tok_dev // 2
    kv_low = lax.all_gather(kv_own[:half], ("chip", "core"), axis=0, tiled=True)
    kv_high = lax.all_gather(kv_own[half:], ("chip", "core"), axis=0, tiled=True)

    block = KEY_BLOCK
    last_block = (block_first + tok_dev - 1) // block
    first_block = doc_low // block
    max_blocks = min((tok_dev - 1) // block + -(-(DOC_MAX - 1) // block) + 1, owners * tok_dev // block)
    max_pairs = min(max_blocks // 2 + 1, owners * tok_dev // block // 2)
    max_start = jnp.max(row_start)

    def span_for(offset):
        return jnp.stack(
            [first_block, last_block // 2 - first_block // 2 + 1, max_start, block_first, block, offset]
        ).astype(jnp.int32)

    queries_t = jnp.transpose(queries.reshape(tok_dev, heads_dev, HD), (1, 2, 0))
    state = flash_pass(
        span_for(0), queries_t, kv_low, row_start[None, :], row_index[None, :], half, max_pairs, None
    )
    context_t = flash_pass(
        span_for(half), queries_t, kv_high, row_start[None, :], row_index[None, :], half, max_pairs,
        state,
    )
    context = jnp.transpose(context_t, (2, 0, 1)).reshape(tok_dev, heads_dev * HD)
    context_all = lax.all_gather(context, "mp", axis=1, tiled=True)
    mp_size = lax.axis_size("mp")
    w_split = jnp.transpose(w_out.reshape(w_out.shape[0], mp_size, -1), (1, 0, 2))
    w_cols = lax.all_to_all(w_split, "mp", split_axis=0, concat_axis=0, tiled=True)
    summed = jnp.einsum(
        "tsr,src->tc",
        context_all.reshape(tok_dev, mp_size, -1),
        w_cols,
        preferred_element_type=jnp.float32,
    )
    attended = (routed_part.astype(jnp.float32) + summed).astype(jnp.bfloat16)
    backward = attended[jnp.minimum(arrived_rows, tok_dev - 1)].reshape(owners, capacity, columns)
    returned = lax.all_to_all(backward, ("chip", "core"), split_axis=0, concat_axis=0, tiled=True)
    return returned.reshape(owners * capacity, columns)[flat_slot]


def solution(mesh):
    dp_size, mp_size = mesh.devices.shape
    split_mesh = jax.sharding.Mesh(
        mesh.devices.reshape(dp_size // 2, 2, mp_size), ("chip", "core", "mp")
    )
    rows = ("chip", "core")
    in_specs = (
        P(rows, "mp"),
        P(rows),
        P(rows),
        P(),
        P(None, "mp"),
        P(None, "mp"),
        P(None, "mp"),
        P("mp", None),
    )
    out_specs = P(rows, "mp")
    return jax.shard_map(
        local, mesh=split_mesh, in_specs=in_specs, out_specs=out_specs, check_vma=False
    )
```

```python
import functools
import math

import jax
import jax.numpy as jnp
from jax import lax
from jax.experimental import pallas as pl
from jax.experimental.pallas import tpu as pltpu
from jax.sharding import PartitionSpec as P

HD = 128
DOC_MAX = 8704

ROPE_BASE = 500000.0
NORM_EPS = 1e-05
NEG_START = -1e30
KEY_BLOCK = 512
GROUP = 4


def rope_angles(row_index):
    lane_index = jnp.arange(HD // 2, dtype=jnp.float32)
    frequency = jnp.power(jnp.float32(ROPE_BASE), -2.0 * lane_index / HD)
    return row_index.astype(jnp.float32)[:, None] * frequency[None, :]


def rotate(head_values, angles):
    half_width = head_values.shape[-1] // 2
    first_half = head_values[..., :half_width]
    second_half = head_values[..., half_width:]
    cosine = jnp.cos(angles)[:, None, :]
    sine_part = jnp.sin(angles)[:, None, :]
    return jnp.concatenate(
        [
            first_half * cosine - second_half * sine_part,
            second_half * cosine + first_half * sine_part,
        ],
        axis=-1,
    )


def normalize(routed, norm_gain):
    wide_rows = routed.astype(jnp.float32)
    inv_rms = lax.rsqrt(jnp.mean(wide_rows * wide_rows, axis=1, keepdims=True) + NORM_EPS)
    return (wide_rows * inv_rms * norm_gain[None, :]).astype(jnp.bfloat16)


def flash_kernel(final, span_ref, *refs):
    if final:
        q_ref, k_ref, v_ref, start_ref, row_ref, m_in, l_in, acc_in, o_ref, m_sc, l_sc, acc_sc = refs
    else:
        q_ref, k_ref, v_ref, start_ref, row_ref, m_sc, l_sc, acc_sc = refs
    step = pl.program_id(0)
    heads = m_sc.shape[0]
    block = k_ref.shape[0]
    scale = HD ** (-0.5)

    @pl.when(step == 0)
    def _init():
        if final:
            m_sc[...] = m_in[...]
            l_sc[...] = l_in[...]
            acc_sc[...] = acc_in[...]
        else:
            m_sc[...] = jnp.full(m_sc.shape, NEG_START, jnp.float32)
            l_sc[...] = jnp.zeros(l_sc.shape, jnp.float32)
            acc_sc[...] = jnp.zeros(acc_sc.shape, jnp.float32)

    part = block // GROUP
    pair = span_ref[0] // GROUP + step
    key_first = GROUP * pair * span_ref[4] + span_ref[5]
    key_last = (GROUP * pair + GROUP - 1) * span_ref[4] + span_ref[5] + part - 1
    active = step < span_ref[1]
    whole = (key_first >= span_ref[2]) & (key_last <= span_ref[3])

    def accumulate(masked):
        keys = k_ref[...]
        values = v_ref[...]
        if masked:
            sub = lax.broadcasted_iota(jnp.int32, (block, 1), 0)
            key_rows = key_first + (sub // part) * span_ref[4] + sub % part
            allowed = (key_rows >= start_ref[...]) & (key_rows <= row_ref[...])
        for h in range(heads):
            scores = jnp.dot(keys, q_ref[h], preferred_element_type=jnp.float32) * scale
            if masked:
                scores = jnp.where(allowed, scores, -jnp.inf)
            m_old = m_sc[h]
            m_new = jnp.maximum(m_old, jnp.max(scores, axis=0, keepdims=True))
            rescale = jnp.exp(m_old - m_new)
            exp_scores = jnp.exp(scores - m_new)
            l_sc[h] = l_sc[h] * rescale + jnp.sum(exp_scores, axis=0, keepdims=True)
            acc_sc[h] = acc_sc[h] * rescale + lax.dot_general(
                values, exp_scores.astype(jnp.bfloat16), (((0,), (0,)), ((), ())),
                preferred_element_type=jnp.float32,
            )
            m_sc[h] = m_new

    @pl.when(active & whole)
    def _whole():
        accumulate(False)

    @pl.when(active & jnp.logical_not(whole))
    def _masked():
        accumulate(True)

    if final:
        @pl.when(step == pl.num_programs(0) - 1)
        def _finish():
            for h in range(heads):
                o_ref[h] = (acc_sc[h] / l_sc[h]).astype(o_ref.dtype)


def flash_pass(span, queries_t, kv_part, row_start, row_index, block, max_blocks, state):
    heads, _, rows = queries_t.shape
    final = state is not None

    def kv_map(column):
        def index_map(step, span_ref):
            return (span_ref[0] // GROUP + jnp.minimum(step, span_ref[1] - 1), column)
        return index_map

    fixed2 = lambda step, span_ref: (0, 0)
    fixed3 = lambda step, span_ref: (0, 0, 0)
    in_specs = [
        pl.BlockSpec((heads, HD, rows), fixed3),
        pl.BlockSpec((GROUP * block, HD), kv_map(0)),
        pl.BlockSpec((GROUP * block, HD), kv_map(1)),
        pl.BlockSpec((1, rows), fixed2),
        pl.BlockSpec((1, rows), fixed2),
    ]
    state_shapes = [
        jax.ShapeDtypeStruct((heads, 1, rows), jnp.float32),
        jax.ShapeDtypeStruct((heads, 1, rows), jnp.float32),
        jax.ShapeDtypeStruct((heads, HD, rows), jnp.float32),
    ]
    state_specs = [pl.BlockSpec(x.shape, fixed3) for x in state_shapes]
    if final:
        in_specs = in_specs + state_specs
        out_specs = pl.BlockSpec((heads, HD, rows), fixed3)
        out_shape = jax.ShapeDtypeStruct((heads, HD, rows), jnp.bfloat16)
        scratch = [pltpu.VMEM(x.shape, jnp.float32) for x in state_shapes]
        operands = (span, queries_t, kv_part, kv_part, row_start, row_index) + tuple(state)
    else:
        out_specs = state_specs
        out_shape = state_shapes
        scratch = []
        operands = (span, queries_t, kv_part, kv_part, row_start, row_index)
    grid_spec = pltpu.PrefetchScalarGridSpec(
        num_scalar_prefetch=1,
        grid=(max_blocks,),
        in_specs=in_specs,
        out_specs=out_specs,
        scratch_shapes=scratch,
    )
    flops = 4 * GROUP * heads * rows * block * HD * max_blocks
    return pl.pallas_call(
        functools.partial(flash_kernel, final),
        grid_spec=grid_spec,
        out_shape=out_shape,
        compiler_params=pltpu.CompilerParams(dimension_semantics=("arbitrary",)),
        cost_estimate=pl.CostEstimate(
            flops=flops,
            transcendentals=GROUP * heads * rows * block * max_blocks,
            bytes_accessed=2 * GROUP * block * HD * 2 * max_blocks + 2 * 2 * rows * heads * HD,
        ),
    )(*operands)


def local(hidden_rows, destination, doc_ids, norm_gain, w_query, w_key, w_value, w_out):
    owners = lax.axis_size(("chip", "core"))
    my_index = lax.axis_index(("chip", "core"))
    tok_dev, columns = hidden_rows.shape
    capacity = 2 * tok_dev // owners
    target = destination // tok_dev
    owner_ids = jnp.arange(owners, dtype=jnp.int32)
    one_hot = (target[:, None] == owner_ids[None, :]).astype(jnp.int32)
    slot_rank = jnp.sum((jnp.cumsum(one_hot, axis=0) - 1) * one_hot, axis=1)
    flat_slot = target * capacity + slot_rank
    outgoing = (
        jnp.zeros((owners * capacity, columns), hidden_rows.dtype).at[flat_slot].set(hidden_rows)
    )
    places = (
        jnp.full((owners * capacity,), tok_dev, jnp.int32).at[flat_slot].set(destination % tok_dev)
    )
    block_first = my_index * tok_dev
    first_id = doc_ids[0]
    last_id = doc_ids[tok_dev - 1]
    less_count = jnp.sum((doc_ids[None, :] < doc_ids[:, None]).astype(jnp.int32), axis=1)
    last_run_start = block_first + less_count[tok_dev - 1]
    digit = 64
    slot_count = owners * capacity
    meta = jnp.stack(
        [
            places // digit,
            places % digit,
            jnp.broadcast_to(last_id, (slot_count,)),
            jnp.broadcast_to(last_run_start // digit, (slot_count,)),
            jnp.broadcast_to(last_run_start % digit, (slot_count,)),
        ],
        axis=1,
    )
    meta_width = 128
    meta = jnp.pad(meta, ((0, 0), (0, meta_width - meta.shape[1]))).astype(hidden_rows.dtype)
    wide = jnp.concatenate([outgoing, meta], axis=1)
    arrived_wide = lax.all_to_all(
        wide.reshape(owners, capacity, columns + meta_width), ("chip", "core"),
        split_axis=0, concat_axis=0, tiled=True,
    )
    arrived = arrived_wide[:, :, :columns]
    arrived_meta = arrived_wide[:, :, columns:columns + 5].astype(jnp.int32)
    arrived_rows = (arrived_meta[:, :, 0] * digit + arrived_meta[:, :, 1]).reshape(-1)
    peer_last_id = arrived_meta[:, 0, 2]
    peer_run_start = arrived_meta[:, 0, 3] * digit + arrived_meta[:, 0, 4]
    earlier = (owner_ids < my_index) & (peer_last_id == first_id)
    doc_low = jnp.minimum(block_first, jnp.min(jnp.where(earlier, peer_run_start, block_first)))
    row_index = block_first + jnp.arange(tok_dev, dtype=jnp.int32)
    row_start = jnp.where(doc_ids == first_id, doc_low, block_first + less_count)

    routed_part = (
        jnp.zeros((tok_dev, columns), hidden_rows.dtype)
        .at[arrived_rows]
        .set(arrived.reshape(-1, columns), mode="drop")
    )
    routed = lax.all_gather(routed_part, "mp", axis=1, tiled=True)
    normed = normalize(routed, norm_gain)
    heads_dev = w_query.shape[1] // HD
    kv_dev = w_key.shape[1] // HD
    angles = rope_angles(row_index)
    queries = jnp.dot(normed, w_query, preferred_element_type=jnp.float32).reshape(
        tok_dev, heads_dev, HD
    )
    queries = rotate(queries, angles).astype(jnp.bfloat16).reshape(tok_dev, heads_dev * HD)
    keys_own = jnp.dot(normed, w_key, preferred_element_type=jnp.float32).reshape(
        tok_dev, kv_dev, HD
    )
    keys_own = rotate(keys_own, angles).astype(jnp.bfloat16).reshape(tok_dev, kv_dev * HD)
    values_own = jnp.dot(normed, w_value, preferred_element_type=jnp.float32).astype(jnp.bfloat16)
    kv_own = jnp.concatenate([keys_own, values_own], axis=1)
    half = tok_dev // 2
    kv_low = lax.all_gather(kv_own[:half], ("chip", "core"), axis=0, tiled=True)
    kv_high = lax.all_gather(kv_own[half:], ("chip", "core"), axis=0, tiled=True)

    block = KEY_BLOCK
    last_block = (block_first + tok_dev - 1) // block
    first_block = doc_low // block
    max_blocks = min((tok_dev - 1) // block + -(-(DOC_MAX - 1) // block) + 1, owners * tok_dev // block)
    max_pairs = min((max_blocks - 1) // GROUP + 2, owners * tok_dev // block // GROUP)
    max_start = jnp.max(row_start)

    def span_for(offset):
        return jnp.stack(
            [first_block, last_block // GROUP - first_block // GROUP + 1, max_start, block_first, block, offset]
        ).astype(jnp.int32)

    queries_t = jnp.transpose(queries.reshape(tok_dev, heads_dev, HD), (1, 2, 0))
    state = flash_pass(
        span_for(0), queries_t, kv_low, row_start[None, :], row_index[None, :], half, max_pairs, None
    )
    context_t = flash_pass(
        span_for(half), queries_t, kv_high, row_start[None, :], row_index[None, :], half, max_pairs,
        state,
    )
    context = jnp.transpose(context_t, (2, 0, 1)).reshape(tok_dev, heads_dev * HD)
    context_all = lax.all_gather(context, "mp", axis=1, tiled=True)
    mp_size = lax.axis_size("mp")
    w_split = jnp.transpose(w_out.reshape(w_out.shape[0], mp_size, -1), (1, 0, 2))
    w_cols = lax.all_to_all(w_split, "mp", split_axis=0, concat_axis=0, tiled=True)
    summed = jnp.einsum(
        "tsr,src->tc",
        context_all.reshape(tok_dev, mp_size, -1),
        w_cols,
        preferred_element_type=jnp.float32,
    )
    attended = (routed_part.astype(jnp.float32) + summed).astype(jnp.bfloat16)
    backward = attended[jnp.minimum(arrived_rows, tok_dev - 1)].reshape(owners, capacity, columns)
    returned = lax.all_to_all(backward, ("chip", "core"), split_axis=0, concat_axis=0, tiled=True)
    return returned.reshape(owners * capacity, columns)[flat_slot]


def solution(mesh):
    dp_size, mp_size = mesh.devices.shape
    split_mesh = jax.sharding.Mesh(
        mesh.devices.reshape(dp_size // 2, 2, mp_size), ("chip", "core", "mp")
    )
    rows = ("chip", "core")
    in_specs = (
        P(rows, "mp"),
        P(rows),
        P(rows),
        P(),
        P(None, "mp"),
        P(None, "mp"),
        P(None, "mp"),
        P("mp", None),
    )
    out_specs = P(rows, "mp")
    return jax.shard_map(
        local, mesh=split_mesh, in_specs=in_specs, out_specs=out_specs, check_vma=False
    )
```

```python
import functools
import math

import jax
import jax.numpy as jnp
from jax import lax
from jax.experimental import pallas as pl
from jax.experimental.pallas import tpu as pltpu
from jax.sharding import PartitionSpec as P

HD = 128
DOC_MAX = 8704

ROPE_BASE = 500000.0
NORM_EPS = 1e-05
NEG_START = -1e30
KEY_BLOCK = 512


def rope_angles(row_index):
    lane_index = jnp.arange(HD // 2, dtype=jnp.float32)
    frequency = jnp.power(jnp.float32(ROPE_BASE), -2.0 * lane_index / HD)
    return row_index.astype(jnp.float32)[:, None] * frequency[None, :]


def rotate(head_values, angles):
    half_width = head_values.shape[-1] // 2
    first_half = head_values[..., :half_width]
    second_half = head_values[..., half_width:]
    cosine = jnp.cos(angles)[:, None, :]
    sine_part = jnp.sin(angles)[:, None, :]
    return jnp.concatenate(
        [
            first_half * cosine - second_half * sine_part,
            second_half * cosine + first_half * sine_part,
        ],
        axis=-1,
    )


def normalize(routed, norm_gain):
    wide_rows = routed.astype(jnp.float32)
    inv_rms = lax.rsqrt(jnp.mean(wide_rows * wide_rows, axis=1, keepdims=True) + NORM_EPS)
    return (wide_rows * inv_rms * norm_gain[None, :]).astype(jnp.bfloat16)


def flash_kernel(final, span_ref, *refs):
    if final:
        q_ref, k_ref, v_ref, start_ref, row_ref, m_in, l_in, acc_in, o_ref, m_sc, l_sc, acc_sc = refs
    else:
        q_ref, k_ref, v_ref, start_ref, row_ref, m_sc, l_sc, acc_sc = refs
    step = pl.program_id(0)
    heads = m_sc.shape[0]
    block = k_ref.shape[0]
    scale = HD ** (-0.5)

    @pl.when(step == 0)
    def _init():
        if final:
            m_sc[...] = m_in[...]
            l_sc[...] = l_in[...]
            acc_sc[...] = acc_in[...]
        else:
            m_sc[...] = jnp.full(m_sc.shape, NEG_START, jnp.float32)
            l_sc[...] = jnp.zeros(l_sc.shape, jnp.float32)
            acc_sc[...] = jnp.zeros(acc_sc.shape, jnp.float32)

    part = block // 2
    pair = span_ref[0] // 2 + step
    key_first = 2 * pair * span_ref[4] + span_ref[5]
    key_last = (2 * pair + 1) * span_ref[4] + span_ref[5] + part - 1
    active = step < span_ref[1]
    whole = (key_first >= span_ref[2]) & (key_last <= span_ref[3])

    def accumulate(masked):
        keys = k_ref[...]
        values = v_ref[...]
        if masked:
            sub = lax.broadcasted_iota(jnp.int32, (block, 1), 0)
            key_rows = key_first + (sub // part) * span_ref[4] + sub % part
            allowed = (key_rows >= start_ref[...]) & (key_rows <= row_ref[...])
        def one_head(h, carry):
            scores = jnp.dot(keys, q_ref[h], preferred_element_type=jnp.float32) * scale
            if masked:
                scores = jnp.where(allowed, scores, -jnp.inf)
            m_old = m_sc[h]
            m_new = jnp.maximum(m_old, jnp.max(scores, axis=0, keepdims=True))
            rescale = jnp.exp(m_old - m_new)
            exp_scores = jnp.exp(scores - m_new)
            l_sc[h] = l_sc[h] * rescale + jnp.sum(exp_scores, axis=0, keepdims=True)
            acc_sc[h] = acc_sc[h] * rescale + lax.dot_general(
                values, exp_scores.astype(jnp.bfloat16), (((0,), (0,)), ((), ())),
                preferred_element_type=jnp.float32,
            )
            m_sc[h] = m_new
            return carry

        lax.fori_loop(0, heads, one_head, 0)

    @pl.when(active & whole)
    def _whole():
        accumulate(False)

    @pl.when(active & jnp.logical_not(whole))
    def _masked():
        accumulate(True)

    if final:
        @pl.when(step == pl.num_programs(0) - 1)
        def _finish():
            for h in range(heads):
                o_ref[h] = (acc_sc[h] / l_sc[h]).astype(o_ref.dtype)


def flash_pass(span, queries_t, kv_part, row_start, row_index, block, max_blocks, state):
    heads, _, rows = queries_t.shape
    final = state is not None

    def kv_map(column):
        def index_map(step, span_ref):
            return (span_ref[0] // 2 + jnp.minimum(step, span_ref[1] - 1), column)
        return index_map

    fixed2 = lambda step, span_ref: (0, 0)
    fixed3 = lambda step, span_ref: (0, 0, 0)
    in_specs = [
        pl.BlockSpec((heads, HD, rows), fixed3),
        pl.BlockSpec((2 * block, HD), kv_map(0)),
        pl.BlockSpec((2 * block, HD), kv_map(1)),
        pl.BlockSpec((1, rows), fixed2),
        pl.BlockSpec((1, rows), fixed2),
    ]
    state_shapes = [
        jax.ShapeDtypeStruct((heads, 1, rows), jnp.float32),
        jax.ShapeDtypeStruct((heads, 1, rows), jnp.float32),
        jax.ShapeDtypeStruct((heads, HD, rows), jnp.float32),
    ]
    state_specs = [pl.BlockSpec(x.shape, fixed3) for x in state_shapes]
    if final:
        in_specs = in_specs + state_specs
        out_specs = pl.BlockSpec((heads, HD, rows), fixed3)
        out_shape = jax.ShapeDtypeStruct((heads, HD, rows), jnp.bfloat16)
        scratch = [pltpu.VMEM(x.shape, jnp.float32) for x in state_shapes]
        operands = (span, queries_t, kv_part, kv_part, row_start, row_index) + tuple(state)
    else:
        out_specs = state_specs
        out_shape = state_shapes
        scratch = []
        operands = (span, queries_t, kv_part, kv_part, row_start, row_index)
    grid_spec = pltpu.PrefetchScalarGridSpec(
        num_scalar_prefetch=1,
        grid=(max_blocks,),
        in_specs=in_specs,
        out_specs=out_specs,
        scratch_shapes=scratch,
    )
    flops = 8 * heads * rows * block * HD * max_blocks
    return pl.pallas_call(
        functools.partial(flash_kernel, final),
        grid_spec=grid_spec,
        out_shape=out_shape,
        compiler_params=pltpu.CompilerParams(dimension_semantics=("arbitrary",)),
        cost_estimate=pl.CostEstimate(
            flops=flops,
            transcendentals=2 * heads * rows * block * max_blocks,
            bytes_accessed=4 * block * HD * 2 * max_blocks + 2 * 2 * rows * heads * HD,
        ),
    )(*operands)


def local(hidden_rows, destination, doc_ids, norm_gain, w_query, w_key, w_value, w_out):
    owners = lax.axis_size(("chip", "core"))
    my_index = lax.axis_index(("chip", "core"))
    tok_dev, columns = hidden_rows.shape
    capacity = 2 * tok_dev // owners
    target = destination // tok_dev
    owner_ids = jnp.arange(owners, dtype=jnp.int32)
    one_hot = (target[:, None] == owner_ids[None, :]).astype(jnp.int32)
    slot_rank = jnp.sum((jnp.cumsum(one_hot, axis=0) - 1) * one_hot, axis=1)
    flat_slot = target * capacity + slot_rank
    outgoing = (
        jnp.zeros((owners * capacity, columns), hidden_rows.dtype).at[flat_slot].set(hidden_rows)
    )
    places = (
        jnp.full((owners * capacity,), tok_dev, jnp.int32).at[flat_slot].set(destination % tok_dev)
    )
    block_first = my_index * tok_dev
    first_id = doc_ids[0]
    last_id = doc_ids[tok_dev - 1]
    less_count = jnp.sum((doc_ids[None, :] < doc_ids[:, None]).astype(jnp.int32), axis=1)
    last_run_start = block_first + less_count[tok_dev - 1]
    digit = 64
    slot_count = owners * capacity
    meta = jnp.stack(
        [
            places // digit,
            places % digit,
            jnp.broadcast_to(last_id, (slot_count,)),
            jnp.broadcast_to(last_run_start // digit, (slot_count,)),
            jnp.broadcast_to(last_run_start % digit, (slot_count,)),
        ],
        axis=1,
    )
    meta_width = 128
    meta = jnp.pad(meta, ((0, 0), (0, meta_width - meta.shape[1]))).astype(hidden_rows.dtype)
    wide = jnp.concatenate([outgoing, meta], axis=1)
    arrived_wide = lax.all_to_all(
        wide.reshape(owners, capacity, columns + meta_width), ("chip", "core"),
        split_axis=0, concat_axis=0, tiled=True,
    )
    arrived = arrived_wide[:, :, :columns]
    arrived_meta = arrived_wide[:, :, columns:columns + 5].astype(jnp.int32)
    arrived_rows = (arrived_meta[:, :, 0] * digit + arrived_meta[:, :, 1]).reshape(-1)
    peer_last_id = arrived_meta[:, 0, 2]
    peer_run_start = arrived_meta[:, 0, 3] * digit + arrived_meta[:, 0, 4]
    earlier = (owner_ids < my_index) & (peer_last_id == first_id)
    doc_low = jnp.minimum(block_first, jnp.min(jnp.where(earlier, peer_run_start, block_first)))
    row_index = block_first + jnp.arange(tok_dev, dtype=jnp.int32)
    row_start = jnp.where(doc_ids == first_id, doc_low, block_first + less_count)

    routed_part = (
        jnp.zeros((tok_dev, columns), hidden_rows.dtype)
        .at[arrived_rows]
        .set(arrived.reshape(-1, columns), mode="drop")
    )
    routed = lax.all_gather(routed_part, "mp", axis=1, tiled=True)
    normed = normalize(routed, norm_gain)
    heads_dev = w_query.shape[1] // HD
    kv_dev = w_key.shape[1] // HD
    angles = rope_angles(row_index)
    queries = jnp.dot(normed, w_query, preferred_element_type=jnp.float32).reshape(
        tok_dev, heads_dev, HD
    )
    queries = rotate(queries, angles).astype(jnp.bfloat16).reshape(tok_dev, heads_dev * HD)
    keys_own = jnp.dot(normed, w_key, preferred_element_type=jnp.float32).reshape(
        tok_dev, kv_dev, HD
    )
    keys_own = rotate(keys_own, angles).astype(jnp.bfloat16).reshape(tok_dev, kv_dev * HD)
    values_own = jnp.dot(normed, w_value, preferred_element_type=jnp.float32).astype(jnp.bfloat16)
    kv_own = jnp.concatenate([keys_own, values_own], axis=1)
    half = tok_dev // 2
    kv_low = lax.all_gather(kv_own[:half], ("chip", "core"), axis=0, tiled=True)
    kv_high = lax.all_gather(kv_own[half:], ("chip", "core"), axis=0, tiled=True)

    block = KEY_BLOCK
    last_block = (block_first + tok_dev - 1) // block
    first_block = doc_low // block
    max_blocks = min((tok_dev - 1) // block + -(-(DOC_MAX - 1) // block) + 1, owners * tok_dev // block)
    max_pairs = min(max_blocks // 2 + 1, owners * tok_dev // block // 2)
    max_start = jnp.max(row_start)

    def span_for(offset):
        return jnp.stack(
            [first_block, last_block // 2 - first_block // 2 + 1, max_start, block_first, block, offset]
        ).astype(jnp.int32)

    queries_t = jnp.transpose(queries.reshape(tok_dev, heads_dev, HD), (1, 2, 0))
    state = flash_pass(
        span_for(0), queries_t, kv_low, row_start[None, :], row_index[None, :], half, max_pairs, None
    )
    context_t = flash_pass(
        span_for(half), queries_t, kv_high, row_start[None, :], row_index[None, :], half, max_pairs,
        state,
    )
    context = jnp.transpose(context_t, (2, 0, 1)).reshape(tok_dev, heads_dev * HD)
    context_all = lax.all_gather(context, "mp", axis=1, tiled=True)
    mp_size = lax.axis_size("mp")
    w_split = jnp.transpose(w_out.reshape(w_out.shape[0], mp_size, -1), (1, 0, 2))
    w_cols = lax.all_to_all(w_split, "mp", split_axis=0, concat_axis=0, tiled=True)
    summed = jnp.einsum(
        "tsr,src->tc",
        context_all.reshape(tok_dev, mp_size, -1),
        w_cols,
        preferred_element_type=jnp.float32,
    )
    attended = (routed_part.astype(jnp.float32) + summed).astype(jnp.bfloat16)
    backward = attended[jnp.minimum(arrived_rows, tok_dev - 1)].reshape(owners, capacity, columns)
    returned = lax.all_to_all(backward, ("chip", "core"), split_axis=0, concat_axis=0, tiled=True)
    return returned.reshape(owners * capacity, columns)[flat_slot]


def solution(mesh):
    dp_size, mp_size = mesh.devices.shape
    split_mesh = jax.sharding.Mesh(
        mesh.devices.reshape(dp_size // 2, 2, mp_size), ("chip", "core", "mp")
    )
    rows = ("chip", "core")
    in_specs = (
        P(rows, "mp"),
        P(rows),
        P(rows),
        P(),
        P(None, "mp"),
        P(None, "mp"),
        P(None, "mp"),
        P("mp", None),
    )
    out_specs = P(rows, "mp")
    return jax.shard_map(
        local, mesh=split_mesh, in_specs=in_specs, out_specs=out_specs, check_vma=False
    )
```

```python
import functools
import math

import jax
import jax.numpy as jnp
from jax import lax
from jax.experimental import pallas as pl
from jax.experimental.pallas import tpu as pltpu
from jax.sharding import PartitionSpec as P

HD = 128
DOC_MAX = 8704

ROPE_BASE = 500000.0
NORM_EPS = 1e-05
NEG_START = -1e30
KEY_BLOCK = 512


def rope_angles(row_index):
    lane_index = jnp.arange(HD // 2, dtype=jnp.float32)
    frequency = jnp.power(jnp.float32(ROPE_BASE), -2.0 * lane_index / HD)
    return row_index.astype(jnp.float32)[:, None] * frequency[None, :]


def rotate(head_values, angles):
    half_width = head_values.shape[-1] // 2
    first_half = head_values[..., :half_width]
    second_half = head_values[..., half_width:]
    cosine = jnp.cos(angles)[:, None, :]
    sine_part = jnp.sin(angles)[:, None, :]
    return jnp.concatenate(
        [
            first_half * cosine - second_half * sine_part,
            second_half * cosine + first_half * sine_part,
        ],
        axis=-1,
    )


def normalize(routed, norm_gain):
    wide_rows = routed.astype(jnp.float32)
    inv_rms = lax.rsqrt(jnp.mean(wide_rows * wide_rows, axis=1, keepdims=True) + NORM_EPS)
    return (wide_rows * inv_rms * norm_gain[None, :]).astype(jnp.bfloat16)


def flash_kernel(final, span_ref, *refs):
    if final:
        q_ref, k_ref, v_ref, start_ref, row_ref, m_in, l_in, acc_in, o_ref, m_sc, l_sc, acc_sc = refs
    else:
        q_ref, k_ref, v_ref, start_ref, row_ref, m_sc, l_sc, acc_sc = refs
    step = pl.program_id(0)
    heads = m_sc.shape[0]
    block = k_ref.shape[0]
    scale = HD ** (-0.5)

    @pl.when(step == 0)
    def _init():
        if final:
            m_sc[...] = m_in[...]
            l_sc[...] = l_in[...]
            acc_sc[...] = acc_in[...]
        else:
            m_sc[...] = jnp.full(m_sc.shape, NEG_START, jnp.float32)
            l_sc[...] = jnp.zeros(l_sc.shape, jnp.float32)
            acc_sc[...] = jnp.zeros(acc_sc.shape, jnp.float32)

    part = block // 2
    pair = span_ref[0] // 2 + step
    key_first = 2 * pair * span_ref[4] + span_ref[5]
    key_last = (2 * pair + 1) * span_ref[4] + span_ref[5] + part - 1
    active = step < span_ref[1]
    whole = (key_first >= span_ref[2]) & (key_last <= span_ref[3])

    def accumulate(masked):
        keys = k_ref[...]
        values = v_ref[...]
        if masked:
            sub = lax.broadcasted_iota(jnp.int32, (block, 1), 0)
            key_rows = key_first + (sub // part) * span_ref[4] + sub % part
            allowed = (key_rows >= start_ref[...]) & (key_rows <= row_ref[...])
        for h in range(heads):
            scores = jnp.dot(keys, q_ref[h], preferred_element_type=jnp.float32) * scale
            if masked:
                scores = jnp.where(allowed, scores, -jnp.inf)
            m_old = m_sc[h]
            m_new = jnp.maximum(m_old, jnp.max(scores, axis=0, keepdims=True))
            rescale = jnp.exp(m_old - m_new)
            exp_scores = jnp.exp(scores - m_new)
            l_sc[h] = l_sc[h] * rescale + jnp.sum(exp_scores, axis=0, keepdims=True)
            acc_sc[h] = acc_sc[h] * rescale + lax.dot_general(
                values, exp_scores.astype(jnp.bfloat16), (((0,), (0,)), ((), ())),
                preferred_element_type=jnp.float32,
            )
            m_sc[h] = m_new

    @pl.when(active & whole)
    def _whole():
        accumulate(False)

    @pl.when(active & jnp.logical_not(whole))
    def _masked():
        accumulate(True)

    if final:
        @pl.when(step == pl.num_programs(0) - 1)
        def _finish():
            for h in range(heads):
                o_ref[h] = (acc_sc[h] / l_sc[h]).astype(o_ref.dtype)


def flash_pass(span, queries_t, kv_part, row_start, row_index, block, max_blocks, state):
    heads, _, rows = queries_t.shape
    final = state is not None

    def kv_map(column):
        def index_map(step, span_ref):
            return (span_ref[0] // 2 + jnp.minimum(step, span_ref[1] - 1), column)
        return index_map

    fixed2 = lambda step, span_ref: (0, 0)
    fixed3 = lambda step, span_ref: (0, 0, 0)
    in_specs = [
        pl.BlockSpec((heads, HD, rows), fixed3),
        pl.BlockSpec((2 * block, HD), kv_map(0)),
        pl.BlockSpec((2 * block, HD), kv_map(1)),
        pl.BlockSpec((1, rows), fixed2),
        pl.BlockSpec((1, rows), fixed2),
    ]
    state_shapes = [
        jax.ShapeDtypeStruct((heads, 1, rows), jnp.float32),
        jax.ShapeDtypeStruct((heads, 1, rows), jnp.float32),
        jax.ShapeDtypeStruct((heads, HD, rows), jnp.float32),
    ]
    state_specs = [pl.BlockSpec(x.shape, fixed3) for x in state_shapes]
    if final:
        in_specs = in_specs + state_specs
        out_specs = pl.BlockSpec((heads, HD, rows), fixed3)
        out_shape = jax.ShapeDtypeStruct((heads, HD, rows), jnp.bfloat16)
        scratch = [pltpu.VMEM(x.shape, jnp.float32) for x in state_shapes]
        operands = (span, queries_t, kv_part, kv_part, row_start, row_index) + tuple(state)
    else:
        out_specs = state_specs
        out_shape = state_shapes
        scratch = []
        operands = (span, queries_t, kv_part, kv_part, row_start, row_index)
    grid_spec = pltpu.PrefetchScalarGridSpec(
        num_scalar_prefetch=1,
        grid=(max_blocks,),
        in_specs=in_specs,
        out_specs=out_specs,
        scratch_shapes=scratch,
    )
    flops = 8 * heads * rows * block * HD * max_blocks
    return pl.pallas_call(
        functools.partial(flash_kernel, final),
        grid_spec=grid_spec,
        out_shape=out_shape,
        compiler_params=pltpu.CompilerParams(dimension_semantics=("arbitrary",)),
        cost_estimate=pl.CostEstimate(
            flops=flops,
            transcendentals=2 * heads * rows * block * max_blocks,
            bytes_accessed=4 * block * HD * 2 * max_blocks + 2 * 2 * rows * heads * HD,
        ),
    )(*operands)


def local(hidden_rows, destination, doc_ids, norm_gain, w_query, w_key, w_value, w_out):
    owners = lax.axis_size(("chip", "core"))
    my_index = lax.axis_index(("chip", "core"))
    tok_dev, columns = hidden_rows.shape
    capacity = 2 * tok_dev // owners
    target = destination // tok_dev
    owner_ids = jnp.arange(owners, dtype=jnp.int32)
    one_hot = (target[:, None] == owner_ids[None, :]).astype(jnp.int32)
    slot_rank = jnp.sum((jnp.cumsum(one_hot, axis=0) - 1) * one_hot, axis=1)
    flat_slot = target * capacity + slot_rank
    outgoing = (
        jnp.zeros((owners * capacity, columns), hidden_rows.dtype).at[flat_slot].set(hidden_rows)
    )
    places = (
        jnp.full((owners * capacity,), tok_dev, jnp.int32).at[flat_slot].set(destination % tok_dev)
    )
    block_first = my_index * tok_dev
    first_id = doc_ids[0]
    last_id = doc_ids[tok_dev - 1]
    less_count = jnp.sum((doc_ids[None, :] < doc_ids[:, None]).astype(jnp.int32), axis=1)
    last_run_start = block_first + less_count[tok_dev - 1]
    digit = 64
    slot_count = owners * capacity
    meta = jnp.stack(
        [
            places // digit,
            places % digit,
            jnp.broadcast_to(last_id, (slot_count,)),
            jnp.broadcast_to(last_run_start // digit, (slot_count,)),
            jnp.broadcast_to(last_run_start % digit, (slot_count,)),
        ],
        axis=1,
    )
    meta_width = 128
    meta = jnp.pad(meta, ((0, 0), (0, meta_width - meta.shape[1]))).astype(hidden_rows.dtype)
    wide = jnp.concatenate([outgoing, meta], axis=1)
    arrived_wide = lax.all_to_all(
        wide.reshape(owners, capacity, columns + meta_width), ("chip", "core"),
        split_axis=0, concat_axis=0, tiled=True,
    )
    arrived = arrived_wide[:, :, :columns]
    arrived_meta = arrived_wide[:, :, columns:columns + 5].astype(jnp.int32)
    arrived_rows = (arrived_meta[:, :, 0] * digit + arrived_meta[:, :, 1]).reshape(-1)
    peer_last_id = arrived_meta[:, 0, 2]
    peer_run_start = arrived_meta[:, 0, 3] * digit + arrived_meta[:, 0, 4]
    earlier = (owner_ids < my_index) & (peer_last_id == first_id)
    doc_low = jnp.minimum(block_first, jnp.min(jnp.where(earlier, peer_run_start, block_first)))
    row_index = block_first + jnp.arange(tok_dev, dtype=jnp.int32)
    row_start = jnp.where(doc_ids == first_id, doc_low, block_first + less_count)

    routed_part = (
        jnp.zeros((tok_dev, columns), hidden_rows.dtype)
        .at[arrived_rows]
        .set(arrived.reshape(-1, columns), mode="drop")
    )
    routed = lax.all_gather(routed_part, "mp", axis=1, tiled=True)
    normed = normalize(routed, norm_gain)
    heads_dev = w_query.shape[1] // HD
    kv_dev = w_key.shape[1] // HD
    angles = rope_angles(row_index)
    queries = jnp.dot(normed, w_query, preferred_element_type=jnp.float32).reshape(
        tok_dev, heads_dev, HD
    )
    queries = rotate(queries, angles).astype(jnp.bfloat16).reshape(tok_dev, heads_dev * HD)
    keys_own = jnp.dot(normed, w_key, preferred_element_type=jnp.float32).reshape(
        tok_dev, kv_dev, HD
    )
    keys_own = rotate(keys_own, angles).astype(jnp.bfloat16).reshape(tok_dev, kv_dev * HD)
    values_own = jnp.dot(normed, w_value, preferred_element_type=jnp.float32).astype(jnp.bfloat16)
    kv_own = jnp.concatenate([keys_own, values_own], axis=1)
    half = 5 * tok_dev // 8
    kv_low = lax.all_gather(kv_own[:half], ("chip", "core"), axis=0, tiled=True)
    kv_high = lax.all_gather(kv_own[half:], ("chip", "core"), axis=0, tiled=True)

    block = KEY_BLOCK
    last_block = (block_first + tok_dev - 1) // block
    first_block = doc_low // block
    max_blocks = min((tok_dev - 1) // block + -(-(DOC_MAX - 1) // block) + 1, owners * tok_dev // block)
    max_pairs = min(max_blocks // 2 + 1, owners * tok_dev // block // 2)
    max_start = jnp.max(row_start)

    def span_for(offset):
        return jnp.stack(
            [first_block, last_block // 2 - first_block // 2 + 1, max_start, block_first, block, offset]
        ).astype(jnp.int32)

    queries_t = jnp.transpose(queries.reshape(tok_dev, heads_dev, HD), (1, 2, 0))
    state = flash_pass(
        span_for(0), queries_t, kv_low, row_start[None, :], row_index[None, :], half, max_pairs, None
    )
    context_t = flash_pass(
        span_for(half), queries_t, kv_high, row_start[None, :], row_index[None, :], tok_dev - half, max_pairs,
        state,
    )
    context = jnp.transpose(context_t, (2, 0, 1)).reshape(tok_dev, heads_dev * HD)
    context_all = lax.all_gather(context, "mp", axis=1, tiled=True)
    mp_size = lax.axis_size("mp")
    w_split = jnp.transpose(w_out.reshape(w_out.shape[0], mp_size, -1), (1, 0, 2))
    w_cols = lax.all_to_all(w_split, "mp", split_axis=0, concat_axis=0, tiled=True)
    summed = jnp.einsum(
        "tsr,src->tc",
        context_all.reshape(tok_dev, mp_size, -1),
        w_cols,
        preferred_element_type=jnp.float32,
    )
    attended = (routed_part.astype(jnp.float32) + summed).astype(jnp.bfloat16)
    backward = attended[jnp.minimum(arrived_rows, tok_dev - 1)].reshape(owners, capacity, columns)
    returned = lax.all_to_all(backward, ("chip", "core"), split_axis=0, concat_axis=0, tiled=True)
    return returned.reshape(owners * capacity, columns)[flat_slot]


def solution(mesh):
    dp_size, mp_size = mesh.devices.shape
    split_mesh = jax.sharding.Mesh(
        mesh.devices.reshape(dp_size // 2, 2, mp_size), ("chip", "core", "mp")
    )
    rows = ("chip", "core")
    in_specs = (
        P(rows, "mp"),
        P(rows),
        P(rows),
        P(),
        P(None, "mp"),
        P(None, "mp"),
        P(None, "mp"),
        P("mp", None),
    )
    out_specs = P(rows, "mp")
    return jax.shard_map(
        local, mesh=split_mesh, in_specs=in_specs, out_specs=out_specs, check_vma=False
    )
```

```python
import functools
import math

import jax
import jax.numpy as jnp
from jax import lax
from jax.experimental import pallas as pl
from jax.experimental.pallas import tpu as pltpu
from jax.sharding import PartitionSpec as P

HD = 128
DOC_MAX = 8704

ROPE_BASE = 500000.0
NORM_EPS = 1e-05
NEG_START = -1e30
KEY_BLOCK = 512


def rope_angles(row_index):
    lane_index = jnp.arange(HD // 2, dtype=jnp.float32)
    frequency = jnp.power(jnp.float32(ROPE_BASE), -2.0 * lane_index / HD)
    return row_index.astype(jnp.float32)[:, None] * frequency[None, :]


def rotate(head_values, angles):
    half_width = head_values.shape[-1] // 2
    first_half = head_values[..., :half_width]
    second_half = head_values[..., half_width:]
    cosine = jnp.cos(angles)[:, None, :]
    sine_part = jnp.sin(angles)[:, None, :]
    return jnp.concatenate(
        [
            first_half * cosine - second_half * sine_part,
            second_half * cosine + first_half * sine_part,
        ],
        axis=-1,
    )


def normalize(routed, norm_gain):
    wide_rows = routed.astype(jnp.float32)
    inv_rms = lax.rsqrt(jnp.mean(wide_rows * wide_rows, axis=1, keepdims=True) + NORM_EPS)
    return (wide_rows * inv_rms * norm_gain[None, :]).astype(jnp.bfloat16)


def flash_kernel(final, group, span_ref, *refs):
    if final:
        q_ref, k_ref, v_ref, start_ref, row_ref, m_in, l_in, acc_in, o_ref, m_sc, l_sc, acc_sc = refs
    else:
        q_ref, k_ref, v_ref, start_ref, row_ref, m_sc, l_sc, acc_sc = refs
    step = pl.program_id(0)
    heads = m_sc.shape[0]
    block = k_ref.shape[0]
    scale = HD ** (-0.5)

    @pl.when(step == 0)
    def _init():
        if final:
            m_sc[...] = m_in[...]
            l_sc[...] = l_in[...]
            acc_sc[...] = acc_in[...]
        else:
            m_sc[...] = jnp.full(m_sc.shape, NEG_START, jnp.float32)
            l_sc[...] = jnp.zeros(l_sc.shape, jnp.float32)
            acc_sc[...] = jnp.zeros(acc_sc.shape, jnp.float32)

    part = block // group
    pair = span_ref[0] // group + step
    key_first = group * pair * span_ref[4] + span_ref[5]
    key_last = (group * pair + group - 1) * span_ref[4] + span_ref[5] + part - 1
    active = step < span_ref[1]
    whole = (key_first >= span_ref[2]) & (key_last <= span_ref[3])

    def accumulate(masked):
        keys = k_ref[...]
        values = v_ref[...]
        if masked:
            sub = lax.broadcasted_iota(jnp.int32, (block, 1), 0)
            key_rows = key_first + (sub // part) * span_ref[4] + sub % part
            allowed = (key_rows >= start_ref[...]) & (key_rows <= row_ref[...])
        for h in range(heads):
            scores = jnp.dot(keys, q_ref[h], preferred_element_type=jnp.float32) * scale
            if masked:
                scores = jnp.where(allowed, scores, -jnp.inf)
            m_old = m_sc[h]
            m_new = jnp.maximum(m_old, jnp.max(scores, axis=0, keepdims=True))
            rescale = jnp.exp(m_old - m_new)
            exp_scores = jnp.exp(scores - m_new)
            l_sc[h] = l_sc[h] * rescale + jnp.sum(exp_scores, axis=0, keepdims=True)
            acc_sc[h] = acc_sc[h] * rescale + lax.dot_general(
                values, exp_scores.astype(jnp.bfloat16), (((0,), (0,)), ((), ())),
                preferred_element_type=jnp.float32,
            )
            m_sc[h] = m_new

    @pl.when(active & whole)
    def _whole():
        accumulate(False)

    @pl.when(active & jnp.logical_not(whole))
    def _masked():
        accumulate(True)

    if final:
        @pl.when(step == pl.num_programs(0) - 1)
        def _finish():
            for h in range(heads):
                o_ref[h] = (acc_sc[h] / l_sc[h]).astype(o_ref.dtype)


def flash_pass(span, queries_t, kv_part, row_start, row_index, block, group, max_blocks, state):
    heads, _, rows = queries_t.shape
    final = state is not None

    def kv_map(column):
        def index_map(step, span_ref):
            return (span_ref[0] // group + jnp.minimum(step, span_ref[1] - 1), column)
        return index_map

    fixed2 = lambda step, span_ref: (0, 0)
    fixed3 = lambda step, span_ref: (0, 0, 0)
    in_specs = [
        pl.BlockSpec((heads, HD, rows), fixed3),
        pl.BlockSpec((group * block, HD), kv_map(0)),
        pl.BlockSpec((group * block, HD), kv_map(1)),
        pl.BlockSpec((1, rows), fixed2),
        pl.BlockSpec((1, rows), fixed2),
    ]
    state_shapes = [
        jax.ShapeDtypeStruct((heads, 1, rows), jnp.float32),
        jax.ShapeDtypeStruct((heads, 1, rows), jnp.float32),
        jax.ShapeDtypeStruct((heads, HD, rows), jnp.float32),
    ]
    state_specs = [pl.BlockSpec(x.shape, fixed3) for x in state_shapes]
    if final:
        in_specs = in_specs + state_specs
        out_specs = pl.BlockSpec((heads, HD, rows), fixed3)
        out_shape = jax.ShapeDtypeStruct((heads, HD, rows), jnp.bfloat16)
        scratch = [pltpu.VMEM(x.shape, jnp.float32) for x in state_shapes]
        operands = (span, queries_t, kv_part, kv_part, row_start, row_index) + tuple(state)
    else:
        out_specs = state_specs
        out_shape = state_shapes
        scratch = []
        operands = (span, queries_t, kv_part, kv_part, row_start, row_index)
    grid_spec = pltpu.PrefetchScalarGridSpec(
        num_scalar_prefetch=1,
        grid=(max_blocks,),
        in_specs=in_specs,
        out_specs=out_specs,
        scratch_shapes=scratch,
    )
    flops = 4 * group * heads * rows * block * HD * max_blocks
    return pl.pallas_call(
        functools.partial(flash_kernel, final, group),
        grid_spec=grid_spec,
        out_shape=out_shape,
        compiler_params=pltpu.CompilerParams(dimension_semantics=("arbitrary",)),
        cost_estimate=pl.CostEstimate(
            flops=flops,
            transcendentals=group * heads * rows * block * max_blocks,
            bytes_accessed=2 * group * block * HD * 2 * max_blocks + 2 * 2 * rows * heads * HD,
        ),
    )(*operands)


def local(hidden_rows, destination, doc_ids, norm_gain, w_query, w_key, w_value, w_out):
    owners = lax.axis_size(("chip", "core"))
    my_index = lax.axis_index(("chip", "core"))
    tok_dev, columns = hidden_rows.shape
    capacity = 2 * tok_dev // owners
    target = destination // tok_dev
    owner_ids = jnp.arange(owners, dtype=jnp.int32)
    one_hot = (target[:, None] == owner_ids[None, :]).astype(jnp.int32)
    slot_rank = jnp.sum((jnp.cumsum(one_hot, axis=0) - 1) * one_hot, axis=1)
    flat_slot = target * capacity + slot_rank
    outgoing = (
        jnp.zeros((owners * capacity, columns), hidden_rows.dtype).at[flat_slot].set(hidden_rows)
    )
    places = (
        jnp.full((owners * capacity,), tok_dev, jnp.int32).at[flat_slot].set(destination % tok_dev)
    )
    block_first = my_index * tok_dev
    first_id = doc_ids[0]
    last_id = doc_ids[tok_dev - 1]
    less_count = jnp.sum((doc_ids[None, :] < doc_ids[:, None]).astype(jnp.int32), axis=1)
    last_run_start = block_first + less_count[tok_dev - 1]
    digit = 64
    slot_count = owners * capacity
    meta = jnp.stack(
        [
            places // digit,
            places % digit,
            jnp.broadcast_to(last_id, (slot_count,)),
            jnp.broadcast_to(last_run_start // digit, (slot_count,)),
            jnp.broadcast_to(last_run_start % digit, (slot_count,)),
        ],
        axis=1,
    )
    meta_width = 128
    meta = jnp.pad(meta, ((0, 0), (0, meta_width - meta.shape[1]))).astype(hidden_rows.dtype)
    wide = jnp.concatenate([outgoing, meta], axis=1)
    arrived_wide = lax.all_to_all(
        wide.reshape(owners, capacity, columns + meta_width), ("chip", "core"),
        split_axis=0, concat_axis=0, tiled=True,
    )
    arrived = arrived_wide[:, :, :columns]
    arrived_meta = arrived_wide[:, :, columns:columns + 5].astype(jnp.int32)
    arrived_rows = (arrived_meta[:, :, 0] * digit + arrived_meta[:, :, 1]).reshape(-1)
    peer_last_id = arrived_meta[:, 0, 2]
    peer_run_start = arrived_meta[:, 0, 3] * digit + arrived_meta[:, 0, 4]
    earlier = (owner_ids < my_index) & (peer_last_id == first_id)
    doc_low = jnp.minimum(block_first, jnp.min(jnp.where(earlier, peer_run_start, block_first)))
    row_index = block_first + jnp.arange(tok_dev, dtype=jnp.int32)
    row_start = jnp.where(doc_ids == first_id, doc_low, block_first + less_count)

    routed_part = (
        jnp.zeros((tok_dev, columns), hidden_rows.dtype)
        .at[arrived_rows]
        .set(arrived.reshape(-1, columns), mode="drop")
    )
    routed = lax.all_gather(routed_part, "mp", axis=1, tiled=True)
    normed = normalize(routed, norm_gain)
    heads_dev = w_query.shape[1] // HD
    kv_dev = w_key.shape[1] // HD
    angles = rope_angles(row_index)
    queries = jnp.dot(normed, w_query, preferred_element_type=jnp.float32).reshape(
        tok_dev, heads_dev, HD
    )
    queries = rotate(queries, angles).astype(jnp.bfloat16).reshape(tok_dev, heads_dev * HD)
    keys_own = jnp.dot(normed, w_key, preferred_element_type=jnp.float32).reshape(
        tok_dev, kv_dev, HD
    )
    keys_own = rotate(keys_own, angles).astype(jnp.bfloat16).reshape(tok_dev, kv_dev * HD)
    values_own = jnp.dot(normed, w_value, preferred_element_type=jnp.float32).astype(jnp.bfloat16)
    kv_own = jnp.concatenate([keys_own, values_own], axis=1)
    half = 5 * tok_dev // 8
    kv_low = lax.all_gather(kv_own[:half], ("chip", "core"), axis=0, tiled=True)
    kv_high = lax.all_gather(kv_own[half:], ("chip", "core"), axis=0, tiled=True)

    block = KEY_BLOCK
    last_block = (block_first + tok_dev - 1) // block
    first_block = doc_low // block
    max_blocks = min((tok_dev - 1) // block + -(-(DOC_MAX - 1) // block) + 1, owners * tok_dev // block)
    max_start = jnp.max(row_start)

    def steps_for(group):
        return min((max_blocks - 1) // group + 2, owners * tok_dev // block // group)

    def span_for(offset, group):
        return jnp.stack(
            [first_block, last_block // group - first_block // group + 1, max_start, block_first, block, offset]
        ).astype(jnp.int32)

    queries_t = jnp.transpose(queries.reshape(tok_dev, heads_dev, HD), (1, 2, 0))
    state = flash_pass(
        span_for(0, 2), queries_t, kv_low, row_start[None, :], row_index[None, :], half, 2, steps_for(2),
        None,
    )
    context_t = flash_pass(
        span_for(half, 4), queries_t, kv_high, row_start[None, :], row_index[None, :], tok_dev - half, 4,
        steps_for(4),
        state,
    )
    context = jnp.transpose(context_t, (2, 0, 1)).reshape(tok_dev, heads_dev * HD)
    context_all = lax.all_gather(context, "mp", axis=1, tiled=True)
    mp_size = lax.axis_size("mp")
    w_split = jnp.transpose(w_out.reshape(w_out.shape[0], mp_size, -1), (1, 0, 2))
    w_cols = lax.all_to_all(w_split, "mp", split_axis=0, concat_axis=0, tiled=True)
    summed = jnp.einsum(
        "tsr,src->tc",
        context_all.reshape(tok_dev, mp_size, -1),
        w_cols,
        preferred_element_type=jnp.float32,
    )
    attended = (routed_part.astype(jnp.float32) + summed).astype(jnp.bfloat16)
    backward = attended[jnp.minimum(arrived_rows, tok_dev - 1)].reshape(owners, capacity, columns)
    returned = lax.all_to_all(backward, ("chip", "core"), split_axis=0, concat_axis=0, tiled=True)
    return returned.reshape(owners * capacity, columns)[flat_slot]


def solution(mesh):
    dp_size, mp_size = mesh.devices.shape
    split_mesh = jax.sharding.Mesh(
        mesh.devices.reshape(dp_size // 2, 2, mp_size), ("chip", "core", "mp")
    )
    rows = ("chip", "core")
    in_specs = (
        P(rows, "mp"),
        P(rows),
        P(rows),
        P(),
        P(None, "mp"),
        P(None, "mp"),
        P(None, "mp"),
        P("mp", None),
    )
    out_specs = P(rows, "mp")
    return jax.shard_map(
        local, mesh=split_mesh, in_specs=in_specs, out_specs=out_specs, check_vma=False
    )
```

```python
import functools
import math

import jax
import jax.numpy as jnp
from jax import lax
from jax.experimental import pallas as pl
from jax.experimental.pallas import tpu as pltpu
from jax.sharding import PartitionSpec as P

HD = 128
DOC_MAX = 8704

ROPE_BASE = 500000.0
NORM_EPS = 1e-05
NEG_START = -1e30
KEY_BLOCK = 512


def rope_angles(row_index):
    lane_index = jnp.arange(HD // 2, dtype=jnp.float32)
    frequency = jnp.power(jnp.float32(ROPE_BASE), -2.0 * lane_index / HD)
    return row_index.astype(jnp.float32)[:, None] * frequency[None, :]


def rotate(head_values, angles):
    half_width = head_values.shape[-1] // 2
    first_half = head_values[..., :half_width]
    second_half = head_values[..., half_width:]
    cosine = jnp.cos(angles)[:, None, :]
    sine_part = jnp.sin(angles)[:, None, :]
    return jnp.concatenate(
        [
            first_half * cosine - second_half * sine_part,
            second_half * cosine + first_half * sine_part,
        ],
        axis=-1,
    )


def normalize(routed, norm_gain):
    wide_rows = routed.astype(jnp.float32)
    inv_rms = lax.rsqrt(jnp.mean(wide_rows * wide_rows, axis=1, keepdims=True) + NORM_EPS)
    return (wide_rows * inv_rms * norm_gain[None, :]).astype(jnp.bfloat16)


def flash_kernel(final, group, span_ref, *refs):
    if final:
        q_ref, k_ref, v_ref, start_ref, row_ref, m_in, l_in, acc_in, o_ref, m_sc, l_sc, acc_sc = refs
    else:
        q_ref, k_ref, v_ref, start_ref, row_ref, m_sc, l_sc, acc_sc = refs
    step = pl.program_id(0)
    heads = m_sc.shape[0]
    block = k_ref.shape[0]
    scale = HD ** (-0.5)

    @pl.when(step == 0)
    def _init():
        if final:
            m_sc[...] = m_in[...]
            l_sc[...] = l_in[...]
            acc_sc[...] = acc_in[...]
        else:
            m_sc[...] = jnp.full(m_sc.shape, NEG_START, jnp.float32)
            l_sc[...] = jnp.zeros(l_sc.shape, jnp.float32)
            acc_sc[...] = jnp.zeros(acc_sc.shape, jnp.float32)

    part = block // group
    pair = span_ref[0] // group + step
    key_first = group * pair * span_ref[4] + span_ref[5]
    key_last = (group * pair + group - 1) * span_ref[4] + span_ref[5] + part - 1
    active = step < span_ref[1]
    whole = (key_first >= span_ref[2]) & (key_last <= span_ref[3])

    def accumulate(masked):
        keys = k_ref[...]
        values = v_ref[...]
        if masked:
            sub = lax.broadcasted_iota(jnp.int32, (block, 1), 0)
            key_rows = key_first + (sub // part) * span_ref[4] + sub % part
            allowed = (key_rows >= start_ref[...]) & (key_rows <= row_ref[...])
        for h in range(heads):
            scores = jnp.dot(keys, q_ref[h], preferred_element_type=jnp.float32) * scale
            if masked:
                scores = jnp.where(allowed, scores, -jnp.inf)
            m_old = m_sc[h]
            m_new = jnp.maximum(m_old, jnp.max(scores, axis=0, keepdims=True))
            rescale = jnp.exp(m_old - m_new)
            exp_scores = jnp.exp(scores - m_new)
            l_sc[h] = l_sc[h] * rescale + jnp.sum(exp_scores, axis=0, keepdims=True)
            acc_sc[h] = acc_sc[h] * rescale + lax.dot_general(
                values, exp_scores.astype(jnp.bfloat16), (((0,), (0,)), ((), ())),
                preferred_element_type=jnp.float32,
            )
            m_sc[h] = m_new

    @pl.when(active & whole)
    def _whole():
        accumulate(False)

    @pl.when(active & jnp.logical_not(whole))
    def _masked():
        accumulate(True)

    if final:
        @pl.when(step == pl.num_programs(0) - 1)
        def _finish():
            for h in range(heads):
                o_ref[h] = (acc_sc[h] / l_sc[h]).astype(o_ref.dtype)


def flash_pass(span, queries_t, kv_part, row_start, row_index, block, group, max_blocks, state):
    heads, _, rows = queries_t.shape
    final = state is not None

    def kv_map(column):
        def index_map(step, span_ref):
            return (span_ref[0] // group + jnp.minimum(step, span_ref[1] - 1), column)
        return index_map

    fixed2 = lambda step, span_ref: (0, 0)
    fixed3 = lambda step, span_ref: (0, 0, 0)
    in_specs = [
        pl.BlockSpec((heads, HD, rows), fixed3),
        pl.BlockSpec((group * block, HD), kv_map(0)),
        pl.BlockSpec((group * block, HD), kv_map(1)),
        pl.BlockSpec((1, rows), fixed2),
        pl.BlockSpec((1, rows), fixed2),
    ]
    state_shapes = [
        jax.ShapeDtypeStruct((heads, 1, rows), jnp.float32),
        jax.ShapeDtypeStruct((heads, 1, rows), jnp.float32),
        jax.ShapeDtypeStruct((heads, HD, rows), jnp.float32),
    ]
    state_specs = [pl.BlockSpec(x.shape, fixed3) for x in state_shapes]
    if final:
        in_specs = in_specs + state_specs
        out_specs = pl.BlockSpec((heads, HD, rows), fixed3)
        out_shape = jax.ShapeDtypeStruct((heads, HD, rows), jnp.bfloat16)
        scratch = [pltpu.VMEM(x.shape, jnp.float32) for x in state_shapes]
        operands = (span, queries_t, kv_part, kv_part, row_start, row_index) + tuple(state)
    else:
        out_specs = state_specs
        out_shape = state_shapes
        scratch = []
        operands = (span, queries_t, kv_part, kv_part, row_start, row_index)
    grid_spec = pltpu.PrefetchScalarGridSpec(
        num_scalar_prefetch=1,
        grid=(max_blocks,),
        in_specs=in_specs,
        out_specs=out_specs,
        scratch_shapes=scratch,
    )
    flops = 4 * group * heads * rows * block * HD * max_blocks
    return pl.pallas_call(
        functools.partial(flash_kernel, final, group),
        grid_spec=grid_spec,
        out_shape=out_shape,
        compiler_params=pltpu.CompilerParams(dimension_semantics=("arbitrary",)),
        cost_estimate=pl.CostEstimate(
            flops=flops,
            transcendentals=group * heads * rows * block * max_blocks,
            bytes_accessed=2 * group * block * HD * 2 * max_blocks + 2 * 2 * rows * heads * HD,
        ),
    )(*operands)


def local(hidden_rows, destination, doc_ids, norm_gain, w_query, w_key, w_value, w_out):
    owners = lax.axis_size(("chip", "core"))
    my_index = lax.axis_index(("chip", "core"))
    tok_dev, columns = hidden_rows.shape
    capacity = 2 * tok_dev // owners
    target = destination // tok_dev
    owner_ids = jnp.arange(owners, dtype=jnp.int32)
    one_hot = (target[:, None] == owner_ids[None, :]).astype(jnp.int32)
    slot_rank = jnp.sum((jnp.cumsum(one_hot, axis=0) - 1) * one_hot, axis=1)
    flat_slot = target * capacity + slot_rank
    outgoing = (
        jnp.zeros((owners * capacity, columns), hidden_rows.dtype).at[flat_slot].set(hidden_rows)
    )
    places = (
        jnp.full((owners * capacity,), tok_dev, jnp.int32).at[flat_slot].set(destination % tok_dev)
    )
    block_first = my_index * tok_dev
    first_id = doc_ids[0]
    last_id = doc_ids[tok_dev - 1]
    less_count = jnp.sum((doc_ids[None, :] < doc_ids[:, None]).astype(jnp.int32), axis=1)
    last_run_start = block_first + less_count[tok_dev - 1]
    digit = 64
    slot_count = owners * capacity
    meta = jnp.stack(
        [
            places // digit,
            places % digit,
            jnp.broadcast_to(last_id, (slot_count,)),
            jnp.broadcast_to(last_run_start // digit, (slot_count,)),
            jnp.broadcast_to(last_run_start % digit, (slot_count,)),
        ],
        axis=1,
    )
    meta_width = 128
    meta = jnp.pad(meta, ((0, 0), (0, meta_width - meta.shape[1]))).astype(hidden_rows.dtype)
    wide = jnp.concatenate([outgoing, meta], axis=1)
    arrived_wide = lax.all_to_all(
        wide.reshape(owners, capacity, columns + meta_width), ("chip", "core"),
        split_axis=0, concat_axis=0, tiled=True,
    )
    arrived = arrived_wide[:, :, :columns]
    arrived_meta = arrived_wide[:, :, columns:columns + 5].astype(jnp.int32)
    arrived_rows = (arrived_meta[:, :, 0] * digit + arrived_meta[:, :, 1]).reshape(-1)
    peer_last_id = arrived_meta[:, 0, 2]
    peer_run_start = arrived_meta[:, 0, 3] * digit + arrived_meta[:, 0, 4]
    earlier = (owner_ids < my_index) & (peer_last_id == first_id)
    doc_low = jnp.minimum(block_first, jnp.min(jnp.where(earlier, peer_run_start, block_first)))
    row_index = block_first + jnp.arange(tok_dev, dtype=jnp.int32)
    row_start = jnp.where(doc_ids == first_id, doc_low, block_first + less_count)

    routed_part = (
        jnp.zeros((tok_dev, columns), hidden_rows.dtype)
        .at[arrived_rows]
        .set(arrived.reshape(-1, columns), mode="drop")
    )
    routed = lax.all_gather(routed_part, "mp", axis=1, tiled=True)
    normed = normalize(routed, norm_gain)
    heads_dev = w_query.shape[1] // HD
    kv_dev = w_key.shape[1] // HD
    angles = rope_angles(row_index)
    queries = jnp.dot(normed, w_query, preferred_element_type=jnp.float32).reshape(
        tok_dev, heads_dev, HD
    )
    queries = rotate(queries, angles).astype(jnp.bfloat16).reshape(tok_dev, heads_dev * HD)
    keys_own = jnp.dot(normed, w_key, preferred_element_type=jnp.float32).reshape(
        tok_dev, kv_dev, HD
    )
    keys_own = rotate(keys_own, angles).astype(jnp.bfloat16).reshape(tok_dev, kv_dev * HD)
    values_own = jnp.dot(normed, w_value, preferred_element_type=jnp.float32).astype(jnp.bfloat16)
    kv_own = jnp.concatenate([keys_own, values_own], axis=1)
    half = 21 * tok_dev // 32
    kv_low = lax.all_gather(kv_own[:half], ("chip", "core"), axis=0, tiled=True)
    kv_high = lax.all_gather(kv_own[half:], ("chip", "core"), axis=0, tiled=True)

    block = KEY_BLOCK
    last_block = (block_first + tok_dev - 1) // block
    first_block = doc_low // block
    max_blocks = min((tok_dev - 1) // block + -(-(DOC_MAX - 1) // block) + 1, owners * tok_dev // block)
    max_start = jnp.max(row_start)

    def steps_for(group):
        return min((max_blocks - 1) // group + 2, owners * tok_dev // block // group)

    def span_for(offset, group):
        return jnp.stack(
            [first_block, last_block // group - first_block // group + 1, max_start, block_first, block, offset]
        ).astype(jnp.int32)

    queries_t = jnp.transpose(queries.reshape(tok_dev, heads_dev, HD), (1, 2, 0))
    state = flash_pass(
        span_for(0, 2), queries_t, kv_low, row_start[None, :], row_index[None, :], half, 2, steps_for(2),
        None,
    )
    context_t = flash_pass(
        span_for(half, 4), queries_t, kv_high, row_start[None, :], row_index[None, :], tok_dev - half, 4,
        steps_for(4),
        state,
    )
    context = jnp.transpose(context_t, (2, 0, 1)).reshape(tok_dev, heads_dev * HD)
    context_all = lax.all_gather(context, "mp", axis=1, tiled=True)
    mp_size = lax.axis_size("mp")
    w_split = jnp.transpose(w_out.reshape(w_out.shape[0], mp_size, -1), (1, 0, 2))
    w_cols = lax.all_to_all(w_split, "mp", split_axis=0, concat_axis=0, tiled=True)
    summed = jnp.einsum(
        "tsr,src->tc",
        context_all.reshape(tok_dev, mp_size, -1),
        w_cols,
        preferred_element_type=jnp.float32,
    )
    attended = (routed_part.astype(jnp.float32) + summed).astype(jnp.bfloat16)
    backward = attended[jnp.minimum(arrived_rows, tok_dev - 1)].reshape(owners, capacity, columns)
    returned = lax.all_to_all(backward, ("chip", "core"), split_axis=0, concat_axis=0, tiled=True)
    return returned.reshape(owners * capacity, columns)[flat_slot]


def solution(mesh):
    dp_size, mp_size = mesh.devices.shape
    split_mesh = jax.sharding.Mesh(
        mesh.devices.reshape(dp_size // 2, 2, mp_size), ("chip", "core", "mp")
    )
    rows = ("chip", "core")
    in_specs = (
        P(rows, "mp"),
        P(rows),
        P(rows),
        P(),
        P(None, "mp"),
        P(None, "mp"),
        P(None, "mp"),
        P("mp", None),
    )
    out_specs = P(rows, "mp")
    return jax.shard_map(
        local, mesh=split_mesh, in_specs=in_specs, out_specs=out_specs, check_vma=False
    )
```

```python
import functools
import math

import jax
import jax.numpy as jnp
from jax import lax
from jax.experimental import pallas as pl
from jax.experimental.pallas import tpu as pltpu
from jax.sharding import PartitionSpec as P

HD = 128
DOC_MAX = 8704

ROPE_BASE = 500000.0
NORM_EPS = 1e-05
NEG_START = -1e30
KEY_BLOCK = 512


def rope_angles(row_index):
    lane_index = jnp.arange(HD // 2, dtype=jnp.float32)
    frequency = jnp.power(jnp.float32(ROPE_BASE), -2.0 * lane_index / HD)
    return row_index.astype(jnp.float32)[:, None] * frequency[None, :]


def rotate(head_values, angles):
    half_width = head_values.shape[-1] // 2
    first_half = head_values[..., :half_width]
    second_half = head_values[..., half_width:]
    cosine = jnp.cos(angles)[:, None, :]
    sine_part = jnp.sin(angles)[:, None, :]
    return jnp.concatenate(
        [
            first_half * cosine - second_half * sine_part,
            second_half * cosine + first_half * sine_part,
        ],
        axis=-1,
    )


def normalize(routed, norm_gain):
    wide_rows = routed.astype(jnp.float32)
    inv_rms = lax.rsqrt(jnp.mean(wide_rows * wide_rows, axis=1, keepdims=True) + NORM_EPS)
    return (wide_rows * inv_rms * norm_gain[None, :]).astype(jnp.bfloat16)


def flash_kernel(final, group, span_ref, *refs):
    if final:
        q_ref, k_ref, v_ref, start_ref, row_ref, m_in, l_in, acc_in, o_ref, m_sc, l_sc, acc_sc = refs
    else:
        q_ref, k_ref, v_ref, start_ref, row_ref, m_sc, l_sc, acc_sc = refs
    step = pl.program_id(0)
    heads = m_sc.shape[0]
    block = k_ref.shape[0]
    scale = HD ** (-0.5)

    @pl.when(step == 0)
    def _init():
        if final:
            m_sc[...] = m_in[...]
            l_sc[...] = l_in[...]
            acc_sc[...] = acc_in[...]
        else:
            m_sc[...] = jnp.full(m_sc.shape, NEG_START, jnp.float32)
            l_sc[...] = jnp.zeros(l_sc.shape, jnp.float32)
            acc_sc[...] = jnp.zeros(acc_sc.shape, jnp.float32)

    part = block // group
    pair = span_ref[0] // group + step
    key_first = group * pair * span_ref[4] + span_ref[5]
    key_last = (group * pair + group - 1) * span_ref[4] + span_ref[5] + part - 1
    active = step < span_ref[1]
    whole = (key_first >= span_ref[2]) & (key_last <= span_ref[3])

    def accumulate(masked):
        keys = k_ref[...]
        values = v_ref[...]
        if masked:
            sub = lax.broadcasted_iota(jnp.int32, (block, 1), 0)
            key_rows = key_first + (sub // part) * span_ref[4] + sub % part
            allowed = (key_rows >= start_ref[...]) & (key_rows <= row_ref[...])
        for h in range(heads):
            scores = jnp.dot(keys, q_ref[h], preferred_element_type=jnp.float32) * scale
            if masked:
                scores = jnp.where(allowed, scores, -jnp.inf)
            m_old = m_sc[h]
            m_new = jnp.maximum(m_old, jnp.max(scores, axis=0, keepdims=True))
            rescale = jnp.exp(m_old - m_new)
            exp_scores = jnp.exp(scores - m_new)
            l_sc[h] = l_sc[h] * rescale + jnp.sum(exp_scores, axis=0, keepdims=True)
            acc_sc[h] = acc_sc[h] * rescale + lax.dot_general(
                values, exp_scores.astype(jnp.bfloat16), (((0,), (0,)), ((), ())),
                preferred_element_type=jnp.float32,
            )
            m_sc[h] = m_new

    @pl.when(active & whole)
    def _whole():
        accumulate(False)

    @pl.when(active & jnp.logical_not(whole))
    def _masked():
        accumulate(True)

    if final:
        @pl.when(step == pl.num_programs(0) - 1)
        def _finish():
            for h in range(heads):
                o_ref[h] = (acc_sc[h] / l_sc[h]).astype(o_ref.dtype)


def flash_pass(span, queries_t, kv_part, row_start, row_index, block, group, max_blocks, state):
    heads, _, rows = queries_t.shape
    final = state is not None

    def kv_map(column):
        def index_map(step, span_ref):
            return (span_ref[0] // group + jnp.minimum(step, span_ref[1] - 1), column)
        return index_map

    fixed2 = lambda step, span_ref: (0, 0)
    fixed3 = lambda step, span_ref: (0, 0, 0)
    in_specs = [
        pl.BlockSpec((heads, HD, rows), fixed3),
        pl.BlockSpec((group * block, HD), kv_map(0)),
        pl.BlockSpec((group * block, HD), kv_map(1)),
        pl.BlockSpec((1, rows), fixed2),
        pl.BlockSpec((1, rows), fixed2),
    ]
    state_shapes = [
        jax.ShapeDtypeStruct((heads, 1, rows), jnp.float32),
        jax.ShapeDtypeStruct((heads, 1, rows), jnp.float32),
        jax.ShapeDtypeStruct((heads, HD, rows), jnp.float32),
    ]
    state_specs = [pl.BlockSpec(x.shape, fixed3) for x in state_shapes]
    if final:
        in_specs = in_specs + state_specs
        out_specs = pl.BlockSpec((heads, HD, rows), fixed3)
        out_shape = jax.ShapeDtypeStruct((heads, HD, rows), jnp.bfloat16)
        scratch = [pltpu.VMEM(x.shape, jnp.float32) for x in state_shapes]
        operands = (span, queries_t, kv_part, kv_part, row_start, row_index) + tuple(state)
    else:
        out_specs = state_specs
        out_shape = state_shapes
        scratch = []
        operands = (span, queries_t, kv_part, kv_part, row_start, row_index)
    grid_spec = pltpu.PrefetchScalarGridSpec(
        num_scalar_prefetch=1,
        grid=(max_blocks,),
        in_specs=in_specs,
        out_specs=out_specs,
        scratch_shapes=scratch,
    )
    flops = 4 * group * heads * rows * block * HD * max_blocks
    return pl.pallas_call(
        functools.partial(flash_kernel, final, group),
        grid_spec=grid_spec,
        out_shape=out_shape,
        compiler_params=pltpu.CompilerParams(dimension_semantics=("arbitrary",)),
        cost_estimate=pl.CostEstimate(
            flops=flops,
            transcendentals=group * heads * rows * block * max_blocks,
            bytes_accessed=2 * group * block * HD * 2 * max_blocks + 2 * 2 * rows * heads * HD,
        ),
    )(*operands)


def local(hidden_rows, destination, doc_ids, norm_gain, w_query, w_key, w_value, w_out):
    owners = lax.axis_size(("chip", "core"))
    my_index = lax.axis_index(("chip", "core"))
    tok_dev, columns = hidden_rows.shape
    capacity = 2 * tok_dev // owners
    target = destination // tok_dev
    owner_ids = jnp.arange(owners, dtype=jnp.int32)
    one_hot = (target[:, None] == owner_ids[None, :]).astype(jnp.int32)
    slot_rank = jnp.sum((jnp.cumsum(one_hot, axis=0) - 1) * one_hot, axis=1)
    flat_slot = target * capacity + slot_rank
    outgoing = (
        jnp.zeros((owners * capacity, columns), hidden_rows.dtype).at[flat_slot].set(hidden_rows)
    )
    places = (
        jnp.full((owners * capacity,), tok_dev, jnp.int32).at[flat_slot].set(destination % tok_dev)
    )
    block_first = my_index * tok_dev
    first_id = doc_ids[0]
    last_id = doc_ids[tok_dev - 1]
    less_count = jnp.sum((doc_ids[None, :] < doc_ids[:, None]).astype(jnp.int32), axis=1)
    last_run_start = block_first + less_count[tok_dev - 1]
    digit = 64
    slot_count = owners * capacity
    meta = jnp.stack(
        [
            places // digit,
            places % digit,
            jnp.broadcast_to(last_id, (slot_count,)),
            jnp.broadcast_to(last_run_start // digit, (slot_count,)),
            jnp.broadcast_to(last_run_start % digit, (slot_count,)),
        ],
        axis=1,
    )
    meta_width = 128
    meta = jnp.pad(meta, ((0, 0), (0, meta_width - meta.shape[1]))).astype(hidden_rows.dtype)
    wide = jnp.concatenate([outgoing, meta], axis=1)
    arrived_wide = lax.all_to_all(
        wide.reshape(owners, capacity, columns + meta_width), ("chip", "core"),
        split_axis=0, concat_axis=0, tiled=True,
    )
    arrived = arrived_wide[:, :, :columns]
    arrived_meta = arrived_wide[:, :, columns:columns + 5].astype(jnp.int32)
    arrived_rows = (arrived_meta[:, :, 0] * digit + arrived_meta[:, :, 1]).reshape(-1)
    peer_last_id = arrived_meta[:, 0, 2]
    peer_run_start = arrived_meta[:, 0, 3] * digit + arrived_meta[:, 0, 4]
    earlier = (owner_ids < my_index) & (peer_last_id == first_id)
    doc_low = jnp.minimum(block_first, jnp.min(jnp.where(earlier, peer_run_start, block_first)))
    row_index = block_first + jnp.arange(tok_dev, dtype=jnp.int32)
    row_start = jnp.where(doc_ids == first_id, doc_low, block_first + less_count)

    routed_part = (
        jnp.zeros((tok_dev, columns), hidden_rows.dtype)
        .at[arrived_rows]
        .set(arrived.reshape(-1, columns), mode="drop")
    )
    routed = lax.all_gather(routed_part, "mp", axis=1, tiled=True)
    normed = normalize(routed, norm_gain)
    heads_dev = w_query.shape[1] // HD
    kv_dev = w_key.shape[1] // HD
    angles = rope_angles(row_index)
    queries = jnp.dot(normed, w_query, preferred_element_type=jnp.float32).reshape(
        tok_dev, heads_dev, HD
    )
    queries = rotate(queries, angles).astype(jnp.bfloat16).reshape(tok_dev, heads_dev * HD)
    keys_own = jnp.dot(normed, w_key, preferred_element_type=jnp.float32).reshape(
        tok_dev, kv_dev, HD
    )
    keys_own = rotate(keys_own, angles).astype(jnp.bfloat16).reshape(tok_dev, kv_dev * HD)
    values_own = jnp.dot(normed, w_value, preferred_element_type=jnp.float32).astype(jnp.bfloat16)
    kv_own = jnp.concatenate([keys_own, values_own], axis=1)
    half = 11 * tok_dev // 16
    kv_low = lax.all_gather(kv_own[:half], ("chip", "core"), axis=0, tiled=True)
    kv_high = lax.all_gather(kv_own[half:], ("chip", "core"), axis=0, tiled=True)

    block = KEY_BLOCK
    last_block = (block_first + tok_dev - 1) // block
    first_block = doc_low // block
    max_blocks = min((tok_dev - 1) // block + -(-(DOC_MAX - 1) // block) + 1, owners * tok_dev // block)
    max_start = jnp.max(row_start)

    def steps_for(group):
        return min((max_blocks - 1) // group + 2, owners * tok_dev // block // group)

    def span_for(offset, group):
        return jnp.stack(
            [first_block, last_block // group - first_block // group + 1, max_start, block_first, block, offset]
        ).astype(jnp.int32)

    queries_t = jnp.transpose(queries.reshape(tok_dev, heads_dev, HD), (1, 2, 0))
    state = flash_pass(
        span_for(0, 2), queries_t, kv_low, row_start[None, :], row_index[None, :], half, 2, steps_for(2),
        None,
    )
    context_t = flash_pass(
        span_for(half, 4), queries_t, kv_high, row_start[None, :], row_index[None, :], tok_dev - half, 4,
        steps_for(4),
        state,
    )
    context = jnp.transpose(context_t, (2, 0, 1)).reshape(tok_dev, heads_dev * HD)
    context_all = lax.all_gather(context, "mp", axis=1, tiled=True)
    mp_size = lax.axis_size("mp")
    w_split = jnp.transpose(w_out.reshape(w_out.shape[0], mp_size, -1), (1, 0, 2))
    w_cols = lax.all_to_all(w_split, "mp", split_axis=0, concat_axis=0, tiled=True)
    summed = jnp.einsum(
        "tsr,src->tc",
        context_all.reshape(tok_dev, mp_size, -1),
        w_cols,
        preferred_element_type=jnp.float32,
    )
    attended = (routed_part.astype(jnp.float32) + summed).astype(jnp.bfloat16)
    backward = attended[jnp.minimum(arrived_rows, tok_dev - 1)].reshape(owners, capacity, columns)
    returned = lax.all_to_all(backward, ("chip", "core"), split_axis=0, concat_axis=0, tiled=True)
    return returned.reshape(owners * capacity, columns)[flat_slot]


def solution(mesh):
    dp_size, mp_size = mesh.devices.shape
    split_mesh = jax.sharding.Mesh(
        mesh.devices.reshape(dp_size // 2, 2, mp_size), ("chip", "core", "mp")
    )
    rows = ("chip", "core")
    in_specs = (
        P(rows, "mp"),
        P(rows),
        P(rows),
        P(),
        P(None, "mp"),
        P(None, "mp"),
        P(None, "mp"),
        P("mp", None),
    )
    out_specs = P(rows, "mp")
    return jax.shard_map(
        local, mesh=split_mesh, in_specs=in_specs, out_specs=out_specs, check_vma=False
    )
```
